32 devices in a mesh: dp: 8 (over z, y), tensor: 4 (over x, core).
Axes of the slice: x: 2, y: 2, z: 4, core: 2. Of those that a mesh axis runs over, the one named last changes fastest.
Arguments:
- pre_hidden: bfloat16 [8192, 2048], P(('dp', 'tensor')), may hold values from -6 to 6
- dec_hidden: bfloat16 [16, 2048], P('dp'), may hold values from -6 to 6
- norm_gain: bfloat16 [2048], replicated, may hold values from 0.5 to 1.5
- norm_shift: bfloat16 [2048], replicated, may hold values from -3 to 3
- qkv_weight: bfloat16 [2048, 6144], P(None, 'tensor'), may hold values from -0.125 to 0.125
- qkv_bias: bfloat16 [6144], P('tensor'), may hold values from -3 to 3
- out_weight: bfloat16 [2048, 2048], P('tensor'), may hold values from -0.125 to 0.125
- out_bias: bfloat16 [2048], replicated, may hold values from -3 to 3
- pre_keys: bfloat16 [8, 1024, 2048], P('dp', None, 'tensor'), may hold values from -480 to 480
- pre_values: bfloat16 [8, 1024, 2048], P('dp', None, 'tensor'), may hold values from -6 to 6
- dec_keys: bfloat16 [16, 2048, 2048], P('dp', None, 'tensor'), may hold values from -480 to 480
- dec_values: bfloat16 [16, 2048, 2048], P('dp', None, 'tensor'), may hold values from -6 to 6
- prefix_lengths: int32 [8], P('dp'), may hold values from 0 to 1024, as said below
- cache_lengths: int32 [16], P('dp'), may hold values from 1 to 2048, as said below
- slot_of: int32 [16], replicated, may hold values from 0 to 15, each once
Outputs:
- pre_output: bfloat16 [8192, 2048], P(('dp', 'tensor'))
- dec_output: bfloat16 [16, 2048], P('dp')
The draws below stay inside these ranges and needn't reach their ends.
Inputs may be any that keep to these rules, and one draw needn't show every extreme that they name: `slot_of`: each decode slot is used by exactly one decode request. `prefix_lengths`: the longest prefix equals 1024. `cache_lengths`: the longest decode cache equals 2048.
All inputs are finite; a program needn't handle non-finite values.
Results may differ from the reference program's by a relative error of at most 0.0049.
The reference program's roundings to bfloat16 on the way count: a program that leaves them out, or rounds other values in their place, can miss the bound.
Values may be sent and summed in bfloat16 or wider, within the bound.
No kernel may reach another device: no remote copies, remote signals or barrier semaphores. Data moves between devices by JAX's collectives and lax.ppermute only.
A program may use at most 128 MiB of HBM per device.

```python
import math
import jax
import jax.numpy as jnp
from jax import lax

D = 2048
H = 16
HD = 128
GROUP = 1024
PRE_CACHE = 1024
DEC_CACHE = 2048
PREFILLS = 8
DECODES = 16
PRE_ROWS = 8192


def scaled_keys(key, leading, positions):
    values = jnp.clip(jax.random.normal(key, (leading, positions, D), jnp.float32), -6.0, 6.0)
    return values


def draw_pre_keys(key, part):
    return scaled_keys(key, PREFILLS, PRE_CACHE).astype(jnp.bfloat16)


def draw_dec_keys(key, part):
    return scaled_keys(key, DECODES, DEC_CACHE).astype(jnp.bfloat16)


def draw_prefix_lengths(key, part):
    first = jax.random.randint(jax.random.fold_in(key, 1), (PREFILLS,), 0, PRE_CACHE + 1)
    second = jax.random.randint(jax.random.fold_in(key, 2), (PREFILLS,), 0, PRE_CACHE + 1)
    lengths = first * second // PRE_CACHE
    longest = jax.random.randint(jax.random.fold_in(key, 3), (), 0, PREFILLS)
    return lengths.at[longest].set(PRE_CACHE).astype(jnp.int32)


def draw_cache_lengths(key, part):
    first = jax.random.randint(jax.random.fold_in(key, 4), (DECODES,), 0, DEC_CACHE)
    second = jax.random.randint(jax.random.fold_in(key, 5), (DECODES,), 0, DEC_CACHE)
    lengths = 1 + first * second // DEC_CACHE
    longest = jax.random.randint(jax.random.fold_in(key, 6), (), 0, DECODES)
    return lengths.at[longest].set(DEC_CACHE).astype(jnp.int32)


def shard_levels(stream_key, shape, cuts, smallest, largest):
    def one(position, blocks):
        steps = jax.random.uniform(jax.random.fold_in(jax.random.fold_in(stream_key, 6), position), (blocks,), jnp.float32, smallest / len(cuts), largest / len(cuts))
        return jnp.repeat(jnp.exp(steps), shape[position] // blocks).reshape((-1,) + (1,) * (len(shape) - position - 1))

    level = one(*cuts[0])
    for cut in cuts[1:]:
        level = level * one(*cut)
    return level


def centred(rng, dims, scale, most, split=(), kind=jnp.bfloat16):
    values = scale * jax.random.normal(rng, dims, jnp.float32)
    if split:
        values = values * shard_levels(rng, dims, split, -0.22, 0.18)
    return jnp.clip(values, -most, most).astype(kind)


def setup_inputs(seed: int = 0) -> dict:
    key_list = jax.random.split(jax.random.key(seed), 16)
    pre_hidden = centred(key_list[0], (PRE_ROWS, D), 1.0, 6.0, ((0, 32),))
    dec_hidden = centred(key_list[1], (DECODES, D), 1.0, 6.0, ((0, 8),))
    norm_gain = jnp.clip(1.0 + 0.1 * jax.random.normal(key_list[2], (D,), jnp.float32), 0.5, 1.5).astype(jnp.bfloat16)
    norm_shift = centred(key_list[3], (D,), 0.5, 3.0)
    qkv_weight = centred(key_list[4], (D, 3 * D), D ** -0.5, 0.125, ((1, 4),))
    qkv_bias = centred(key_list[5], (3 * D,), 0.5, 3.0, ((0, 4),))
    out_weight = centred(key_list[6], (D, D), D ** -0.5, 0.125, ((0, 4),))
    out_bias = centred(key_list[7], (D,), 0.5, 3.0)
    pre_keys = draw_pre_keys(jax.random.fold_in(key_list[15], 71), 0)
    pre_values = centred(key_list[9], (PREFILLS, PRE_CACHE, D), 1.0, 6.0, ((0, 8), (2, 4)))
    dec_keys = draw_dec_keys(jax.random.fold_in(key_list[15], 71), 0)
    dec_values = centred(key_list[11], (DECODES, DEC_CACHE, D), 1.0, 6.0, ((0, 8), (2, 4)))
    prefix_lengths = draw_prefix_lengths(jax.random.fold_in(key_list[15], 71), 0)
    cache_lengths = draw_cache_lengths(jax.random.fold_in(key_list[15], 71), 0)
    slot_of = jax.random.permutation(key_list[14], DECODES).astype(jnp.int32)
    return {"pre_hidden": pre_hidden, "dec_hidden": dec_hidden, "norm_gain": norm_gain, "norm_shift": norm_shift, "qkv_weight": qkv_weight, "qkv_bias": qkv_bias, "out_weight": out_weight, "out_bias": out_bias, "pre_keys": pre_keys, "pre_values": pre_values, "dec_keys": dec_keys, "dec_values": dec_values, "prefix_lengths": prefix_lengths, "cache_lengths": cache_lengths, "slot_of": slot_of}


EPSILON = 1e-05

def normalize(values, norm_gain, norm_shift):
    values = values.astype(jnp.float32)
    center = values - lax.optimization_barrier(jnp.mean(values, axis=-1, keepdims=True))
    spread = lax.optimization_barrier(jnp.mean(center * center, axis=-1, keepdims=True))
    scaled = center * lax.rsqrt(spread + EPSILON)
    return (scaled * norm_gain.astype(jnp.float32) + norm_shift.astype(jnp.float32)).astype(jnp.bfloat16)

def alibi_slopes(first_head, head_count, total_heads):
    head_ids = (first_head + jnp.arange(head_count, dtype=jnp.int32)).astype(jnp.float32)
    return jnp.exp2(-8.0 * (head_ids + 1.0) / total_heads)

def attend(queries, keys_all, values_all, distance, allowed, slopes):
    factor = 1.0 / math.sqrt(queries.shape[-1])
    scores = jnp.einsum('qhd,khd->hqk', queries.astype(jnp.float32), keys_all.astype(jnp.float32)) * factor
    scores = scores - slopes[:, None, None] * distance[None]
    scores = jnp.where(allowed[None], scores, -jnp.inf)
    highest = lax.optimization_barrier(jnp.max(scores, axis=-1, keepdims=True))
    weights = jnp.exp(scores - highest)
    probs = (weights / lax.optimization_barrier(jnp.sum(weights, axis=-1, keepdims=True))).astype(jnp.bfloat16)
    context = jnp.einsum('hqk,khd->qhd', probs.astype(jnp.float32), values_all.astype(jnp.float32))
    return context.astype(jnp.bfloat16).reshape(queries.shape[0], -1)

def reference(pre_hidden, dec_hidden, norm_gain, norm_shift, qkv_weight, qkv_bias, out_weight, out_bias, pre_keys, pre_values, dec_keys, dec_values, prefix_lengths, cache_lengths, slot_of):
    slopes = alibi_slopes(0, H, H)

    def project(rows_in):
        normed = normalize(rows_in, norm_gain, norm_shift)
        merged_rows = (jnp.dot(normed, qkv_weight, preferred_element_type=jnp.float32) + qkv_bias.astype(jnp.float32)).astype(jnp.bfloat16)
        return merged_rows.reshape(rows_in.shape[0], H, 3, HD)

    def finish(context, rows_in):
        summed = jnp.dot(context, out_weight, preferred_element_type=jnp.float32)
        return (summed + out_bias.astype(jnp.float32) + rows_in.astype(jnp.float32)).astype(jnp.bfloat16)

    def prefill_one(inputs):
        rows_in, cache_keys, cache_values, prefix = inputs
        merged_rows = project(rows_in)
        query_pos = prefix + jnp.arange(GROUP, dtype=jnp.int32)
        cache_pos = jnp.arange(PRE_CACHE, dtype=jnp.int32)
        key_pos = jnp.concatenate([cache_pos, query_pos])
        causal = jnp.arange(GROUP, dtype=jnp.int32)[None, :] <= jnp.arange(GROUP, dtype=jnp.int32)[:, None]
        prefix_mask = jnp.broadcast_to((cache_pos < prefix)[None, :], (GROUP, PRE_CACHE))
        allowed = jnp.concatenate([prefix_mask, causal], axis=1)
        distance = (query_pos[:, None] - key_pos[None, :]).astype(jnp.float32)
        keys_all = jnp.concatenate([cache_keys.reshape(PRE_CACHE, H, HD), merged_rows[:, :, 1]], axis=0)
        values_all = jnp.concatenate([cache_values.reshape(PRE_CACHE, H, HD), merged_rows[:, :, 2]], axis=0)
        context = attend(merged_rows[:, :, 0], keys_all, values_all, distance, allowed, slopes)
        return finish(context, rows_in)
    pre_output = lax.map(prefill_one, (pre_hidden.reshape(PREFILLS, GROUP, D), pre_keys, pre_values, prefix_lengths))
    pre_output = pre_output.reshape(PREFILLS * GROUP, D)

    def decode_one(inputs):
        row_in, slot_index = inputs
        cache_keys = lax.dynamic_index_in_dim(dec_keys, slot_index, 0, keepdims=False)
        cache_values = lax.dynamic_index_in_dim(dec_values, slot_index, 0, keepdims=False)
        length = lax.dynamic_index_in_dim(cache_lengths, slot_index, 0, keepdims=False)
        rows_in = row_in[None, :]
        merged_rows = project(rows_in)
        cache_pos = jnp.arange(DEC_CACHE, dtype=jnp.int32)
        key_pos = jnp.concatenate([cache_pos, length[None]])
        allowed = jnp.concatenate([cache_pos < length, jnp.ones((1,), dtype=bool)])[None, :]
        distance = (length - key_pos).astype(jnp.float32)[None, :]
        keys_all = jnp.concatenate([cache_keys.reshape(DEC_CACHE, H, HD), merged_rows[:, :, 1]], axis=0)
        values_all = jnp.concatenate([cache_values.reshape(DEC_CACHE, H, HD), merged_rows[:, :, 2]], axis=0)
        context = attend(merged_rows[:, :, 0], keys_all, values_all, distance, allowed, slopes)
        return finish(context, rows_in)[0]
    dec_output = lax.map(decode_one, (dec_hidden, slot_of))
    return (pre_output, dec_output)
```

```python
import math

import jax
import jax.numpy as jnp
from jax import lax
from jax.sharding import PartitionSpec as P

H = 16
HD = 128


EPSILON = 1e-05


def normalize(values, norm_gain, norm_shift):
    values = values.astype(jnp.float32)
    center = values - jnp.mean(values, axis=-1, keepdims=True)
    spread = jnp.mean(center * center, axis=-1, keepdims=True)
    scaled = center * lax.rsqrt(spread + EPSILON)
    return (scaled * norm_gain.astype(jnp.float32) + norm_shift.astype(jnp.float32)).astype(
        jnp.bfloat16
    )


def alibi_slopes(first_head, head_count, total_heads):
    head_ids = (first_head + jnp.arange(head_count, dtype=jnp.int32)).astype(jnp.float32)
    return jnp.exp2(-8.0 * (head_ids + 1.0) / total_heads)


def prefill_attention(merged_rows, cache_keys, cache_values, prefix, slopes):
    queries = merged_rows[:, :, 0]
    new_keys = merged_rows[:, :, 1]
    new_values = merged_rows[:, :, 2]
    group_size = merged_rows.shape[0]
    cache_size = cache_keys.shape[0]
    factor = 1.0 / math.sqrt(merged_rows.shape[-1])
    query_pos = prefix + jnp.arange(group_size, dtype=jnp.int32)
    cache_pos = jnp.arange(cache_size, dtype=jnp.int32)
    cache_dist = (query_pos[:, None] - cache_pos[None, :]).astype(jnp.float32)
    new_dist = (query_pos[:, None] - query_pos[None, :]).astype(jnp.float32)
    cache_scores = (
        jnp.einsum("qhd,khd->hqk", queries, cache_keys, preferred_element_type=jnp.float32) * factor
    )
    cache_scores = cache_scores - slopes[:, None, None] * cache_dist[None]
    cache_scores = jnp.where((cache_pos < prefix)[None, None, :], cache_scores, -jnp.inf)
    new_scores = (
        jnp.einsum("qhd,khd->hqk", queries, new_keys, preferred_element_type=jnp.float32) * factor
    )
    new_scores = new_scores - slopes[:, None, None] * new_dist[None]
    causal = (
        jnp.arange(group_size, dtype=jnp.int32)[None, :]
        <= jnp.arange(group_size, dtype=jnp.int32)[:, None]
    )
    new_scores = jnp.where(causal[None], new_scores, -jnp.inf)
    highest = jnp.maximum(
        jnp.max(cache_scores, axis=-1, keepdims=True), jnp.max(new_scores, axis=-1, keepdims=True)
    )
    cache_exp = jnp.exp(cache_scores - highest)
    new_exp = jnp.exp(new_scores - highest)
    denominator = jnp.sum(cache_exp, axis=-1, keepdims=True) + jnp.sum(
        new_exp, axis=-1, keepdims=True
    )
    cache_probs = (cache_exp / denominator).astype(jnp.bfloat16)
    new_probs = (new_exp / denominator).astype(jnp.bfloat16)
    context = jnp.einsum(
        "hqk,khd->qhd", cache_probs, cache_values, preferred_element_type=jnp.float32
    )
    context = context + jnp.einsum(
        "hqk,khd->qhd", new_probs, new_values, preferred_element_type=jnp.float32
    )
    return context.astype(jnp.bfloat16).reshape(group_size, -1)


def decode_attention(query_row, new_key, new_value, cache_keys, cache_values, length, slopes):
    factor = 1.0 / math.sqrt(query_row.shape[-1])
    cache_pos = jnp.arange(cache_keys.shape[0], dtype=jnp.int32)
    distance = (length - cache_pos).astype(jnp.float32)
    cache_scores = (
        jnp.einsum("hd,khd->hk", query_row, cache_keys, preferred_element_type=jnp.float32) * factor
    )
    cache_scores = cache_scores - slopes[:, None] * distance[None, :]
    cache_scores = jnp.where((cache_pos < length)[None, :], cache_scores, -jnp.inf)
    own_score = (
        jnp.einsum("hd,hd->h", query_row, new_key, preferred_element_type=jnp.float32)[:, None]
        * factor
    )
    highest = jnp.maximum(jnp.max(cache_scores, axis=-1, keepdims=True), own_score)
    cache_exp = jnp.exp(cache_scores - highest)
    own_exp = jnp.exp(own_score - highest)
    denominator = jnp.sum(cache_exp, axis=-1, keepdims=True) + own_exp
    cache_probs = (cache_exp / denominator).astype(jnp.bfloat16)
    own_prob = (own_exp / denominator).astype(jnp.bfloat16)
    context = jnp.einsum(
        "hk,khd->hd", cache_probs, cache_values, preferred_element_type=jnp.float32
    )
    context = context + own_prob.astype(jnp.float32) * new_value.astype(jnp.float32)
    return context.astype(jnp.bfloat16).reshape(-1)


def per_device(
    pre_hidden,
    dec_hidden,
    norm_gain,
    norm_shift,
    qkv_weight,
    qkv_bias,
    out_weight,
    out_bias,
    pre_keys,
    pre_values,
    dec_keys,
    dec_values,
    prefix_lengths,
    cache_lengths,
    slot_of,
):
    head_size = HD
    local_heads = qkv_weight.shape[1] // (3 * head_size)
    slopes = alibi_slopes(lax.axis_index("tensor") * local_heads, local_heads, H)
    bias_sum = out_bias.astype(jnp.float32)
    normed = normalize(pre_hidden, norm_gain, norm_shift)
    product = jnp.dot(
        lax.all_gather(normed, "tensor", axis=0, tiled=True),
        qkv_weight,
        preferred_element_type=jnp.float32,
    )
    merged_rows = (product + qkv_bias.astype(jnp.float32)).astype(jnp.bfloat16)
    group_size = merged_rows.shape[0]
    merged_rows = merged_rows.reshape(group_size, local_heads, 3, head_size)
    cache_size = pre_keys.shape[1]
    context = prefill_attention(
        merged_rows,
        pre_keys[0].reshape(cache_size, local_heads, head_size),
        pre_values[0].reshape(cache_size, local_heads, head_size),
        prefix_lengths[0],
        slopes,
    )
    summed = lax.psum_scatter(
        jnp.dot(context, out_weight, preferred_element_type=jnp.float32),
        "tensor",
        scatter_dimension=0,
        tiled=True,
    )
    pre_output = (summed + bias_sum + pre_hidden.astype(jnp.float32)).astype(jnp.bfloat16)
    slot_count = dec_hidden.shape[0]
    first_slot = lax.axis_index("dp") * slot_count
    slot_ids = first_slot + jnp.arange(slot_count, dtype=jnp.int32)
    request_ids = jnp.arange(slot_of.shape[0], dtype=jnp.int32)
    own_requests_slots = lax.dynamic_slice_in_dim(slot_of, first_slot, slot_count)
    to_slot = request_ids[:, None] == own_requests_slots[None, :]
    outgoing = jnp.zeros((slot_of.shape[0], dec_hidden.shape[1]), jnp.float32)
    for j in range(slot_count):
        outgoing = jnp.where(to_slot[:, j, None], dec_hidden[j][None, :].astype(jnp.float32), outgoing)
    arrived = lax.psum_scatter(outgoing, "dp", scatter_dimension=0, tiled=True).astype(jnp.bfloat16)
    normed_slots = normalize(arrived, norm_gain, norm_shift)
    merged_slots = (
        jnp.dot(normed_slots, qkv_weight, preferred_element_type=jnp.float32)
        + qkv_bias.astype(jnp.float32)
    ).astype(jnp.bfloat16)
    merged_slots = merged_slots.reshape(slot_count, local_heads, 3, head_size)
    dec_cache = dec_keys.shape[1]
    slot_context = jax.vmap(decode_attention, in_axes=(0, 0, 0, 0, 0, 0, None))(
        merged_slots[:, :, 0],
        merged_slots[:, :, 1],
        merged_slots[:, :, 2],
        dec_keys.reshape(slot_count, dec_cache, local_heads, head_size),
        dec_values.reshape(slot_count, dec_cache, local_heads, head_size),
        cache_lengths,
        slopes,
    )
    slot_partial = jnp.dot(slot_context, out_weight, preferred_element_type=jnp.float32)
    from_slot = slot_of[:, None] == slot_ids[None, :]
    returning = jnp.zeros((slot_of.shape[0], slot_partial.shape[1]), jnp.float32)
    for j in range(slot_count):
        returning = jnp.where(from_slot[:, j, None], slot_partial[j][None, :], returning)
    summed_all = lax.psum(returning, ("dp", "tensor"))
    slot_summed = lax.dynamic_slice_in_dim(summed_all, first_slot, slot_count)
    dec_output = (slot_summed + bias_sum + dec_hidden.astype(jnp.float32)).astype(jnp.bfloat16)
    return (pre_output, dec_output)


def solution(mesh):
    placed = (
        P(("dp", "tensor"), None),
        P("dp", None),
        P(),
        P(),
        P(None, "tensor"),
        P("tensor"),
        P("tensor", None),
        P(),
        P("dp", None, "tensor"),
        P("dp", None, "tensor"),
        P("dp", None, "tensor"),
        P("dp", None, "tensor"),
        P("dp"),
        P("dp"),
        P(),
    )
    return jax.shard_map(
        per_device,
        mesh=mesh,
        in_specs=placed,
        out_specs=(P(("dp", "tensor"), None), P("dp", None)),
        check_vma=False,
    )
```

```python
import math

import jax
import jax.numpy as jnp
from jax import lax
from jax.sharding import PartitionSpec as P

H = 16
HD = 128


EPSILON = 1e-05


def normalize(values, norm_gain, norm_shift):
    values = values.astype(jnp.float32)
    center = values - jnp.mean(values, axis=-1, keepdims=True)
    spread = jnp.mean(center * center, axis=-1, keepdims=True)
    scaled = center * lax.rsqrt(spread + EPSILON)
    return (scaled * norm_gain.astype(jnp.float32) + norm_shift.astype(jnp.float32)).astype(
        jnp.bfloat16
    )


def alibi_slopes(first_head, head_count, total_heads):
    head_ids = (first_head + jnp.arange(head_count, dtype=jnp.int32)).astype(jnp.float32)
    return jnp.exp2(-8.0 * (head_ids + 1.0) / total_heads)


def prefill_attention(merged_rows, cache_keys, cache_values, prefix, slopes):
    queries = merged_rows[:, :, 0]
    new_keys = merged_rows[:, :, 1]
    new_values = merged_rows[:, :, 2]
    group_size = merged_rows.shape[0]
    cache_size = cache_keys.shape[0]
    factor = 1.0 / math.sqrt(merged_rows.shape[-1])
    query_pos = prefix + jnp.arange(group_size, dtype=jnp.int32)
    cache_pos = jnp.arange(cache_size, dtype=jnp.int32)
    cache_dist = (query_pos[:, None] - cache_pos[None, :]).astype(jnp.float32)
    new_dist = (query_pos[:, None] - query_pos[None, :]).astype(jnp.float32)
    cache_scores = (
        jnp.einsum("qhd,khd->hqk", queries, cache_keys, preferred_element_type=jnp.float32) * factor
    )
    cache_scores = cache_scores - slopes[:, None, None] * cache_dist[None]
    cache_scores = jnp.where((cache_pos < prefix)[None, None, :], cache_scores, -jnp.inf)
    new_scores = (
        jnp.einsum("qhd,khd->hqk", queries, new_keys, preferred_element_type=jnp.float32) * factor
    )
    new_scores = new_scores - slopes[:, None, None] * new_dist[None]
    causal = (
        jnp.arange(group_size, dtype=jnp.int32)[None, :]
        <= jnp.arange(group_size, dtype=jnp.int32)[:, None]
    )
    new_scores = jnp.where(causal[None], new_scores, -jnp.inf)
    highest = jnp.maximum(
        jnp.max(cache_scores, axis=-1, keepdims=True), jnp.max(new_scores, axis=-1, keepdims=True)
    )
    cache_exp = jnp.exp(cache_scores - highest)
    new_exp = jnp.exp(new_scores - highest)
    denominator = jnp.sum(cache_exp, axis=-1, keepdims=True) + jnp.sum(
        new_exp, axis=-1, keepdims=True
    )
    cache_probs = (cache_exp / denominator).astype(jnp.bfloat16)
    new_probs = (new_exp / denominator).astype(jnp.bfloat16)
    context = jnp.einsum(
        "hqk,khd->qhd", cache_probs, cache_values, preferred_element_type=jnp.float32
    )
    context = context + jnp.einsum(
        "hqk,khd->qhd", new_probs, new_values, preferred_element_type=jnp.float32
    )
    return context.astype(jnp.bfloat16).reshape(group_size, -1)


def decode_attention(query_row, new_key, new_value, cache_keys, cache_values, length, slopes):
    factor = 1.0 / math.sqrt(query_row.shape[-1])
    cache_pos = jnp.arange(cache_keys.shape[0], dtype=jnp.int32)
    distance = (length - cache_pos).astype(jnp.float32)
    cache_scores = (
        jnp.einsum("hd,khd->hk", query_row, cache_keys, preferred_element_type=jnp.float32) * factor
    )
    cache_scores = cache_scores - slopes[:, None] * distance[None, :]
    cache_scores = jnp.where((cache_pos < length)[None, :], cache_scores, -jnp.inf)
    own_score = (
        jnp.einsum("hd,hd->h", query_row, new_key, preferred_element_type=jnp.float32)[:, None]
        * factor
    )
    highest = jnp.maximum(jnp.max(cache_scores, axis=-1, keepdims=True), own_score)
    cache_exp = jnp.exp(cache_scores - highest)
    own_exp = jnp.exp(own_score - highest)
    denominator = jnp.sum(cache_exp, axis=-1, keepdims=True) + own_exp
    cache_probs = (cache_exp / denominator).astype(jnp.bfloat16)
    own_prob = (own_exp / denominator).astype(jnp.bfloat16)
    context = jnp.einsum(
        "hk,khd->hd", cache_probs, cache_values, preferred_element_type=jnp.float32
    )
    context = context + own_prob.astype(jnp.float32) * new_value.astype(jnp.float32)
    return context.astype(jnp.bfloat16).reshape(-1)


def per_device(
    pre_hidden,
    dec_hidden,
    norm_gain,
    norm_shift,
    qkv_weight,
    qkv_bias,
    out_weight,
    out_bias,
    pre_keys,
    pre_values,
    dec_keys,
    dec_values,
    prefix_lengths,
    cache_lengths,
    slot_of,
):
    head_size = HD
    local_heads = qkv_weight.shape[1] // (3 * head_size)
    slopes = alibi_slopes(lax.axis_index("tensor") * local_heads, local_heads, H)
    bias_sum = out_bias.astype(jnp.float32)
    normed = normalize(pre_hidden, norm_gain, norm_shift)
    product = jnp.dot(
        lax.all_gather(normed, "tensor", axis=0, tiled=True),
        qkv_weight,
        preferred_element_type=jnp.float32,
    )
    merged_rows = (product + qkv_bias.astype(jnp.float32)).astype(jnp.bfloat16)
    group_size = merged_rows.shape[0]
    merged_rows = merged_rows.reshape(group_size, local_heads, 3, head_size)
    cache_size = pre_keys.shape[1]
    context = prefill_attention(
        merged_rows,
        pre_keys[0].reshape(cache_size, local_heads, head_size),
        pre_values[0].reshape(cache_size, local_heads, head_size),
        prefix_lengths[0],
        slopes,
    )
    summed = lax.psum_scatter(
        jnp.dot(context, out_weight, preferred_element_type=jnp.float32),
        "tensor",
        scatter_dimension=0,
        tiled=True,
    )
    pre_output = (summed + bias_sum + pre_hidden.astype(jnp.float32)).astype(jnp.bfloat16)
    slot_count = dec_hidden.shape[0]
    dp_size = lax.axis_size("dp")
    tensor_size = lax.axis_size("tensor")
    group = lax.axis_index("dp")
    member = lax.axis_index("tensor")
    first_slot = group * slot_count
    shifted_rows = [dec_hidden] + [
        lax.ppermute(dec_hidden, "dp", [(i, (i + k) % dp_size) for i in range(dp_size)])
        for k in range(1, dp_size)
    ]
    shifted_rows = jnp.concatenate(shifted_rows, axis=0)
    slot_ids = first_slot + jnp.arange(slot_count, dtype=jnp.int32)
    request_ids = jnp.arange(slot_of.shape[0], dtype=jnp.int32)
    uses_slot = slot_of[None, :] == slot_ids[:, None]
    request_of_slot = jnp.sum(jnp.where(uses_slot, request_ids[None, :], 0), axis=1)
    arrival = ((group - request_of_slot // slot_count) % dp_size) * slot_count + request_of_slot % slot_count
    pick = (arrival[:, None] == jnp.arange(shifted_rows.shape[0], dtype=jnp.int32)[None, :]).astype(
        jnp.bfloat16
    )
    arrived = jnp.dot(pick, shifted_rows, preferred_element_type=jnp.float32).astype(jnp.bfloat16)
    normed_slots = normalize(arrived, norm_gain, norm_shift)
    merged_slots = (
        jnp.dot(normed_slots, qkv_weight, preferred_element_type=jnp.float32)
        + qkv_bias.astype(jnp.float32)
    ).astype(jnp.bfloat16)
    merged_slots = merged_slots.reshape(slot_count, local_heads, 3, head_size)
    dec_cache = dec_keys.shape[1]
    slot_context = jax.vmap(decode_attention, in_axes=(0, 0, 0, 0, 0, 0, None))(
        merged_slots[:, :, 0],
        merged_slots[:, :, 1],
        merged_slots[:, :, 2],
        dec_keys.reshape(slot_count, dec_cache, local_heads, head_size),
        dec_values.reshape(slot_count, dec_cache, local_heads, head_size),
        cache_lengths,
        slopes,
    )
    slot_partial = jnp.dot(slot_context, out_weight, preferred_element_type=jnp.float32)
    partials = jnp.stack(
        [slot_partial]
        + [
            lax.ppermute(slot_partial, "tensor", [(i, (i + k) % tensor_size) for i in range(tensor_size)])
            for k in range(1, tensor_size)
        ]
    )
    slot_summed = partials[member % tensor_size]
    for source in range(1, tensor_size):
        slot_summed = slot_summed + partials[(member - source) % tensor_size]
    slot_rows = (slot_summed + bias_sum + arrived.astype(jnp.float32)).astype(jnp.bfloat16)
    returned = [slot_rows] + [
        lax.ppermute(slot_rows, "dp", [(i, (i + k) % dp_size) for i in range(dp_size)])
        for k in range(1, dp_size)
    ]
    returned = jnp.concatenate(returned, axis=0)
    slot_wanted = lax.dynamic_slice_in_dim(slot_of, first_slot, slot_count)
    back = ((group - slot_wanted // slot_count) % dp_size) * slot_count + slot_wanted % slot_count
    take = (back[:, None] == jnp.arange(returned.shape[0], dtype=jnp.int32)[None, :]).astype(jnp.bfloat16)
    dec_output = jnp.dot(take, returned, preferred_element_type=jnp.float32).astype(jnp.bfloat16)
    return (pre_output, dec_output)


def solution(mesh):
    placed = (
        P(("dp", "tensor"), None),
        P("dp", None),
        P(),
        P(),
        P(None, "tensor"),
        P("tensor"),
        P("tensor", None),
        P(),
        P("dp", None, "tensor"),
        P("dp", None, "tensor"),
        P("dp", None, "tensor"),
        P("dp", None, "tensor"),
        P("dp"),
        P("dp"),
        P(),
    )
    return jax.shard_map(
        per_device,
        mesh=mesh,
        in_specs=placed,
        out_specs=(P(("dp", "tensor"), None), P("dp", None)),
        check_vma=False,
    )
```

```python
import math

import jax
import jax.numpy as jnp
from jax import lax
from jax.sharding import PartitionSpec as P

H = 16
HD = 128


EPSILON = 1e-05


def normalize(values, norm_gain, norm_shift):
    values = values.astype(jnp.float32)
    center = values - jnp.mean(values, axis=-1, keepdims=True)
    spread = jnp.mean(center * center, axis=-1, keepdims=True)
    scaled = center * lax.rsqrt(spread + EPSILON)
    return (scaled * norm_gain.astype(jnp.float32) + norm_shift.astype(jnp.float32)).astype(
        jnp.bfloat16
    )


def alibi_slopes(first_head, head_count, total_heads):
    head_ids = (first_head + jnp.arange(head_count, dtype=jnp.int32)).astype(jnp.float32)
    return jnp.exp2(-8.0 * (head_ids + 1.0) / total_heads)


def prefill_attention(queries, query_tok, new_keys, new_values, key_tok, cache_keys, cache_values, prefix, slopes):
    cache_size = cache_keys.shape[0]
    factor = 1.0 / math.sqrt(queries.shape[-1])
    query_pos = prefix + query_tok
    cache_pos = jnp.arange(cache_size, dtype=jnp.int32)
    cache_dist = (query_pos[:, None] - cache_pos[None, :]).astype(jnp.float32)
    new_dist = (query_tok[:, None] - key_tok[None, :]).astype(jnp.float32)
    cache_scores = (
        jnp.einsum("qhd,khd->hqk", queries, cache_keys, preferred_element_type=jnp.float32) * factor
    )
    cache_scores = cache_scores - slopes[:, None, None] * cache_dist[None]
    cache_scores = jnp.where((cache_pos < prefix)[None, None, :], cache_scores, -jnp.inf)
    new_scores = (
        jnp.einsum("qhd,khd->hqk", queries, new_keys, preferred_element_type=jnp.float32) * factor
    )
    new_scores = new_scores - slopes[:, None, None] * new_dist[None]
    causal = key_tok[None, :] <= query_tok[:, None]
    new_scores = jnp.where(causal[None], new_scores, -jnp.inf)
    highest = jnp.maximum(
        jnp.max(cache_scores, axis=-1, keepdims=True), jnp.max(new_scores, axis=-1, keepdims=True)
    )
    cache_exp = jnp.exp(cache_scores - highest)
    new_exp = jnp.exp(new_scores - highest)
    denominator = jnp.sum(cache_exp, axis=-1, keepdims=True) + jnp.sum(
        new_exp, axis=-1, keepdims=True
    )
    cache_probs = (cache_exp / denominator).astype(jnp.bfloat16)
    new_probs = (new_exp / denominator).astype(jnp.bfloat16)
    context = jnp.einsum(
        "hqk,khd->qhd", cache_probs, cache_values, preferred_element_type=jnp.float32
    )
    context = context + jnp.einsum(
        "hqk,khd->qhd", new_probs, new_values, preferred_element_type=jnp.float32
    )
    return context.astype(jnp.bfloat16).reshape(queries.shape[0], -1)


def decode_attention(query_row, new_key, new_value, cache_keys, cache_values, length, slopes):
    factor = 1.0 / math.sqrt(query_row.shape[-1])
    cache_pos = jnp.arange(cache_keys.shape[0], dtype=jnp.int32)
    distance = (length - cache_pos).astype(jnp.float32)
    cache_scores = (
        jnp.einsum("hd,khd->hk", query_row, cache_keys, preferred_element_type=jnp.float32) * factor
    )
    cache_scores = cache_scores - slopes[:, None] * distance[None, :]
    cache_scores = jnp.where((cache_pos < length)[None, :], cache_scores, -jnp.inf)
    own_score = (
        jnp.einsum("hd,hd->h", query_row, new_key, preferred_element_type=jnp.float32)[:, None]
        * factor
    )
    highest = jnp.maximum(jnp.max(cache_scores, axis=-1, keepdims=True), own_score)
    cache_exp = jnp.exp(cache_scores - highest)
    own_exp = jnp.exp(own_score - highest)
    denominator = jnp.sum(cache_exp, axis=-1, keepdims=True) + own_exp
    cache_probs = (cache_exp / denominator).astype(jnp.bfloat16)
    own_prob = (own_exp / denominator).astype(jnp.bfloat16)
    context = jnp.einsum(
        "hk,khd->hd", cache_probs, cache_values, preferred_element_type=jnp.float32
    )
    context = context + own_prob.astype(jnp.float32) * new_value.astype(jnp.float32)
    return context.astype(jnp.bfloat16).reshape(-1)


def per_device(
    pre_hidden,
    dec_hidden,
    norm_gain,
    norm_shift,
    qkv_weight,
    qkv_bias,
    out_weight,
    out_bias,
    pre_keys,
    pre_values,
    dec_keys,
    dec_values,
    prefix_lengths,
    cache_lengths,
    slot_of,
):
    head_size = HD
    local_heads = qkv_weight.shape[1] // (3 * head_size)
    slopes = alibi_slopes(lax.axis_index("tensor") * local_heads, local_heads, H)
    bias_sum = out_bias.astype(jnp.float32)
    tensor_size = lax.axis_size("tensor")
    chips = tensor_size // 2
    member = lax.axis_index("tensor")
    chip = member // 2
    core = member % 2
    sibling = [(i, i ^ 1) for i in range(tensor_size)]

    def across(k):
        return [(i, ((i // 2 + k) % chips) * 2 + i % 2) for i in range(tensor_size)]

    block = pre_hidden.shape[0]
    normed = normalize(pre_hidden, norm_gain, norm_shift)
    same_core = jnp.concatenate(
        [normed] + [lax.ppermute(normed, "tensor", across(k)) for k in range(1, chips)], axis=0
    )
    other_core = lax.ppermute(same_core, "tensor", sibling)
    tokens = jnp.concatenate([same_core, other_core], axis=0)
    block_chip = (chip - jnp.arange(chips, dtype=jnp.int32)) % chips
    block_member = jnp.concatenate([block_chip * 2 + core, block_chip * 2 + (1 - core)])
    token_index = block_member[:, None] * block + jnp.arange(block, dtype=jnp.int32)[None, :]
    product = jnp.dot(tokens, qkv_weight, preferred_element_type=jnp.float32)
    merged_rows = (product + qkv_bias.astype(jnp.float32)).astype(jnp.bfloat16)
    merged_rows = merged_rows.reshape(tensor_size, block, local_heads, 3, head_size)
    all_tok = token_index.reshape(-1)
    new_keys = merged_rows[:, :, :, 1].reshape(tensor_size * block, local_heads, head_size)
    new_values = merged_rows[:, :, :, 2].reshape(tensor_size * block, local_heads, head_size)
    cache_size = pre_keys.shape[1]
    cache_keys = pre_keys[0].reshape(cache_size, local_heads, head_size)
    cache_values = pre_values[0].reshape(cache_size, local_heads, head_size)
    chunks = 2
    part = block // chunks
    pieces = []
    for h in range(chunks):
        rows = slice(h * part, (h + 1) * part)
        queries = merged_rows[:, rows, :, 0].reshape(tensor_size * part, local_heads, head_size)
        query_tok = token_index[:, rows].reshape(-1)
        context = prefill_attention(
            queries, query_tok, new_keys, new_values, all_tok, cache_keys, cache_values,
            prefix_lengths[0], slopes,
        )
        partial = jnp.dot(context, out_weight, preferred_element_type=jnp.float32)
        partial = partial.reshape(2, chips, part, partial.shape[-1])
        chip_sum = partial[0] + lax.ppermute(partial[1], "tensor", sibling)
        total = chip_sum[0]
        for k in range(1, chips):
            total = total + lax.ppermute(chip_sum[k], "tensor", across(-k))
        pieces.append(total)
    summed = jnp.concatenate(pieces, axis=0)
    pre_output = (summed + bias_sum + pre_hidden.astype(jnp.float32)).astype(jnp.bfloat16)
    slot_count = dec_hidden.shape[0]
    dp_size = lax.axis_size("dp")
    group = lax.axis_index("dp")
    first_slot = group * slot_count
    shifted_rows = [dec_hidden] + [
        lax.ppermute(dec_hidden, "dp", [(i, (i + k) % dp_size) for i in range(dp_size)])
        for k in range(1, dp_size)
    ]
    shifted_rows = jnp.concatenate(shifted_rows, axis=0)
    slot_ids = first_slot + jnp.arange(slot_count, dtype=jnp.int32)
    request_ids = jnp.arange(slot_of.shape[0], dtype=jnp.int32)
    uses_slot = slot_of[None, :] == slot_ids[:, None]
    request_of_slot = jnp.sum(jnp.where(uses_slot, request_ids[None, :], 0), axis=1)
    arrival = ((group - request_of_slot // slot_count) % dp_size) * slot_count + request_of_slot % slot_count
    pick = (arrival[:, None] == jnp.arange(shifted_rows.shape[0], dtype=jnp.int32)[None, :]).astype(
        jnp.bfloat16
    )
    arrived = jnp.dot(pick, shifted_rows, preferred_element_type=jnp.float32).astype(jnp.bfloat16)
    normed_slots = normalize(arrived, norm_gain, norm_shift)
    merged_slots = (
        jnp.dot(normed_slots, qkv_weight, preferred_element_type=jnp.float32)
        + qkv_bias.astype(jnp.float32)
    ).astype(jnp.bfloat16)
    merged_slots = merged_slots.reshape(slot_count, local_heads, 3, head_size)
    dec_cache = dec_keys.shape[1]
    slot_context = jax.vmap(decode_attention, in_axes=(0, 0, 0, 0, 0, 0, None))(
        merged_slots[:, :, 0],
        merged_slots[:, :, 1],
        merged_slots[:, :, 2],
        dec_keys.reshape(slot_count, dec_cache, local_heads, head_size),
        dec_values.reshape(slot_count, dec_cache, local_heads, head_size),
        cache_lengths,
        slopes,
    )
    slot_partial = jnp.dot(slot_context, out_weight, preferred_element_type=jnp.float32)
    partials = jnp.stack(
        [slot_partial]
        + [
            lax.ppermute(slot_partial, "tensor", [(i, (i + k) % tensor_size) for i in range(tensor_size)])
            for k in range(1, tensor_size)
        ]
    )
    slot_summed = partials[member % tensor_size]
    for source in range(1, tensor_size):
        slot_summed = slot_summed + partials[(member - source) % tensor_size]
    slot_rows = (slot_summed + bias_sum + arrived.astype(jnp.float32)).astype(jnp.bfloat16)
    returned = [slot_rows] + [
        lax.ppermute(slot_rows, "dp", [(i, (i + k) % dp_size) for i in range(dp_size)])
        for k in range(1, dp_size)
    ]
    returned = jnp.concatenate(returned, axis=0)
    slot_wanted = lax.dynamic_slice_in_dim(slot_of, first_slot, slot_count)
    back = ((group - slot_wanted // slot_count) % dp_size) * slot_count + slot_wanted % slot_count
    take = (back[:, None] == jnp.arange(returned.shape[0], dtype=jnp.int32)[None, :]).astype(jnp.bfloat16)
    dec_output = jnp.dot(take, returned, preferred_element_type=jnp.float32).astype(jnp.bfloat16)
    return (pre_output, dec_output)


def solution(mesh):
    placed = (
        P(("dp", "tensor"), None),
        P("dp", None),
        P(),
        P(),
        P(None, "tensor"),
        P("tensor"),
        P("tensor", None),
        P(),
        P("dp", None, "tensor"),
        P("dp", None, "tensor"),
        P("dp", None, "tensor"),
        P("dp", None, "tensor"),
        P("dp"),
        P("dp"),
        P(),
    )
    return jax.shard_map(
        per_device,
        mesh=mesh,
        in_specs=placed,
        out_specs=(P(("dp", "tensor"), None), P("dp", None)),
        check_vma=False,
    )
```

```python
import math

import jax
import jax.numpy as jnp
from jax import lax
from jax.sharding import PartitionSpec as P
from jax.experimental import pallas as pl
from jax.experimental.pallas import tpu as pltpu
import functools

H = 16
HD = 128


EPSILON = 1e-05


def normalize(values, norm_gain, norm_shift):
    values = values.astype(jnp.float32)
    center = values - jnp.mean(values, axis=-1, keepdims=True)
    spread = jnp.mean(center * center, axis=-1, keepdims=True)
    scaled = center * lax.rsqrt(spread + EPSILON)
    return (scaled * norm_gain.astype(jnp.float32) + norm_shift.astype(jnp.float32)).astype(
        jnp.bfloat16
    )


def alibi_slopes(first_head, head_count, total_heads):
    head_ids = (first_head + jnp.arange(head_count, dtype=jnp.int32)).astype(jnp.float32)
    return jnp.exp2(-8.0 * (head_ids + 1.0) / total_heads)


def prefill_attention(merged_rows, cache_keys, cache_values, prefix, slopes):
    queries = merged_rows[:, :, 0]
    new_keys = merged_rows[:, :, 1]
    new_values = merged_rows[:, :, 2]
    group_size = merged_rows.shape[0]
    cache_size = cache_keys.shape[0]
    factor = 1.0 / math.sqrt(merged_rows.shape[-1])
    query_pos = prefix + jnp.arange(group_size, dtype=jnp.int32)
    cache_pos = jnp.arange(cache_size, dtype=jnp.int32)
    cache_dist = (query_pos[:, None] - cache_pos[None, :]).astype(jnp.float32)
    new_dist = (query_pos[:, None] - query_pos[None, :]).astype(jnp.float32)
    cache_scores = (
        jnp.einsum("qhd,khd->hqk", queries, cache_keys, preferred_element_type=jnp.float32) * factor
    )
    cache_scores = cache_scores - slopes[:, None, None] * cache_dist[None]
    cache_scores = jnp.where((cache_pos < prefix)[None, None, :], cache_scores, -jnp.inf)
    new_scores = (
        jnp.einsum("qhd,khd->hqk", queries, new_keys, preferred_element_type=jnp.float32) * factor
    )
    new_scores = new_scores - slopes[:, None, None] * new_dist[None]
    causal = (
        jnp.arange(group_size, dtype=jnp.int32)[None, :]
        <= jnp.arange(group_size, dtype=jnp.int32)[:, None]
    )
    new_scores = jnp.where(causal[None], new_scores, -jnp.inf)
    highest = jnp.maximum(
        jnp.max(cache_scores, axis=-1, keepdims=True), jnp.max(new_scores, axis=-1, keepdims=True)
    )
    cache_exp = jnp.exp(cache_scores - highest)
    new_exp = jnp.exp(new_scores - highest)
    denominator = jnp.sum(cache_exp, axis=-1, keepdims=True) + jnp.sum(
        new_exp, axis=-1, keepdims=True
    )
    cache_probs = (cache_exp / denominator).astype(jnp.bfloat16)
    new_probs = (new_exp / denominator).astype(jnp.bfloat16)
    context = jnp.einsum(
        "hqk,khd->qhd", cache_probs, cache_values, preferred_element_type=jnp.float32
    )
    context = context + jnp.einsum(
        "hqk,khd->qhd", new_probs, new_values, preferred_element_type=jnp.float32
    )
    return context.astype(jnp.bfloat16).reshape(group_size, -1)


def _prefill_kernel(prefix_ref, slopes_ref, q_ref, kn_ref, vn_ref, kc_ref, vc_ref, o_ref, *, tq):
    h = pl.program_id(0)
    i = pl.program_id(1)
    prefix = prefix_ref[0]
    slope = slopes_ref[h]
    factor = 1.0 / math.sqrt(q_ref.shape[-1])
    q = q_ref[...]
    dims = (((1,), (1,)), ((), ()))
    cache_size = kc_ref.shape[0]
    group = kn_ref.shape[0]
    q_tok = i * tq + lax.broadcasted_iota(jnp.int32, (tq, 1), 0)
    q_pos = prefix + q_tok
    c_pos = lax.broadcasted_iota(jnp.int32, (1, cache_size), 1)
    k_tok = lax.broadcasted_iota(jnp.int32, (1, group), 1)
    s_c = lax.dot_general(q, kc_ref[...], dims, preferred_element_type=jnp.float32) * factor
    s_c = s_c - slope * (q_pos - c_pos).astype(jnp.float32)
    s_c = jnp.where(c_pos < prefix, s_c, -jnp.inf)
    s_n = lax.dot_general(q, kn_ref[...], dims, preferred_element_type=jnp.float32) * factor
    s_n = s_n - slope * (q_tok - k_tok).astype(jnp.float32)
    s_n = jnp.where(k_tok <= q_tok, s_n, -jnp.inf)
    m = jnp.maximum(jnp.max(s_c, axis=-1, keepdims=True), jnp.max(s_n, axis=-1, keepdims=True))
    e_c = jnp.exp(s_c - m)
    e_n = jnp.exp(s_n - m)
    l = jnp.sum(e_c, axis=-1, keepdims=True) + jnp.sum(e_n, axis=-1, keepdims=True)
    p_c = (e_c / l).astype(jnp.bfloat16)
    p_n = (e_n / l).astype(jnp.bfloat16)
    ctx = jnp.dot(p_c, vc_ref[...], preferred_element_type=jnp.float32)
    ctx = ctx + jnp.dot(p_n, vn_ref[...], preferred_element_type=jnp.float32)
    o_ref[...] = ctx.astype(o_ref.dtype)

def prefill_attention_kernel(merged, cache_keys, cache_values, prefix, slopes, head_size, tq=256):
    group = merged.shape[0]
    heads = merged.shape[1] // (3 * head_size)
    cache_size = cache_keys.shape[0]
    col = lambda c: (lambda h, i, *_: (0, h * 3 + c))
    return pl.pallas_call(
        functools.partial(_prefill_kernel, tq=tq),
        out_shape=jax.ShapeDtypeStruct((group, heads * head_size), jnp.bfloat16),
        grid_spec=pltpu.PrefetchScalarGridSpec(
            num_scalar_prefetch=2,
            grid=(heads, group // tq),
            in_specs=[
                pl.BlockSpec((tq, head_size), lambda h, i, *_: (i, h * 3)),
                pl.BlockSpec((group, head_size), col(1)),
                pl.BlockSpec((group, head_size), col(2)),
                pl.BlockSpec((cache_size, head_size), lambda h, i, *_: (0, h)),
                pl.BlockSpec((cache_size, head_size), lambda h, i, *_: (0, h)),
            ],
            out_specs=pl.BlockSpec((tq, head_size), lambda h, i, *_: (i, h)),
        ),
        cost_estimate=pl.CostEstimate(
            flops=4 * heads * group * (group + cache_size) * head_size,
            transcendentals=heads * group * (group + cache_size),
            bytes_accessed=2 * (group * heads * 3 * head_size + 2 * cache_size * heads * head_size + group * heads * head_size),
        ),
    )(prefix, slopes, merged, merged, merged, cache_keys, cache_values)


def decode_attention(query_row, new_key, new_value, cache_keys, cache_values, length, slopes):
    factor = 1.0 / math.sqrt(query_row.shape[-1])
    cache_pos = jnp.arange(cache_keys.shape[0], dtype=jnp.int32)
    distance = (length - cache_pos).astype(jnp.float32)
    cache_scores = (
        jnp.einsum("hd,khd->hk", query_row, cache_keys, preferred_element_type=jnp.float32) * factor
    )
    cache_scores = cache_scores - slopes[:, None] * distance[None, :]
    cache_scores = jnp.where((cache_pos < length)[None, :], cache_scores, -jnp.inf)
    own_score = (
        jnp.einsum("hd,hd->h", query_row, new_key, preferred_element_type=jnp.float32)[:, None]
        * factor
    )
    highest = jnp.maximum(jnp.max(cache_scores, axis=-1, keepdims=True), own_score)
    cache_exp = jnp.exp(cache_scores - highest)
    own_exp = jnp.exp(own_score - highest)
    denominator = jnp.sum(cache_exp, axis=-1, keepdims=True) + own_exp
    cache_probs = (cache_exp / denominator).astype(jnp.bfloat16)
    own_prob = (own_exp / denominator).astype(jnp.bfloat16)
    context = jnp.einsum(
        "hk,khd->hd", cache_probs, cache_values, preferred_element_type=jnp.float32
    )
    context = context + own_prob.astype(jnp.float32) * new_value.astype(jnp.float32)
    return context.astype(jnp.bfloat16).reshape(-1)


def per_device(
    pre_hidden,
    dec_hidden,
    norm_gain,
    norm_shift,
    qkv_weight,
    qkv_bias,
    out_weight,
    out_bias,
    pre_keys,
    pre_values,
    dec_keys,
    dec_values,
    prefix_lengths,
    cache_lengths,
    slot_of,
):
    head_size = HD
    local_heads = qkv_weight.shape[1] // (3 * head_size)
    slopes = alibi_slopes(lax.axis_index("tensor") * local_heads, local_heads, H)
    bias_sum = out_bias.astype(jnp.float32)
    normed = normalize(pre_hidden, norm_gain, norm_shift)
    product = jnp.dot(
        lax.all_gather(normed, "tensor", axis=0, tiled=True),
        qkv_weight,
        preferred_element_type=jnp.float32,
    )
    merged_rows = (product + qkv_bias.astype(jnp.float32)).astype(jnp.bfloat16)
    context = prefill_attention_kernel(
        merged_rows, pre_keys[0], pre_values[0], prefix_lengths, slopes, head_size
    )
    summed = lax.psum_scatter(
        jnp.dot(context, out_weight, preferred_element_type=jnp.float32),
        "tensor",
        scatter_dimension=0,
        tiled=True,
    )
    pre_output = (summed + bias_sum + pre_hidden.astype(jnp.float32)).astype(jnp.bfloat16)
    slot_count = dec_hidden.shape[0]
    dp_size = lax.axis_size("dp")
    tensor_size = lax.axis_size("tensor")
    group = lax.axis_index("dp")
    member = lax.axis_index("tensor")
    first_slot = group * slot_count
    shifted_rows = [dec_hidden] + [
        lax.ppermute(dec_hidden, "dp", [(i, (i + k) % dp_size) for i in range(dp_size)])
        for k in range(1, dp_size)
    ]
    shifted_rows = jnp.concatenate(shifted_rows, axis=0)
    slot_ids = first_slot + jnp.arange(slot_count, dtype=jnp.int32)
    request_ids = jnp.arange(slot_of.shape[0], dtype=jnp.int32)
    uses_slot = slot_of[None, :] == slot_ids[:, None]
    request_of_slot = jnp.sum(jnp.where(uses_slot, request_ids[None, :], 0), axis=1)
    arrival = ((group - request_of_slot // slot_count) % dp_size) * slot_count + request_of_slot % slot_count
    pick = (arrival[:, None] == jnp.arange(shifted_rows.shape[0], dtype=jnp.int32)[None, :]).astype(
        jnp.bfloat16
    )
    arrived = jnp.dot(pick, shifted_rows, preferred_element_type=jnp.float32).astype(jnp.bfloat16)
    normed_slots = normalize(arrived, norm_gain, norm_shift)
    merged_slots = (
        jnp.dot(normed_slots, qkv_weight, preferred_element_type=jnp.float32)
        + qkv_bias.astype(jnp.float32)
    ).astype(jnp.bfloat16)
    merged_slots = merged_slots.reshape(slot_count, local_heads, 3, head_size)
    dec_cache = dec_keys.shape[1]
    slot_context = jax.vmap(decode_attention, in_axes=(0, 0, 0, 0, 0, 0, None))(
        merged_slots[:, :, 0],
        merged_slots[:, :, 1],
        merged_slots[:, :, 2],
        dec_keys.reshape(slot_count, dec_cache, local_heads, head_size),
        dec_values.reshape(slot_count, dec_cache, local_heads, head_size),
        cache_lengths,
        slopes,
    )
    slot_partial = jnp.dot(slot_context, out_weight, preferred_element_type=jnp.float32)
    partials = jnp.stack(
        [slot_partial]
        + [
            lax.ppermute(slot_partial, "tensor", [(i, (i + k) % tensor_size) for i in range(tensor_size)])
            for k in range(1, tensor_size)
        ]
    )
    slot_summed = partials[member % tensor_size]
    for source in range(1, tensor_size):
        slot_summed = slot_summed + partials[(member - source) % tensor_size]
    slot_rows = (slot_summed + bias_sum + arrived.astype(jnp.float32)).astype(jnp.bfloat16)
    returned = [slot_rows] + [
        lax.ppermute(slot_rows, "dp", [(i, (i + k) % dp_size) for i in range(dp_size)])
        for k in range(1, dp_size)
    ]
    returned = jnp.concatenate(returned, axis=0)
    slot_wanted = lax.dynamic_slice_in_dim(slot_of, first_slot, slot_count)
    back = ((group - slot_wanted // slot_count) % dp_size) * slot_count + slot_wanted % slot_count
    take = (back[:, None] == jnp.arange(returned.shape[0], dtype=jnp.int32)[None, :]).astype(jnp.bfloat16)
    dec_output = jnp.dot(take, returned, preferred_element_type=jnp.float32).astype(jnp.bfloat16)
    return (pre_output, dec_output)


def solution(mesh):
    placed = (
        P(("dp", "tensor"), None),
        P("dp", None),
        P(),
        P(),
        P(None, "tensor"),
        P("tensor"),
        P("tensor", None),
        P(),
        P("dp", None, "tensor"),
        P("dp", None, "tensor"),
        P("dp", None, "tensor"),
        P("dp", None, "tensor"),
        P("dp"),
        P("dp"),
        P(),
    )
    return jax.shard_map(
        per_device,
        mesh=mesh,
        in_specs=placed,
        out_specs=(P(("dp", "tensor"), None), P("dp", None)),
        check_vma=False,
    )
```

```python
import math

import jax
import jax.numpy as jnp
from jax import lax
from jax.sharding import PartitionSpec as P
from jax.experimental import pallas as pl
from jax.experimental.pallas import tpu as pltpu
import functools

H = 16
HD = 128


EPSILON = 1e-05


def normalize(values, norm_gain, norm_shift):
    values = values.astype(jnp.float32)
    center = values - jnp.mean(values, axis=-1, keepdims=True)
    spread = jnp.mean(center * center, axis=-1, keepdims=True)
    scaled = center * lax.rsqrt(spread + EPSILON)
    return (scaled * norm_gain.astype(jnp.float32) + norm_shift.astype(jnp.float32)).astype(
        jnp.bfloat16
    )


def alibi_slopes(first_head, head_count, total_heads):
    head_ids = (first_head + jnp.arange(head_count, dtype=jnp.int32)).astype(jnp.float32)
    return jnp.exp2(-8.0 * (head_ids + 1.0) / total_heads)


def prefill_attention(merged_rows, cache_keys, cache_values, prefix, slopes):
    queries = merged_rows[:, :, 0]
    new_keys = merged_rows[:, :, 1]
    new_values = merged_rows[:, :, 2]
    group_size = merged_rows.shape[0]
    cache_size = cache_keys.shape[0]
    factor = 1.0 / math.sqrt(merged_rows.shape[-1])
    query_pos = prefix + jnp.arange(group_size, dtype=jnp.int32)
    cache_pos = jnp.arange(cache_size, dtype=jnp.int32)
    cache_dist = (query_pos[:, None] - cache_pos[None, :]).astype(jnp.float32)
    new_dist = (query_pos[:, None] - query_pos[None, :]).astype(jnp.float32)
    cache_scores = (
        jnp.einsum("qhd,khd->hqk", queries, cache_keys, preferred_element_type=jnp.float32) * factor
    )
    cache_scores = cache_scores - slopes[:, None, None] * cache_dist[None]
    cache_scores = jnp.where((cache_pos < prefix)[None, None, :], cache_scores, -jnp.inf)
    new_scores = (
        jnp.einsum("qhd,khd->hqk", queries, new_keys, preferred_element_type=jnp.float32) * factor
    )
    new_scores = new_scores - slopes[:, None, None] * new_dist[None]
    causal = (
        jnp.arange(group_size, dtype=jnp.int32)[None, :]
        <= jnp.arange(group_size, dtype=jnp.int32)[:, None]
    )
    new_scores = jnp.where(causal[None], new_scores, -jnp.inf)
    highest = jnp.maximum(
        jnp.max(cache_scores, axis=-1, keepdims=True), jnp.max(new_scores, axis=-1, keepdims=True)
    )
    cache_exp = jnp.exp(cache_scores - highest)
    new_exp = jnp.exp(new_scores - highest)
    denominator = jnp.sum(cache_exp, axis=-1, keepdims=True) + jnp.sum(
        new_exp, axis=-1, keepdims=True
    )
    cache_probs = (cache_exp / denominator).astype(jnp.bfloat16)
    new_probs = (new_exp / denominator).astype(jnp.bfloat16)
    context = jnp.einsum(
        "hqk,khd->qhd", cache_probs, cache_values, preferred_element_type=jnp.float32
    )
    context = context + jnp.einsum(
        "hqk,khd->qhd", new_probs, new_values, preferred_element_type=jnp.float32
    )
    return context.astype(jnp.bfloat16).reshape(group_size, -1)


def _prefill_kernel(prefix_ref, slopes_ref, q_ref, kn_ref, vn_ref, kc_ref, vc_ref, o_ref, *, tq, chunks, chunk):
    h = pl.program_id(0)
    i = pl.program_id(1) * chunks + chunk
    prefix = prefix_ref[0]
    slope = slopes_ref[h]
    factor = 1.0 / math.sqrt(q_ref.shape[-1])
    q = q_ref[...]
    dims = (((1,), (1,)), ((), ()))
    cache_size = kc_ref.shape[0]
    group = kn_ref.shape[0]
    q_tok = i * tq + lax.broadcasted_iota(jnp.int32, (tq, 1), 0)
    q_pos = prefix + q_tok
    c_pos = lax.broadcasted_iota(jnp.int32, (1, cache_size), 1)
    k_tok = lax.broadcasted_iota(jnp.int32, (1, group), 1)
    s_c = lax.dot_general(q, kc_ref[...], dims, preferred_element_type=jnp.float32) * factor
    s_c = s_c - slope * (q_pos - c_pos).astype(jnp.float32)
    s_c = jnp.where(c_pos < prefix, s_c, -jnp.inf)
    s_n = lax.dot_general(q, kn_ref[...], dims, preferred_element_type=jnp.float32) * factor
    s_n = s_n - slope * (q_tok - k_tok).astype(jnp.float32)
    s_n = jnp.where(k_tok <= q_tok, s_n, -jnp.inf)
    m = jnp.maximum(jnp.max(s_c, axis=-1, keepdims=True), jnp.max(s_n, axis=-1, keepdims=True))
    e_c = jnp.exp(s_c - m)
    e_n = jnp.exp(s_n - m)
    l = jnp.sum(e_c, axis=-1, keepdims=True) + jnp.sum(e_n, axis=-1, keepdims=True)
    p_c = (e_c / l).astype(jnp.bfloat16)
    p_n = (e_n / l).astype(jnp.bfloat16)
    ctx = jnp.dot(p_c, vc_ref[...], preferred_element_type=jnp.float32)
    ctx = ctx + jnp.dot(p_n, vn_ref[...], preferred_element_type=jnp.float32)
    o_ref[...] = ctx.astype(o_ref.dtype)

def prefill_attention_kernel(merged, cache_keys, cache_values, prefix, slopes, head_size, tq, chunks, chunk):
    group = merged.shape[0]
    heads = merged.shape[1] // (3 * head_size)
    cache_size = cache_keys.shape[0]
    col = lambda c: (lambda h, i, *_: (0, h * 3 + c))
    return pl.pallas_call(
        functools.partial(_prefill_kernel, tq=tq, chunks=chunks, chunk=chunk),
        out_shape=jax.ShapeDtypeStruct((group // chunks, heads * head_size), jnp.bfloat16),
        grid_spec=pltpu.PrefetchScalarGridSpec(
            num_scalar_prefetch=2,
            grid=(heads, group // (tq * chunks)),
            in_specs=[
                pl.BlockSpec((tq, head_size), lambda h, i, *_: (i * chunks + chunk, h * 3)),
                pl.BlockSpec((group, head_size), col(1)),
                pl.BlockSpec((group, head_size), col(2)),
                pl.BlockSpec((cache_size, head_size), lambda h, i, *_: (0, h)),
                pl.BlockSpec((cache_size, head_size), lambda h, i, *_: (0, h)),
            ],
            out_specs=pl.BlockSpec((tq, head_size), lambda h, i, *_: (i, h)),
        ),
        cost_estimate=pl.CostEstimate(
            flops=4 * heads * group * (group + cache_size) * head_size // chunks,
            transcendentals=heads * group * (group + cache_size) // chunks,
            bytes_accessed=2 * (group * heads * 3 * head_size + 2 * cache_size * heads * head_size) // chunks,
        ),
    )(prefix, slopes, merged, merged, merged, cache_keys, cache_values)


def decode_attention(query_row, new_key, new_value, cache_keys, cache_values, length, slopes):
    factor = 1.0 / math.sqrt(query_row.shape[-1])
    cache_pos = jnp.arange(cache_keys.shape[0], dtype=jnp.int32)
    distance = (length - cache_pos).astype(jnp.float32)
    cache_scores = (
        jnp.einsum("hd,khd->hk", query_row, cache_keys, preferred_element_type=jnp.float32) * factor
    )
    cache_scores = cache_scores - slopes[:, None] * distance[None, :]
    cache_scores = jnp.where((cache_pos < length)[None, :], cache_scores, -jnp.inf)
    own_score = (
        jnp.einsum("hd,hd->h", query_row, new_key, preferred_element_type=jnp.float32)[:, None]
        * factor
    )
    highest = jnp.maximum(jnp.max(cache_scores, axis=-1, keepdims=True), own_score)
    cache_exp = jnp.exp(cache_scores - highest)
    own_exp = jnp.exp(own_score - highest)
    denominator = jnp.sum(cache_exp, axis=-1, keepdims=True) + own_exp
    cache_probs = (cache_exp / denominator).astype(jnp.bfloat16)
    own_prob = (own_exp / denominator).astype(jnp.bfloat16)
    context = jnp.einsum(
        "hk,khd->hd", cache_probs, cache_values, preferred_element_type=jnp.float32
    )
    context = context + own_prob.astype(jnp.float32) * new_value.astype(jnp.float32)
    return context.astype(jnp.bfloat16).reshape(-1)


def per_device(
    pre_hidden,
    dec_hidden,
    norm_gain,
    norm_shift,
    qkv_weight,
    qkv_bias,
    out_weight,
    out_bias,
    pre_keys,
    pre_values,
    dec_keys,
    dec_values,
    prefix_lengths,
    cache_lengths,
    slot_of,
):
    head_size = HD
    local_heads = qkv_weight.shape[1] // (3 * head_size)
    slopes = alibi_slopes(lax.axis_index("tensor") * local_heads, local_heads, H)
    bias_sum = out_bias.astype(jnp.float32)
    normed = normalize(pre_hidden, norm_gain, norm_shift)
    product = jnp.dot(
        lax.all_gather(normed, "tensor", axis=0, tiled=True),
        qkv_weight,
        preferred_element_type=jnp.float32,
    )
    merged_rows = (product + qkv_bias.astype(jnp.float32)).astype(jnp.bfloat16)
    chunks = 2
    part = pre_hidden.shape[0] // chunks
    pieces = []
    for chunk in range(chunks):
        context = prefill_attention_kernel(
            merged_rows, pre_keys[0], pre_values[0], prefix_lengths, slopes, head_size, part, chunks, chunk
        )
        pieces.append(
            lax.psum_scatter(
                jnp.dot(context, out_weight, preferred_element_type=jnp.float32),
                "tensor",
                scatter_dimension=0,
                tiled=True,
            )
        )
    summed = jnp.concatenate(pieces, axis=0)
    pre_output = (summed + bias_sum + pre_hidden.astype(jnp.float32)).astype(jnp.bfloat16)
    slot_count = dec_hidden.shape[0]
    dp_size = lax.axis_size("dp")
    tensor_size = lax.axis_size("tensor")
    group = lax.axis_index("dp")
    member = lax.axis_index("tensor")
    first_slot = group * slot_count
    shifted_rows = [dec_hidden] + [
        lax.ppermute(dec_hidden, "dp", [(i, (i + k) % dp_size) for i in range(dp_size)])
        for k in range(1, dp_size)
    ]
    shifted_rows = jnp.concatenate(shifted_rows, axis=0)
    slot_ids = first_slot + jnp.arange(slot_count, dtype=jnp.int32)
    request_ids = jnp.arange(slot_of.shape[0], dtype=jnp.int32)
    uses_slot = slot_of[None, :] == slot_ids[:, None]
    request_of_slot = jnp.sum(jnp.where(uses_slot, request_ids[None, :], 0), axis=1)
    arrival = ((group - request_of_slot // slot_count) % dp_size) * slot_count + request_of_slot % slot_count
    pick = (arrival[:, None] == jnp.arange(shifted_rows.shape[0], dtype=jnp.int32)[None, :]).astype(
        jnp.bfloat16
    )
    arrived = jnp.dot(pick, shifted_rows, preferred_element_type=jnp.float32).astype(jnp.bfloat16)
    normed_slots = normalize(arrived, norm_gain, norm_shift)
    merged_slots = (
        jnp.dot(normed_slots, qkv_weight, preferred_element_type=jnp.float32)
        + qkv_bias.astype(jnp.float32)
    ).astype(jnp.bfloat16)
    merged_slots = merged_slots.reshape(slot_count, local_heads, 3, head_size)
    dec_cache = dec_keys.shape[1]
    slot_context = jax.vmap(decode_attention, in_axes=(0, 0, 0, 0, 0, 0, None))(
        merged_slots[:, :, 0],
        merged_slots[:, :, 1],
        merged_slots[:, :, 2],
        dec_keys.reshape(slot_count, dec_cache, local_heads, head_size),
        dec_values.reshape(slot_count, dec_cache, local_heads, head_size),
        cache_lengths,
        slopes,
    )
    slot_partial = jnp.dot(slot_context, out_weight, preferred_element_type=jnp.float32)
    partials = jnp.stack(
        [slot_partial]
        + [
            lax.ppermute(slot_partial, "tensor", [(i, (i + k) % tensor_size) for i in range(tensor_size)])
            for k in range(1, tensor_size)
        ]
    )
    slot_summed = partials[member % tensor_size]
    for source in range(1, tensor_size):
        slot_summed = slot_summed + partials[(member - source) % tensor_size]
    slot_rows = (slot_summed + bias_sum + arrived.astype(jnp.float32)).astype(jnp.bfloat16)
    returned = [slot_rows] + [
        lax.ppermute(slot_rows, "dp", [(i, (i + k) % dp_size) for i in range(dp_size)])
        for k in range(1, dp_size)
    ]
    returned = jnp.concatenate(returned, axis=0)
    slot_wanted = lax.dynamic_slice_in_dim(slot_of, first_slot, slot_count)
    back = ((group - slot_wanted // slot_count) % dp_size) * slot_count + slot_wanted % slot_count
    take = (back[:, None] == jnp.arange(returned.shape[0], dtype=jnp.int32)[None, :]).astype(jnp.bfloat16)
    dec_output = jnp.dot(take, returned, preferred_element_type=jnp.float32).astype(jnp.bfloat16)
    return (pre_output, dec_output)


def solution(mesh):
    placed = (
        P(("dp", "tensor"), None),
        P("dp", None),
        P(),
        P(),
        P(None, "tensor"),
        P("tensor"),
        P("tensor", None),
        P(),
        P("dp", None, "tensor"),
        P("dp", None, "tensor"),
        P("dp", None, "tensor"),
        P("dp", None, "tensor"),
        P("dp"),
        P("dp"),
        P(),
    )
    return jax.shard_map(
        per_device,
        mesh=mesh,
        in_specs=placed,
        out_specs=(P(("dp", "tensor"), None), P("dp", None)),
        check_vma=False,
    )
```

```python
import math

import jax
import jax.numpy as jnp
from jax import lax
from jax.sharding import PartitionSpec as P
from jax.experimental import pallas as pl
from jax.experimental.pallas import tpu as pltpu
import functools

H = 16
HD = 128


EPSILON = 1e-05


def normalize(values, norm_gain, norm_shift):
    values = values.astype(jnp.float32)
    center = values - jnp.mean(values, axis=-1, keepdims=True)
    spread = jnp.mean(center * center, axis=-1, keepdims=True)
    scaled = center * lax.rsqrt(spread + EPSILON)
    return (scaled * norm_gain.astype(jnp.float32) + norm_shift.astype(jnp.float32)).astype(
        jnp.bfloat16
    )


def alibi_slopes(first_head, head_count, total_heads):
    head_ids = (first_head + jnp.arange(head_count, dtype=jnp.int32)).astype(jnp.float32)
    return jnp.exp2(-8.0 * (head_ids + 1.0) / total_heads)


def prefill_attention(merged_rows, cache_keys, cache_values, prefix, slopes):
    queries = merged_rows[:, :, 0]
    new_keys = merged_rows[:, :, 1]
    new_values = merged_rows[:, :, 2]
    group_size = merged_rows.shape[0]
    cache_size = cache_keys.shape[0]
    factor = 1.0 / math.sqrt(merged_rows.shape[-1])
    query_pos = prefix + jnp.arange(group_size, dtype=jnp.int32)
    cache_pos = jnp.arange(cache_size, dtype=jnp.int32)
    cache_dist = (query_pos[:, None] - cache_pos[None, :]).astype(jnp.float32)
    new_dist = (query_pos[:, None] - query_pos[None, :]).astype(jnp.float32)
    cache_scores = (
        jnp.einsum("qhd,khd->hqk", queries, cache_keys, preferred_element_type=jnp.float32) * factor
    )
    cache_scores = cache_scores - slopes[:, None, None] * cache_dist[None]
    cache_scores = jnp.where((cache_pos < prefix)[None, None, :], cache_scores, -jnp.inf)
    new_scores = (
        jnp.einsum("qhd,khd->hqk", queries, new_keys, preferred_element_type=jnp.float32) * factor
    )
    new_scores = new_scores - slopes[:, None, None] * new_dist[None]
    causal = (
        jnp.arange(group_size, dtype=jnp.int32)[None, :]
        <= jnp.arange(group_size, dtype=jnp.int32)[:, None]
    )
    new_scores = jnp.where(causal[None], new_scores, -jnp.inf)
    highest = jnp.maximum(
        jnp.max(cache_scores, axis=-1, keepdims=True), jnp.max(new_scores, axis=-1, keepdims=True)
    )
    cache_exp = jnp.exp(cache_scores - highest)
    new_exp = jnp.exp(new_scores - highest)
    denominator = jnp.sum(cache_exp, axis=-1, keepdims=True) + jnp.sum(
        new_exp, axis=-1, keepdims=True
    )
    cache_probs = (cache_exp / denominator).astype(jnp.bfloat16)
    new_probs = (new_exp / denominator).astype(jnp.bfloat16)
    context = jnp.einsum(
        "hqk,khd->qhd", cache_probs, cache_values, preferred_element_type=jnp.float32
    )
    context = context + jnp.einsum(
        "hqk,khd->qhd", new_probs, new_values, preferred_element_type=jnp.float32
    )
    return context.astype(jnp.bfloat16).reshape(group_size, -1)


def _prefill_kernel(prefix_ref, slopes_ref, q_ref, kn_ref, vn_ref, kc_ref, vc_ref, o_ref, *, tq):
    h = pl.program_id(0)
    i = pl.program_id(1)
    prefix = prefix_ref[0]
    slope = slopes_ref[h]
    factor = 1.0 / math.sqrt(q_ref.shape[-1])
    q = q_ref[...]
    dims = (((1,), (1,)), ((), ()))
    cache_size = kc_ref.shape[0]
    group = kn_ref.shape[0]
    q_tok = i * tq + lax.broadcasted_iota(jnp.int32, (tq, 1), 0)
    q_pos = prefix + q_tok
    c_pos = lax.broadcasted_iota(jnp.int32, (1, cache_size), 1)
    k_tok = lax.broadcasted_iota(jnp.int32, (1, group), 1)
    s_c = lax.dot_general(q, kc_ref[...], dims, preferred_element_type=jnp.float32) * factor
    s_c = s_c - slope * (q_pos - c_pos).astype(jnp.float32)
    s_c = jnp.where(c_pos < prefix, s_c, -jnp.inf)
    s_n = lax.dot_general(q, kn_ref[...], dims, preferred_element_type=jnp.float32) * factor
    s_n = s_n - slope * (q_tok - k_tok).astype(jnp.float32)
    s_n = jnp.where(k_tok <= q_tok, s_n, -jnp.inf)
    m = jnp.maximum(jnp.max(s_c, axis=-1, keepdims=True), jnp.max(s_n, axis=-1, keepdims=True))
    e_c = jnp.exp(s_c - m)
    e_n = jnp.exp(s_n - m)
    l = jnp.sum(e_c, axis=-1, keepdims=True) + jnp.sum(e_n, axis=-1, keepdims=True)
    p_c = (e_c / l).astype(jnp.bfloat16)
    p_n = (e_n / l).astype(jnp.bfloat16)
    ctx = jnp.dot(p_c, vc_ref[...], preferred_element_type=jnp.float32)
    ctx = ctx + jnp.dot(p_n, vn_ref[...], preferred_element_type=jnp.float32)
    o_ref[...] = ctx.astype(o_ref.dtype)

def prefill_attention_kernel(merged, cache_keys, cache_values, prefix, slopes, head_size, tq=256):
    group = merged.shape[0]
    heads = merged.shape[1] // (3 * head_size)
    cache_size = cache_keys.shape[0]
    col = lambda c: (lambda h, i, *_: (0, h * 3 + c))
    return pl.pallas_call(
        functools.partial(_prefill_kernel, tq=tq),
        out_shape=jax.ShapeDtypeStruct((group, heads * head_size), jnp.bfloat16),
        grid_spec=pltpu.PrefetchScalarGridSpec(
            num_scalar_prefetch=2,
            grid=(heads, group // tq),
            in_specs=[
                pl.BlockSpec((tq, head_size), lambda h, i, *_: (i, h * 3)),
                pl.BlockSpec((group, head_size), col(1)),
                pl.BlockSpec((group, head_size), col(2)),
                pl.BlockSpec((cache_size, head_size), lambda h, i, *_: (0, h)),
                pl.BlockSpec((cache_size, head_size), lambda h, i, *_: (0, h)),
            ],
            out_specs=pl.BlockSpec((tq, head_size), lambda h, i, *_: (i, h)),
        ),
        cost_estimate=pl.CostEstimate(
            flops=4 * heads * group * (group + cache_size) * head_size,
            transcendentals=heads * group * (group + cache_size),
            bytes_accessed=2 * (group * heads * 3 * head_size + 2 * cache_size * heads * head_size + group * heads * head_size),
        ),
    )(prefix, slopes, merged, merged, merged, cache_keys, cache_values)


def decode_attention(query_row, new_key, new_value, cache_keys, cache_values, length, slopes):
    factor = 1.0 / math.sqrt(query_row.shape[-1])
    cache_pos = jnp.arange(cache_keys.shape[0], dtype=jnp.int32)
    distance = (length - cache_pos).astype(jnp.float32)
    cache_scores = (
        jnp.einsum("hd,khd->hk", query_row, cache_keys, preferred_element_type=jnp.float32) * factor
    )
    cache_scores = cache_scores - slopes[:, None] * distance[None, :]
    cache_scores = jnp.where((cache_pos < length)[None, :], cache_scores, -jnp.inf)
    own_score = (
        jnp.einsum("hd,hd->h", query_row, new_key, preferred_element_type=jnp.float32)[:, None]
        * factor
    )
    highest = jnp.maximum(jnp.max(cache_scores, axis=-1, keepdims=True), own_score)
    cache_exp = jnp.exp(cache_scores - highest)
    own_exp = jnp.exp(own_score - highest)
    denominator = jnp.sum(cache_exp, axis=-1, keepdims=True) + own_exp
    cache_probs = (cache_exp / denominator).astype(jnp.bfloat16)
    own_prob = (own_exp / denominator).astype(jnp.bfloat16)
    context = jnp.einsum(
        "hk,khd->hd", cache_probs, cache_values, preferred_element_type=jnp.float32
    )
    context = context + own_prob.astype(jnp.float32) * new_value.astype(jnp.float32)
    return context.astype(jnp.bfloat16).reshape(-1)


def per_device(
    pre_hidden,
    dec_hidden,
    norm_gain,
    norm_shift,
    qkv_weight,
    qkv_bias,
    out_weight,
    out_bias,
    pre_keys,
    pre_values,
    dec_keys,
    dec_values,
    prefix_lengths,
    cache_lengths,
    slot_of,
):
    head_size = HD
    local_heads = qkv_weight.shape[1] // (3 * head_size)
    slopes = alibi_slopes(lax.axis_index("tensor") * local_heads, local_heads, H)
    bias_sum = out_bias.astype(jnp.float32)
    normed = normalize(pre_hidden, norm_gain, norm_shift)
    gathered = lax.all_gather(normed, "tensor", axis=0, tiled=True)
    slot_count = dec_hidden.shape[0]
    dp_size = lax.axis_size("dp")
    tensor_size = lax.axis_size("tensor")
    group = lax.axis_index("dp")
    member = lax.axis_index("tensor")
    first_slot = group * slot_count
    shifted_rows = [dec_hidden] + [
        lax.ppermute(dec_hidden, "dp", [(i, (i + k) % dp_size) for i in range(dp_size)])
        for k in range(1, dp_size)
    ]
    shifted_rows = jnp.concatenate(shifted_rows, axis=0)
    slot_ids = first_slot + jnp.arange(slot_count, dtype=jnp.int32)
    request_ids = jnp.arange(slot_of.shape[0], dtype=jnp.int32)
    uses_slot = slot_of[None, :] == slot_ids[:, None]
    request_of_slot = jnp.sum(jnp.where(uses_slot, request_ids[None, :], 0), axis=1)
    arrival = ((group - request_of_slot // slot_count) % dp_size) * slot_count + request_of_slot % slot_count
    pick = (arrival[:, None] == jnp.arange(shifted_rows.shape[0], dtype=jnp.int32)[None, :]).astype(
        jnp.bfloat16
    )
    arrived = jnp.dot(pick, shifted_rows, preferred_element_type=jnp.float32).astype(jnp.bfloat16)
    normed_slots = normalize(arrived, norm_gain, norm_shift)
    merged_slots = (
        jnp.dot(normed_slots, qkv_weight, preferred_element_type=jnp.float32)
        + qkv_bias.astype(jnp.float32)
    ).astype(jnp.bfloat16)
    merged_slots = merged_slots.reshape(slot_count, local_heads, 3, head_size)
    dec_cache = dec_keys.shape[1]
    slot_context = jax.vmap(decode_attention, in_axes=(0, 0, 0, 0, 0, 0, None))(
        merged_slots[:, :, 0],
        merged_slots[:, :, 1],
        merged_slots[:, :, 2],
        dec_keys.reshape(slot_count, dec_cache, local_heads, head_size),
        dec_values.reshape(slot_count, dec_cache, local_heads, head_size),
        cache_lengths,
        slopes,
    )
    slot_partial = jnp.dot(slot_context, out_weight, preferred_element_type=jnp.float32)
    partials = jnp.stack(
        [slot_partial]
        + [
            lax.ppermute(slot_partial, "tensor", [(i, (i + k) % tensor_size) for i in range(tensor_size)])
            for k in range(1, tensor_size)
        ]
    )
    slot_summed = partials[member % tensor_size]
    for source in range(1, tensor_size):
        slot_summed = slot_summed + partials[(member - source) % tensor_size]
    slot_rows = (slot_summed + bias_sum + arrived.astype(jnp.float32)).astype(jnp.bfloat16)
    tensor_size = lax.axis_size("tensor")
    chips = tensor_size // 2
    member = lax.axis_index("tensor")
    chip = member // 2
    core = member % 2
    block = pre_hidden.shape[0]

    def route(k, flip):
        return [(i, ((i // 2 + k) % chips) * 2 + ((i % 2) ^ flip)) for i in range(tensor_size)]

    gathered, slot_rows = lax.optimization_barrier((gathered, slot_rows))
    across_chips = [lax.ppermute(out_weight, "tensor", route(k, 0)) for k in range(1, chips)]
    product = jnp.dot(gathered, qkv_weight, preferred_element_type=jnp.float32)
    merged_rows = (product + qkv_bias.astype(jnp.float32)).astype(jnp.bfloat16)
    merged_rows, across_chips = lax.optimization_barrier((merged_rows, across_chips))
    same_core = [out_weight] + list(across_chips)
    other_core = lax.ppermute(jnp.concatenate(same_core, axis=0), "tensor", route(0, 1))
    weight_all = jnp.concatenate(same_core + [other_core], axis=0)
    context = prefill_attention_kernel(
        merged_rows, pre_keys[0], pre_values[0], prefix_lengths, slopes, head_size
    )
    pieces = []
    for flip in (0, 1):
        for k in range(chips):
            if k == 0 and flip == 0:
                pieces.append(lax.dynamic_slice_in_dim(context, member * block, block))
                continue
            target = ((chip + k) % chips) * 2 + (core ^ flip)
            outgoing = lax.dynamic_slice_in_dim(context, target * block, block)
            pieces.append(lax.ppermute(outgoing, "tensor", route(k, flip)))
    context_all = jnp.concatenate(pieces, axis=1)
    summed = jnp.dot(context_all, weight_all, preferred_element_type=jnp.float32)
    pre_output = (summed + bias_sum + pre_hidden.astype(jnp.float32)).astype(jnp.bfloat16)
    returned = [slot_rows] + [
        lax.ppermute(slot_rows, "dp", [(i, (i + k) % dp_size) for i in range(dp_size)])
        for k in range(1, dp_size)
    ]
    returned = jnp.concatenate(returned, axis=0)
    slot_wanted = lax.dynamic_slice_in_dim(slot_of, first_slot, slot_count)
    back = ((group - slot_wanted // slot_count) % dp_size) * slot_count + slot_wanted % slot_count
    take = (back[:, None] == jnp.arange(returned.shape[0], dtype=jnp.int32)[None, :]).astype(jnp.bfloat16)
    dec_output = jnp.dot(take, returned, preferred_element_type=jnp.float32).astype(jnp.bfloat16)
    return (pre_output, dec_output)


def solution(mesh):
    placed = (
        P(("dp", "tensor"), None),
        P("dp", None),
        P(),
        P(),
        P(None, "tensor"),
        P("tensor"),
        P("tensor", None),
        P(),
        P("dp", None, "tensor"),
        P("dp", None, "tensor"),
        P("dp", None, "tensor"),
        P("dp", None, "tensor"),
        P("dp"),
        P("dp"),
        P(),
    )
    return jax.shard_map(
        per_device,
        mesh=mesh,
        in_specs=placed,
        out_specs=(P(("dp", "tensor"), None), P("dp", None)),
        check_vma=False,
    )
```

```python
import math

import jax
import jax.numpy as jnp
from jax import lax
from jax.sharding import PartitionSpec as P
from jax.experimental import pallas as pl
from jax.experimental.pallas import tpu as pltpu
import functools

H = 16
HD = 128


EPSILON = 1e-05


def normalize(values, norm_gain, norm_shift):
    values = values.astype(jnp.float32)
    center = values - jnp.mean(values, axis=-1, keepdims=True)
    spread = jnp.mean(center * center, axis=-1, keepdims=True)
    scaled = center * lax.rsqrt(spread + EPSILON)
    return (scaled * norm_gain.astype(jnp.float32) + norm_shift.astype(jnp.float32)).astype(
        jnp.bfloat16
    )


def alibi_slopes(first_head, head_count, total_heads):
    head_ids = (first_head + jnp.arange(head_count, dtype=jnp.int32)).astype(jnp.float32)
    return jnp.exp2(-8.0 * (head_ids + 1.0) / total_heads)


def prefill_attention(merged_rows, cache_keys, cache_values, prefix, slopes):
    queries = merged_rows[:, :, 0]
    new_keys = merged_rows[:, :, 1]
    new_values = merged_rows[:, :, 2]
    group_size = merged_rows.shape[0]
    cache_size = cache_keys.shape[0]
    factor = 1.0 / math.sqrt(merged_rows.shape[-1])
    query_pos = prefix + jnp.arange(group_size, dtype=jnp.int32)
    cache_pos = jnp.arange(cache_size, dtype=jnp.int32)
    cache_dist = (query_pos[:, None] - cache_pos[None, :]).astype(jnp.float32)
    new_dist = (query_pos[:, None] - query_pos[None, :]).astype(jnp.float32)
    cache_scores = (
        jnp.einsum("qhd,khd->hqk", queries, cache_keys, preferred_element_type=jnp.float32) * factor
    )
    cache_scores = cache_scores - slopes[:, None, None] * cache_dist[None]
    cache_scores = jnp.where((cache_pos < prefix)[None, None, :], cache_scores, -jnp.inf)
    new_scores = (
        jnp.einsum("qhd,khd->hqk", queries, new_keys, preferred_element_type=jnp.float32) * factor
    )
    new_scores = new_scores - slopes[:, None, None] * new_dist[None]
    causal = (
        jnp.arange(group_size, dtype=jnp.int32)[None, :]
        <= jnp.arange(group_size, dtype=jnp.int32)[:, None]
    )
    new_scores = jnp.where(causal[None], new_scores, -jnp.inf)
    highest = jnp.maximum(
        jnp.max(cache_scores, axis=-1, keepdims=True), jnp.max(new_scores, axis=-1, keepdims=True)
    )
    cache_exp = jnp.exp(cache_scores - highest)
    new_exp = jnp.exp(new_scores - highest)
    denominator = jnp.sum(cache_exp, axis=-1, keepdims=True) + jnp.sum(
        new_exp, axis=-1, keepdims=True
    )
    cache_probs = (cache_exp / denominator).astype(jnp.bfloat16)
    new_probs = (new_exp / denominator).astype(jnp.bfloat16)
    context = jnp.einsum(
        "hqk,khd->qhd", cache_probs, cache_values, preferred_element_type=jnp.float32
    )
    context = context + jnp.einsum(
        "hqk,khd->qhd", new_probs, new_values, preferred_element_type=jnp.float32
    )
    return context.astype(jnp.bfloat16).reshape(group_size, -1)


def _prefill_kernel(prefix_ref, slopes_ref, q_ref, kn_ref, vn_ref, kc_ref, vc_ref, o_ref, *, tq):
    h = pl.program_id(0)
    i = pl.program_id(1)
    prefix = prefix_ref[0]
    slope = slopes_ref[h]
    factor = 1.0 / math.sqrt(q_ref.shape[-1])
    q = q_ref[...]
    dims = (((1,), (1,)), ((), ()))
    cache_size = kc_ref.shape[0]
    group = kn_ref.shape[0]
    q_tok = i * tq + lax.broadcasted_iota(jnp.int32, (tq, 1), 0)
    q_pos = prefix + q_tok
    c_pos = lax.broadcasted_iota(jnp.int32, (1, cache_size), 1)
    k_tok = lax.broadcasted_iota(jnp.int32, (1, group), 1)
    s_c = lax.dot_general(q, kc_ref[...], dims, preferred_element_type=jnp.float32) * factor
    s_c = s_c - slope * (q_pos - c_pos).astype(jnp.float32)
    s_c = jnp.where(c_pos < prefix, s_c, -jnp.inf)
    s_n = lax.dot_general(q, kn_ref[...], dims, preferred_element_type=jnp.float32) * factor
    s_n = s_n - slope * (q_tok - k_tok).astype(jnp.float32)
    s_n = jnp.where(k_tok <= q_tok, s_n, -jnp.inf)
    m = jnp.maximum(jnp.max(s_c, axis=-1, keepdims=True), jnp.max(s_n, axis=-1, keepdims=True))
    e_c = jnp.exp(s_c - m)
    e_n = jnp.exp(s_n - m)
    l = jnp.sum(e_c, axis=-1, keepdims=True) + jnp.sum(e_n, axis=-1, keepdims=True)
    p_c = (e_c / l).astype(jnp.bfloat16)
    p_n = (e_n / l).astype(jnp.bfloat16)
    ctx = jnp.dot(p_c, vc_ref[...], preferred_element_type=jnp.float32)
    ctx = ctx + jnp.dot(p_n, vn_ref[...], preferred_element_type=jnp.float32)
    o_ref[...] = ctx.astype(o_ref.dtype)

def prefill_attention_kernel(merged, cache_keys, cache_values, prefix, slopes, head_size, tq=256):
    group = merged.shape[0]
    heads = merged.shape[1] // (3 * head_size)
    cache_size = cache_keys.shape[0]
    col = lambda c: (lambda h, i, *_: (0, h * 3 + c))
    return pl.pallas_call(
        functools.partial(_prefill_kernel, tq=tq),
        out_shape=jax.ShapeDtypeStruct((group, heads * head_size), jnp.bfloat16),
        grid_spec=pltpu.PrefetchScalarGridSpec(
            num_scalar_prefetch=2,
            grid=(heads, group // tq),
            in_specs=[
                pl.BlockSpec((tq, head_size), lambda h, i, *_: (i, h * 3)),
                pl.BlockSpec((group, head_size), col(1)),
                pl.BlockSpec((group, head_size), col(2)),
                pl.BlockSpec((cache_size, head_size), lambda h, i, *_: (0, h)),
                pl.BlockSpec((cache_size, head_size), lambda h, i, *_: (0, h)),
            ],
            out_specs=pl.BlockSpec((tq, head_size), lambda h, i, *_: (i, h)),
        ),
        cost_estimate=pl.CostEstimate(
            flops=4 * heads * group * (group + cache_size) * head_size,
            transcendentals=heads * group * (group + cache_size),
            bytes_accessed=2 * (group * heads * 3 * head_size + 2 * cache_size * heads * head_size + group * heads * head_size),
        ),
    )(prefix, slopes, merged, merged, merged, cache_keys, cache_values)


def decode_attention(query_row, new_key, new_value, cache_keys, cache_values, length, slopes):
    factor = 1.0 / math.sqrt(query_row.shape[-1])
    cache_pos = jnp.arange(cache_keys.shape[0], dtype=jnp.int32)
    distance = (length - cache_pos).astype(jnp.float32)
    cache_scores = (
        jnp.einsum("hd,khd->hk", query_row, cache_keys, preferred_element_type=jnp.float32) * factor
    )
    cache_scores = cache_scores - slopes[:, None] * distance[None, :]
    cache_scores = jnp.where((cache_pos < length)[None, :], cache_scores, -jnp.inf)
    own_score = (
        jnp.einsum("hd,hd->h", query_row, new_key, preferred_element_type=jnp.float32)[:, None]
        * factor
    )
    highest = jnp.maximum(jnp.max(cache_scores, axis=-1, keepdims=True), own_score)
    cache_exp = jnp.exp(cache_scores - highest)
    own_exp = jnp.exp(own_score - highest)
    denominator = jnp.sum(cache_exp, axis=-1, keepdims=True) + own_exp
    cache_probs = (cache_exp / denominator).astype(jnp.bfloat16)
    own_prob = (own_exp / denominator).astype(jnp.bfloat16)
    context = jnp.einsum(
        "hk,khd->hd", cache_probs, cache_values, preferred_element_type=jnp.float32
    )
    context = context + own_prob.astype(jnp.float32) * new_value.astype(jnp.float32)
    return context.astype(jnp.bfloat16).reshape(-1)


def per_device(
    pre_hidden,
    dec_hidden,
    norm_gain,
    norm_shift,
    qkv_weight,
    qkv_bias,
    out_weight,
    out_bias,
    pre_keys,
    pre_values,
    dec_keys,
    dec_values,
    prefix_lengths,
    cache_lengths,
    slot_of,
):
    head_size = HD
    local_heads = qkv_weight.shape[1] // (3 * head_size)
    slopes = alibi_slopes(lax.axis_index("tensor") * local_heads, local_heads, H)
    bias_sum = out_bias.astype(jnp.float32)
    normed = normalize(pre_hidden, norm_gain, norm_shift)
    gathered = lax.all_gather(normed, "tensor", axis=0, tiled=True)
    slot_count = dec_hidden.shape[0]
    dp_size = lax.axis_size("dp")
    tensor_size = lax.axis_size("tensor")
    group = lax.axis_index("dp")
    member = lax.axis_index("tensor")
    first_slot = group * slot_count
    shifted_rows = [dec_hidden] + [
        lax.ppermute(dec_hidden, "dp", [(i, (i + k) % dp_size) for i in range(dp_size)])
        for k in range(1, dp_size)
    ]
    shifted_rows = jnp.concatenate(shifted_rows, axis=0)
    slot_ids = first_slot + jnp.arange(slot_count, dtype=jnp.int32)
    request_ids = jnp.arange(slot_of.shape[0], dtype=jnp.int32)
    uses_slot = slot_of[None, :] == slot_ids[:, None]
    request_of_slot = jnp.sum(jnp.where(uses_slot, request_ids[None, :], 0), axis=1)
    arrival = ((group - request_of_slot // slot_count) % dp_size) * slot_count + request_of_slot % slot_count
    pick = (arrival[:, None] == jnp.arange(shifted_rows.shape[0], dtype=jnp.int32)[None, :]).astype(
        jnp.bfloat16
    )
    arrived = jnp.dot(pick, shifted_rows, preferred_element_type=jnp.float32).astype(jnp.bfloat16)
    normed_slots = normalize(arrived, norm_gain, norm_shift)
    merged_slots = (
        jnp.dot(normed_slots, qkv_weight, preferred_element_type=jnp.float32)
        + qkv_bias.astype(jnp.float32)
    ).astype(jnp.bfloat16)
    merged_slots = merged_slots.reshape(slot_count, local_heads, 3, head_size)
    dec_cache = dec_keys.shape[1]
    slot_context = jax.vmap(decode_attention, in_axes=(0, 0, 0, 0, 0, 0, None))(
        merged_slots[:, :, 0],
        merged_slots[:, :, 1],
        merged_slots[:, :, 2],
        dec_keys.reshape(slot_count, dec_cache, local_heads, head_size),
        dec_values.reshape(slot_count, dec_cache, local_heads, head_size),
        cache_lengths,
        slopes,
    )
    slot_partial = jnp.dot(slot_context, out_weight, preferred_element_type=jnp.float32)
    partials = jnp.stack(
        [slot_partial]
        + [
            lax.ppermute(slot_partial, "tensor", [(i, (i + k) % tensor_size) for i in range(tensor_size)])
            for k in range(1, tensor_size)
        ]
    )
    slot_summed = partials[member % tensor_size]
    for source in range(1, tensor_size):
        slot_summed = slot_summed + partials[(member - source) % tensor_size]
    slot_rows = (slot_summed + bias_sum + arrived.astype(jnp.float32)).astype(jnp.bfloat16)
    tensor_size = lax.axis_size("tensor")
    chips = tensor_size // 2
    member = lax.axis_index("tensor")
    chip = member // 2
    core = member % 2
    block = pre_hidden.shape[0]

    def route(k, flip):
        return [(i, ((i // 2 + k) % chips) * 2 + ((i % 2) ^ flip)) for i in range(tensor_size)]

    gathered, slot_rows = lax.optimization_barrier((gathered, slot_rows))
    across_chips = [lax.ppermute(out_weight, "tensor", route(k, 0)) for k in range(1, chips)]
    product = jnp.dot(gathered, qkv_weight, preferred_element_type=jnp.float32)
    merged_rows = (product + qkv_bias.astype(jnp.float32)).astype(jnp.bfloat16)
    context = prefill_attention_kernel(
        merged_rows, pre_keys[0], pre_values[0], prefix_lengths, slopes, head_size
    )
    context, across_chips = lax.optimization_barrier((context, across_chips))
    same_core = [out_weight] + list(across_chips)
    other_core = lax.ppermute(jnp.concatenate(same_core, axis=0), "tensor", route(0, 1))
    weight_all = jnp.concatenate(same_core + [other_core], axis=0)
    pieces = []
    for flip in (0, 1):
        for k in range(chips):
            if k == 0 and flip == 0:
                pieces.append(lax.dynamic_slice_in_dim(context, member * block, block))
                continue
            target = ((chip + k) % chips) * 2 + (core ^ flip)
            outgoing = lax.dynamic_slice_in_dim(context, target * block, block)
            pieces.append(lax.ppermute(outgoing, "tensor", route(k, flip)))
    context_all = jnp.concatenate(pieces, axis=1)
    summed = jnp.dot(context_all, weight_all, preferred_element_type=jnp.float32)
    pre_output = (summed + bias_sum + pre_hidden.astype(jnp.float32)).astype(jnp.bfloat16)
    returned = [slot_rows] + [
        lax.ppermute(slot_rows, "dp", [(i, (i + k) % dp_size) for i in range(dp_size)])
        for k in range(1, dp_size)
    ]
    returned = jnp.concatenate(returned, axis=0)
    slot_wanted = lax.dynamic_slice_in_dim(slot_of, first_slot, slot_count)
    back = ((group - slot_wanted // slot_count) % dp_size) * slot_count + slot_wanted % slot_count
    take = (back[:, None] == jnp.arange(returned.shape[0], dtype=jnp.int32)[None, :]).astype(jnp.bfloat16)
    dec_output = jnp.dot(take, returned, preferred_element_type=jnp.float32).astype(jnp.bfloat16)
    return (pre_output, dec_output)


def solution(mesh):
    placed = (
        P(("dp", "tensor"), None),
        P("dp", None),
        P(),
        P(),
        P(None, "tensor"),
        P("tensor"),
        P("tensor", None),
        P(),
        P("dp", None, "tensor"),
        P("dp", None, "tensor"),
        P("dp", None, "tensor"),
        P("dp", None, "tensor"),
        P("dp"),
        P("dp"),
        P(),
    )
    return jax.shard_map(
        per_device,
        mesh=mesh,
        in_specs=placed,
        out_specs=(P(("dp", "tensor"), None), P("dp", None)),
        check_vma=False,
    )
```

```python
import math

import jax
import jax.numpy as jnp
from jax import lax
from jax.sharding import PartitionSpec as P
from jax.experimental import pallas as pl
from jax.experimental.pallas import tpu as pltpu
import functools

H = 16
HD = 128


EPSILON = 1e-05


def normalize(values, norm_gain, norm_shift):
    values = values.astype(jnp.float32)
    center = values - jnp.mean(values, axis=-1, keepdims=True)
    spread = jnp.mean(center * center, axis=-1, keepdims=True)
    scaled = center * lax.rsqrt(spread + EPSILON)
    return (scaled * norm_gain.astype(jnp.float32) + norm_shift.astype(jnp.float32)).astype(
        jnp.bfloat16
    )


def alibi_slopes(first_head, head_count, total_heads):
    head_ids = (first_head + jnp.arange(head_count, dtype=jnp.int32)).astype(jnp.float32)
    return jnp.exp2(-8.0 * (head_ids + 1.0) / total_heads)


def prefill_attention(merged_rows, cache_keys, cache_values, prefix, slopes):
    queries = merged_rows[:, :, 0]
    new_keys = merged_rows[:, :, 1]
    new_values = merged_rows[:, :, 2]
    group_size = merged_rows.shape[0]
    cache_size = cache_keys.shape[0]
    factor = 1.0 / math.sqrt(merged_rows.shape[-1])
    query_pos = prefix + jnp.arange(group_size, dtype=jnp.int32)
    cache_pos = jnp.arange(cache_size, dtype=jnp.int32)
    cache_dist = (query_pos[:, None] - cache_pos[None, :]).astype(jnp.float32)
    new_dist = (query_pos[:, None] - query_pos[None, :]).astype(jnp.float32)
    cache_scores = (
        jnp.einsum("qhd,khd->hqk", queries, cache_keys, preferred_element_type=jnp.float32) * factor
    )
    cache_scores = cache_scores - slopes[:, None, None] * cache_dist[None]
    cache_scores = jnp.where((cache_pos < prefix)[None, None, :], cache_scores, -jnp.inf)
    new_scores = (
        jnp.einsum("qhd,khd->hqk", queries, new_keys, preferred_element_type=jnp.float32) * factor
    )
    new_scores = new_scores - slopes[:, None, None] * new_dist[None]
    causal = (
        jnp.arange(group_size, dtype=jnp.int32)[None, :]
        <= jnp.arange(group_size, dtype=jnp.int32)[:, None]
    )
    new_scores = jnp.where(causal[None], new_scores, -jnp.inf)
    highest = jnp.maximum(
        jnp.max(cache_scores, axis=-1, keepdims=True), jnp.max(new_scores, axis=-1, keepdims=True)
    )
    cache_exp = jnp.exp(cache_scores - highest)
    new_exp = jnp.exp(new_scores - highest)
    denominator = jnp.sum(cache_exp, axis=-1, keepdims=True) + jnp.sum(
        new_exp, axis=-1, keepdims=True
    )
    cache_probs = (cache_exp / denominator).astype(jnp.bfloat16)
    new_probs = (new_exp / denominator).astype(jnp.bfloat16)
    context = jnp.einsum(
        "hqk,khd->qhd", cache_probs, cache_values, preferred_element_type=jnp.float32
    )
    context = context + jnp.einsum(
        "hqk,khd->qhd", new_probs, new_values, preferred_element_type=jnp.float32
    )
    return context.astype(jnp.bfloat16).reshape(group_size, -1)


def _prefill_kernel(prefix_ref, slopes_ref, q_ref, kn_ref, vn_ref, kc_ref, vc_ref, o_ref, *, tq):
    h = pl.program_id(0)
    i = pl.program_id(1)
    prefix = prefix_ref[0]
    slope = slopes_ref[h]
    factor = 1.0 / math.sqrt(q_ref.shape[-1])
    q = q_ref[...]
    dims = (((1,), (1,)), ((), ()))
    cache_size = kc_ref.shape[0]
    group = kn_ref.shape[0]
    q_tok = i * tq + lax.broadcasted_iota(jnp.int32, (tq, 1), 0)
    q_pos = prefix + q_tok
    c_pos = lax.broadcasted_iota(jnp.int32, (1, cache_size), 1)
    k_tok = lax.broadcasted_iota(jnp.int32, (1, group), 1)
    s_c = lax.dot_general(q, kc_ref[...], dims, preferred_element_type=jnp.float32) * factor
    s_c = s_c - slope * (q_pos - c_pos).astype(jnp.float32)
    s_c = jnp.where(c_pos < prefix, s_c, -jnp.inf)
    s_n = lax.dot_general(q, kn_ref[...], dims, preferred_element_type=jnp.float32) * factor
    s_n = s_n - slope * (q_tok - k_tok).astype(jnp.float32)
    s_n = jnp.where(k_tok <= q_tok, s_n, -jnp.inf)
    m = jnp.maximum(jnp.max(s_c, axis=-1, keepdims=True), jnp.max(s_n, axis=-1, keepdims=True))
    e_c = jnp.exp(s_c - m)
    e_n = jnp.exp(s_n - m)
    l = jnp.sum(e_c, axis=-1, keepdims=True) + jnp.sum(e_n, axis=-1, keepdims=True)
    p_c = (e_c / l).astype(jnp.bfloat16)
    p_n = (e_n / l).astype(jnp.bfloat16)
    ctx = jnp.dot(p_c, vc_ref[...], preferred_element_type=jnp.float32)
    ctx = ctx + jnp.dot(p_n, vn_ref[...], preferred_element_type=jnp.float32)
    o_ref[...] = ctx.astype(o_ref.dtype)

def prefill_attention_kernel(merged, cache_keys, cache_values, prefix, slopes, head_size, tq=256):
    group = merged.shape[0]
    heads = merged.shape[1] // (3 * head_size)
    cache_size = cache_keys.shape[0]
    col = lambda c: (lambda h, i, *_: (0, h * 3 + c))
    return pl.pallas_call(
        functools.partial(_prefill_kernel, tq=tq),
        out_shape=jax.ShapeDtypeStruct((group, heads * head_size), jnp.bfloat16),
        grid_spec=pltpu.PrefetchScalarGridSpec(
            num_scalar_prefetch=2,
            grid=(heads, group // tq),
            in_specs=[
                pl.BlockSpec((tq, head_size), lambda h, i, *_: (i, h * 3)),
                pl.BlockSpec((group, head_size), col(1)),
                pl.BlockSpec((group, head_size), col(2)),
                pl.BlockSpec((cache_size, head_size), lambda h, i, *_: (0, h)),
                pl.BlockSpec((cache_size, head_size), lambda h, i, *_: (0, h)),
            ],
            out_specs=pl.BlockSpec((tq, head_size), lambda h, i, *_: (i, h)),
        ),
        cost_estimate=pl.CostEstimate(
            flops=4 * heads * group * (group + cache_size) * head_size,
            transcendentals=heads * group * (group + cache_size),
            bytes_accessed=2 * (group * heads * 3 * head_size + 2 * cache_size * heads * head_size + group * heads * head_size),
        ),
    )(prefix, slopes, merged, merged, merged, cache_keys, cache_values)


def decode_attention(query_row, new_key, new_value, cache_keys, cache_values, length, slopes):
    heads, head_size = query_row.shape
    factor = 1.0 / math.sqrt(head_size)
    cache_pos = jnp.arange(cache_keys.shape[0], dtype=jnp.int32)
    distance = (length - cache_pos).astype(jnp.float32)
    head_of_col = jnp.arange(heads * head_size, dtype=jnp.int32) // head_size
    own_head = head_of_col[:, None] == jnp.arange(heads, dtype=jnp.int32)[None, :]
    block_query = jnp.where(own_head, query_row.reshape(-1)[:, None], jnp.zeros((), query_row.dtype))
    cache_scores = jnp.dot(cache_keys, block_query, preferred_element_type=jnp.float32).T * factor
    cache_scores = cache_scores - slopes[:, None] * distance[None, :]
    cache_scores = jnp.where((cache_pos < length)[None, :], cache_scores, -jnp.inf)
    own_score = (
        jnp.einsum("hd,hd->h", query_row, new_key, preferred_element_type=jnp.float32)[:, None]
        * factor
    )
    highest = jnp.maximum(jnp.max(cache_scores, axis=-1, keepdims=True), own_score)
    cache_exp = jnp.exp(cache_scores - highest)
    own_exp = jnp.exp(own_score - highest)
    denominator = jnp.sum(cache_exp, axis=-1, keepdims=True) + own_exp
    cache_probs = (cache_exp / denominator).astype(jnp.bfloat16)
    own_prob = (own_exp / denominator).astype(jnp.bfloat16)
    every_head = jnp.dot(cache_probs, cache_values, preferred_element_type=jnp.float32)
    context = jnp.sum(jnp.where(own_head.T, every_head, 0.0), axis=0).reshape(heads, head_size)
    context = context + own_prob.astype(jnp.float32) * new_value.astype(jnp.float32)
    return context.astype(jnp.bfloat16).reshape(-1)


def per_device(
    pre_hidden,
    dec_hidden,
    norm_gain,
    norm_shift,
    qkv_weight,
    qkv_bias,
    out_weight,
    out_bias,
    pre_keys,
    pre_values,
    dec_keys,
    dec_values,
    prefix_lengths,
    cache_lengths,
    slot_of,
):
    head_size = HD
    local_heads = qkv_weight.shape[1] // (3 * head_size)
    slopes = alibi_slopes(lax.axis_index("tensor") * local_heads, local_heads, H)
    bias_sum = out_bias.astype(jnp.float32)
    normed = normalize(pre_hidden, norm_gain, norm_shift)
    gathered = lax.all_gather(normed, "tensor", axis=0, tiled=True)
    slot_count = dec_hidden.shape[0]
    dp_size = lax.axis_size("dp")
    tensor_size = lax.axis_size("tensor")
    group = lax.axis_index("dp")
    member = lax.axis_index("tensor")
    first_slot = group * slot_count
    shifted_rows = dec_hidden
    step = 1
    while step < dp_size:
        shifted_rows = jnp.concatenate(
            [shifted_rows, lax.ppermute(shifted_rows, "dp", [(i, i ^ step) for i in range(dp_size)])], axis=0
        )
        step *= 2
    slot_ids = first_slot + jnp.arange(slot_count, dtype=jnp.int32)
    request_ids = jnp.arange(slot_of.shape[0], dtype=jnp.int32)
    uses_slot = slot_of[None, :] == slot_ids[:, None]
    request_of_slot = jnp.sum(jnp.where(uses_slot, request_ids[None, :], 0), axis=1)
    arrival = ((request_of_slot // slot_count) ^ group) * slot_count + request_of_slot % slot_count
    pick = (arrival[:, None] == jnp.arange(shifted_rows.shape[0], dtype=jnp.int32)[None, :]).astype(
        jnp.bfloat16
    )
    arrived = jnp.dot(pick, shifted_rows, preferred_element_type=jnp.float32).astype(jnp.bfloat16)
    normed_slots = normalize(arrived, norm_gain, norm_shift)
    merged_slots = (
        jnp.dot(normed_slots, qkv_weight, preferred_element_type=jnp.float32)
        + qkv_bias.astype(jnp.float32)
    ).astype(jnp.bfloat16)
    merged_slots = merged_slots.reshape(slot_count, local_heads, 3, head_size)
    dec_cache = dec_keys.shape[1]
    slot_context = jax.vmap(decode_attention, in_axes=(0, 0, 0, 0, 0, 0, None))(
        merged_slots[:, :, 0],
        merged_slots[:, :, 1],
        merged_slots[:, :, 2],
        dec_keys,
        dec_values,
        cache_lengths,
        slopes,
    )
    slot_partial = jnp.dot(slot_context, out_weight, preferred_element_type=jnp.float32)
    partials = slot_partial
    step = 1
    while step < tensor_size:
        partials = jnp.concatenate(
            [partials, lax.ppermute(partials, "tensor", [(i, i ^ step) for i in range(tensor_size)])], axis=0
        )
        step *= 2
    partials = partials.reshape(tensor_size, slot_count, -1)
    slot_summed = partials[member ^ 0]
    for source in range(1, tensor_size):
        slot_summed = slot_summed + partials[member ^ source]
    slot_rows = (slot_summed + bias_sum + arrived.astype(jnp.float32)).astype(jnp.bfloat16)
    tensor_size = lax.axis_size("tensor")
    chips = tensor_size // 2
    member = lax.axis_index("tensor")
    chip = member // 2
    core = member % 2
    block = pre_hidden.shape[0]

    def route(k, flip):
        return [(i, ((i // 2 + k) % chips) * 2 + ((i % 2) ^ flip)) for i in range(tensor_size)]

    gathered, slot_rows = lax.optimization_barrier((gathered, slot_rows))
    across_chips = [lax.ppermute(out_weight, "tensor", route(k, 0)) for k in range(1, chips)]
    product = jnp.dot(gathered, qkv_weight, preferred_element_type=jnp.float32)
    merged_rows = (product + qkv_bias.astype(jnp.float32)).astype(jnp.bfloat16)
    context = prefill_attention_kernel(
        merged_rows, pre_keys[0], pre_values[0], prefix_lengths, slopes, head_size
    )
    context, across_chips = lax.optimization_barrier((context, across_chips))
    same_core = [out_weight] + list(across_chips)
    weight_blocks = same_core + [lax.ppermute(w, "tensor", route(0, 1)) for w in same_core]
    pieces = []
    for flip in (0, 1):
        for k in range(chips):
            if k == 0 and flip == 0:
                pieces.append(lax.dynamic_slice_in_dim(context, member * block, block))
                continue
            target = ((chip + k) % chips) * 2 + (core ^ flip)
            outgoing = lax.dynamic_slice_in_dim(context, target * block, block)
            pieces.append(lax.ppermute(outgoing, "tensor", route(k, flip)))
    summed = jnp.dot(pieces[0], weight_blocks[0], preferred_element_type=jnp.float32)
    for piece, weight in zip(pieces[1:], weight_blocks[1:]):
        summed = summed + jnp.dot(piece, weight, preferred_element_type=jnp.float32)
    pre_output = (summed + bias_sum + pre_hidden.astype(jnp.float32)).astype(jnp.bfloat16)
    returned = slot_rows
    step = 1
    while step < dp_size:
        returned = jnp.concatenate(
            [returned, lax.ppermute(returned, "dp", [(i, i ^ step) for i in range(dp_size)])], axis=0
        )
        step *= 2
    slot_wanted = lax.dynamic_slice_in_dim(slot_of, first_slot, slot_count)
    back = ((slot_wanted // slot_count) ^ group) * slot_count + slot_wanted % slot_count
    take = (back[:, None] == jnp.arange(returned.shape[0], dtype=jnp.int32)[None, :]).astype(jnp.bfloat16)
    dec_output = jnp.dot(take, returned, preferred_element_type=jnp.float32).astype(jnp.bfloat16)
    return (pre_output, dec_output)


def solution(mesh):
    placed = (
        P(("dp", "tensor"), None),
        P("dp", None),
        P(),
        P(),
        P(None, "tensor"),
        P("tensor"),
        P("tensor", None),
        P(),
        P("dp", None, "tensor"),
        P("dp", None, "tensor"),
        P("dp", None, "tensor"),
        P("dp", None, "tensor"),
        P("dp"),
        P("dp"),
        P(),
    )
    return jax.shard_map(
        per_device,
        mesh=mesh,
        in_specs=placed,
        out_specs=(P(("dp", "tensor"), None), P("dp", None)),
        check_vma=False,
    )
```

```python
import math

import jax
import jax.numpy as jnp
from jax import lax
from jax.sharding import PartitionSpec as P
from jax.experimental import pallas as pl
from jax.experimental.pallas import tpu as pltpu
import functools

H = 16
HD = 128


EPSILON = 1e-05


def normalize(values, norm_gain, norm_shift):
    values = values.astype(jnp.float32)
    center = values - jnp.mean(values, axis=-1, keepdims=True)
    spread = jnp.mean(center * center, axis=-1, keepdims=True)
    scaled = center * lax.rsqrt(spread + EPSILON)
    return (scaled * norm_gain.astype(jnp.float32) + norm_shift.astype(jnp.float32)).astype(
        jnp.bfloat16
    )


def alibi_slopes(first_head, head_count, total_heads):
    head_ids = (first_head + jnp.arange(head_count, dtype=jnp.int32)).astype(jnp.float32)
    return jnp.exp2(-8.0 * (head_ids + 1.0) / total_heads)


def prefill_attention(merged_rows, cache_keys, cache_values, prefix, slopes):
    queries = merged_rows[:, :, 0]
    new_keys = merged_rows[:, :, 1]
    new_values = merged_rows[:, :, 2]
    group_size = merged_rows.shape[0]
    cache_size = cache_keys.shape[0]
    factor = 1.0 / math.sqrt(merged_rows.shape[-1])
    query_pos = prefix + jnp.arange(group_size, dtype=jnp.int32)
    cache_pos = jnp.arange(cache_size, dtype=jnp.int32)
    cache_dist = (query_pos[:, None] - cache_pos[None, :]).astype(jnp.float32)
    new_dist = (query_pos[:, None] - query_pos[None, :]).astype(jnp.float32)
    cache_scores = (
        jnp.einsum("qhd,khd->hqk", queries, cache_keys, preferred_element_type=jnp.float32) * factor
    )
    cache_scores = cache_scores - slopes[:, None, None] * cache_dist[None]
    cache_scores = jnp.where((cache_pos < prefix)[None, None, :], cache_scores, -jnp.inf)
    new_scores = (
        jnp.einsum("qhd,khd->hqk", queries, new_keys, preferred_element_type=jnp.float32) * factor
    )
    new_scores = new_scores - slopes[:, None, None] * new_dist[None]
    causal = (
        jnp.arange(group_size, dtype=jnp.int32)[None, :]
        <= jnp.arange(group_size, dtype=jnp.int32)[:, None]
    )
    new_scores = jnp.where(causal[None], new_scores, -jnp.inf)
    highest = jnp.maximum(
        jnp.max(cache_scores, axis=-1, keepdims=True), jnp.max(new_scores, axis=-1, keepdims=True)
    )
    cache_exp = jnp.exp(cache_scores - highest)
    new_exp = jnp.exp(new_scores - highest)
    denominator = jnp.sum(cache_exp, axis=-1, keepdims=True) + jnp.sum(
        new_exp, axis=-1, keepdims=True
    )
    cache_probs = (cache_exp / denominator).astype(jnp.bfloat16)
    new_probs = (new_exp / denominator).astype(jnp.bfloat16)
    context = jnp.einsum(
        "hqk,khd->qhd", cache_probs, cache_values, preferred_element_type=jnp.float32
    )
    context = context + jnp.einsum(
        "hqk,khd->qhd", new_probs, new_values, preferred_element_type=jnp.float32
    )
    return context.astype(jnp.bfloat16).reshape(group_size, -1)


def _prefill_kernel(prefix_ref, slopes_ref, q_ref, kn_ref, vn_ref, kc_ref, vc_ref, o_ref, *, tq):
    h = pl.program_id(0)
    i = pl.program_id(1)
    prefix = prefix_ref[0]
    slope = slopes_ref[h]
    factor = 1.0 / math.sqrt(q_ref.shape[-1])
    q = q_ref[...]
    dims = (((1,), (1,)), ((), ()))
    cache_size = kc_ref.shape[0]
    group = kn_ref.shape[0]
    q_tok = i * tq + lax.broadcasted_iota(jnp.int32, (tq, 1), 0)
    q_pos = prefix + q_tok
    c_pos = lax.broadcasted_iota(jnp.int32, (1, cache_size), 1)
    k_tok = lax.broadcasted_iota(jnp.int32, (1, group), 1)
    s_c = lax.dot_general(q, kc_ref[...], dims, preferred_element_type=jnp.float32) * factor
    s_c = s_c - slope * (q_pos - c_pos).astype(jnp.float32)
    s_c = jnp.where(c_pos < prefix, s_c, -jnp.inf)
    s_n = lax.dot_general(q, kn_ref[...], dims, preferred_element_type=jnp.float32) * factor
    s_n = s_n - slope * (q_tok - k_tok).astype(jnp.float32)
    s_n = jnp.where(k_tok <= q_tok, s_n, -jnp.inf)
    m = jnp.maximum(jnp.max(s_c, axis=-1, keepdims=True), jnp.max(s_n, axis=-1, keepdims=True))
    e_c = jnp.exp(s_c - m)
    e_n = jnp.exp(s_n - m)
    l = jnp.sum(e_c, axis=-1, keepdims=True) + jnp.sum(e_n, axis=-1, keepdims=True)
    p_c = (e_c / l).astype(jnp.bfloat16)
    p_n = (e_n / l).astype(jnp.bfloat16)
    ctx = jnp.dot(p_c, vc_ref[...], preferred_element_type=jnp.float32)
    ctx = ctx + jnp.dot(p_n, vn_ref[...], preferred_element_type=jnp.float32)
    o_ref[...] = ctx.astype(o_ref.dtype)

def prefill_attention_kernel(merged, cache_keys, cache_values, prefix, slopes, head_size, tq=256):
    group = merged.shape[0]
    heads = merged.shape[1] // (3 * head_size)
    cache_size = cache_keys.shape[0]
    col = lambda c: (lambda h, i, *_: (0, h * 3 + c))
    return pl.pallas_call(
        functools.partial(_prefill_kernel, tq=tq),
        out_shape=jax.ShapeDtypeStruct((group, heads * head_size), jnp.bfloat16),
        grid_spec=pltpu.PrefetchScalarGridSpec(
            num_scalar_prefetch=2,
            grid=(heads, group // tq),
            in_specs=[
                pl.BlockSpec((tq, head_size), lambda h, i, *_: (i, h * 3)),
                pl.BlockSpec((group, head_size), col(1)),
                pl.BlockSpec((group, head_size), col(2)),
                pl.BlockSpec((cache_size, head_size), lambda h, i, *_: (0, h)),
                pl.BlockSpec((cache_size, head_size), lambda h, i, *_: (0, h)),
            ],
            out_specs=pl.BlockSpec((tq, head_size), lambda h, i, *_: (i, h)),
        ),
        cost_estimate=pl.CostEstimate(
            flops=4 * heads * group * (group + cache_size) * head_size,
            transcendentals=heads * group * (group + cache_size),
            bytes_accessed=2 * (group * heads * 3 * head_size + 2 * cache_size * heads * head_size + group * heads * head_size),
        ),
    )(prefix, slopes, merged, merged, merged, cache_keys, cache_values)


def decode_attention(query_row, new_key, new_value, cache_keys, cache_values, length, slopes):
    heads, head_size = query_row.shape
    factor = 1.0 / math.sqrt(head_size)
    cache_pos = jnp.arange(cache_keys.shape[0], dtype=jnp.int32)
    distance = (length - cache_pos).astype(jnp.float32)
    head_of_col = jnp.arange(heads * head_size, dtype=jnp.int32) // head_size
    own_head = head_of_col[:, None] == jnp.arange(heads, dtype=jnp.int32)[None, :]
    block_query = jnp.where(own_head, query_row.reshape(-1)[:, None], jnp.zeros((), query_row.dtype))
    cache_scores = jnp.dot(cache_keys, block_query, preferred_element_type=jnp.float32).T * factor
    cache_scores = cache_scores - slopes[:, None] * distance[None, :]
    cache_scores = jnp.where((cache_pos < length)[None, :], cache_scores, -jnp.inf)
    own_score = (
        jnp.einsum("hd,hd->h", query_row, new_key, preferred_element_type=jnp.float32)[:, None]
        * factor
    )
    highest = jnp.maximum(jnp.max(cache_scores, axis=-1, keepdims=True), own_score)
    cache_exp = jnp.exp(cache_scores - highest)
    own_exp = jnp.exp(own_score - highest)
    denominator = jnp.sum(cache_exp, axis=-1, keepdims=True) + own_exp
    cache_probs = (cache_exp / denominator).astype(jnp.bfloat16)
    own_prob = (own_exp / denominator).astype(jnp.bfloat16)
    every_head = jnp.dot(cache_probs, cache_values, preferred_element_type=jnp.float32)
    context = jnp.sum(jnp.where(own_head.T, every_head, 0.0), axis=0).reshape(heads, head_size)
    context = context + own_prob.astype(jnp.float32) * new_value.astype(jnp.float32)
    return context.astype(jnp.bfloat16).reshape(-1)


def per_device(
    pre_hidden,
    dec_hidden,
    norm_gain,
    norm_shift,
    qkv_weight,
    qkv_bias,
    out_weight,
    out_bias,
    pre_keys,
    pre_values,
    dec_keys,
    dec_values,
    prefix_lengths,
    cache_lengths,
    slot_of,
):
    head_size = HD
    local_heads = qkv_weight.shape[1] // (3 * head_size)
    slopes = alibi_slopes(lax.axis_index("tensor") * local_heads, local_heads, H)
    bias_sum = out_bias.astype(jnp.float32)
    normed = normalize(pre_hidden, norm_gain, norm_shift)
    slot_count = dec_hidden.shape[0]
    dp_size = lax.axis_size("dp")
    tensor_size = lax.axis_size("tensor")
    group = lax.axis_index("dp")
    member = lax.axis_index("tensor")
    first_slot = group * slot_count
    shifted_rows = dec_hidden
    step = 1
    while step < dp_size:
        shifted_rows = jnp.concatenate(
            [shifted_rows, lax.ppermute(shifted_rows, "dp", [(i, i ^ step) for i in range(dp_size)])], axis=0
        )
        step *= 2
    slot_ids = first_slot + jnp.arange(slot_count, dtype=jnp.int32)
    request_ids = jnp.arange(slot_of.shape[0], dtype=jnp.int32)
    uses_slot = slot_of[None, :] == slot_ids[:, None]
    request_of_slot = jnp.sum(jnp.where(uses_slot, request_ids[None, :], 0), axis=1)
    arrival = ((request_of_slot // slot_count) ^ group) * slot_count + request_of_slot % slot_count
    pick = (arrival[:, None] == jnp.arange(shifted_rows.shape[0], dtype=jnp.int32)[None, :]).astype(
        jnp.bfloat16
    )
    arrived = jnp.dot(pick, shifted_rows, preferred_element_type=jnp.float32).astype(jnp.bfloat16)
    normed_slots = normalize(arrived, norm_gain, norm_shift)
    merged_slots = (
        jnp.dot(normed_slots, qkv_weight, preferred_element_type=jnp.float32)
        + qkv_bias.astype(jnp.float32)
    ).astype(jnp.bfloat16)
    merged_slots = merged_slots.reshape(slot_count, local_heads, 3, head_size)
    dec_cache = dec_keys.shape[1]
    slot_context = jax.vmap(decode_attention, in_axes=(0, 0, 0, 0, 0, 0, None))(
        merged_slots[:, :, 0],
        merged_slots[:, :, 1],
        merged_slots[:, :, 2],
        dec_keys,
        dec_values,
        cache_lengths,
        slopes,
    )
    slot_partial = jnp.dot(slot_context, out_weight, preferred_element_type=jnp.float32)
    partials = slot_partial
    step = 1
    while step < tensor_size:
        partials = jnp.concatenate(
            [partials, lax.ppermute(partials, "tensor", [(i, i ^ step) for i in range(tensor_size)])], axis=0
        )
        step *= 2
    partials = partials.reshape(tensor_size, slot_count, -1)
    slot_summed = partials[member ^ 0]
    for source in range(1, tensor_size):
        slot_summed = slot_summed + partials[member ^ source]
    slot_rows = (slot_summed + bias_sum + arrived.astype(jnp.float32)).astype(jnp.bfloat16)
    tensor_size = lax.axis_size("tensor")
    chips = tensor_size // 2
    member = lax.axis_index("tensor")
    chip = member // 2
    core = member % 2
    block = pre_hidden.shape[0]

    def route(k, flip):
        return [(i, ((i // 2 + k) % chips) * 2 + ((i % 2) ^ flip)) for i in range(tensor_size)]

    across_tokens = [lax.ppermute(normed, "tensor", route(k, 0)) for k in range(1, chips)]
    across_tokens, held_weight = lax.optimization_barrier((across_tokens, out_weight))
    same_core_tokens = [normed] + list(across_tokens)
    sibling_tokens = [lax.ppermute(t, "tensor", route(0, 1)) for t in same_core_tokens]
    sibling_tokens, slot_rows = lax.optimization_barrier((sibling_tokens, slot_rows))
    across_chips = [lax.ppermute(held_weight, "tensor", route(k, 0)) for k in range(1, chips)]
    bias_row = qkv_bias.astype(jnp.float32)
    merged_rows = jnp.zeros((tensor_size * block, qkv_weight.shape[1]), jnp.bfloat16)
    for flip, token_blocks in ((0, same_core_tokens), (1, sibling_tokens)):
        for k, token_block in enumerate(token_blocks):
            source = ((chip - k) % chips) * 2 + (core ^ flip)
            projected = (
                jnp.dot(token_block, qkv_weight, preferred_element_type=jnp.float32) + bias_row
            ).astype(jnp.bfloat16)
            merged_rows = lax.dynamic_update_slice_in_dim(merged_rows, projected, source * block, 0)
    context = prefill_attention_kernel(
        merged_rows, pre_keys[0], pre_values[0], prefix_lengths, slopes, head_size
    )
    context, across_chips = lax.optimization_barrier((context, across_chips))
    same_core = [out_weight] + list(across_chips)
    weight_blocks = same_core + [lax.ppermute(w, "tensor", route(0, 1)) for w in same_core]
    pieces = []
    for flip in (0, 1):
        for k in range(chips):
            if k == 0 and flip == 0:
                pieces.append(lax.dynamic_slice_in_dim(context, member * block, block))
                continue
            target = ((chip + k) % chips) * 2 + (core ^ flip)
            outgoing = lax.dynamic_slice_in_dim(context, target * block, block)
            pieces.append(lax.ppermute(outgoing, "tensor", route(k, flip)))
    summed = jnp.dot(pieces[0], weight_blocks[0], preferred_element_type=jnp.float32)
    for piece, weight in zip(pieces[1:], weight_blocks[1:]):
        summed = summed + jnp.dot(piece, weight, preferred_element_type=jnp.float32)
    pre_output = (summed + bias_sum + pre_hidden.astype(jnp.float32)).astype(jnp.bfloat16)
    returned = slot_rows
    step = 1
    while step < dp_size:
        returned = jnp.concatenate(
            [returned, lax.ppermute(returned, "dp", [(i, i ^ step) for i in range(dp_size)])], axis=0
        )
        step *= 2
    slot_wanted = lax.dynamic_slice_in_dim(slot_of, first_slot, slot_count)
    back = ((slot_wanted // slot_count) ^ group) * slot_count + slot_wanted % slot_count
    take = (back[:, None] == jnp.arange(returned.shape[0], dtype=jnp.int32)[None, :]).astype(jnp.bfloat16)
    dec_output = jnp.dot(take, returned, preferred_element_type=jnp.float32).astype(jnp.bfloat16)
    return (pre_output, dec_output)


def solution(mesh):
    placed = (
        P(("dp", "tensor"), None),
        P("dp", None),
        P(),
        P(),
        P(None, "tensor"),
        P("tensor"),
        P("tensor", None),
        P(),
        P("dp", None, "tensor"),
        P("dp", None, "tensor"),
        P("dp", None, "tensor"),
        P("dp", None, "tensor"),
        P("dp"),
        P("dp"),
        P(),
    )
    return jax.shard_map(
        per_device,
        mesh=mesh,
        in_specs=placed,
        out_specs=(P(("dp", "tensor"), None), P("dp", None)),
        check_vma=False,
    )
```

```python
import math

import jax
import jax.numpy as jnp
from jax import lax
from jax.sharding import PartitionSpec as P
from jax.experimental import pallas as pl
from jax.experimental.pallas import tpu as pltpu
import functools

H = 16
HD = 128


EPSILON = 1e-05


def normalize(values, norm_gain, norm_shift):
    values = values.astype(jnp.float32)
    center = values - jnp.mean(values, axis=-1, keepdims=True)
    spread = jnp.mean(center * center, axis=-1, keepdims=True)
    scaled = center * lax.rsqrt(spread + EPSILON)
    return (scaled * norm_gain.astype(jnp.float32) + norm_shift.astype(jnp.float32)).astype(
        jnp.bfloat16
    )


def alibi_slopes(first_head, head_count, total_heads):
    head_ids = (first_head + jnp.arange(head_count, dtype=jnp.int32)).astype(jnp.float32)
    return jnp.exp2(-8.0 * (head_ids + 1.0) / total_heads)


def prefill_attention(merged_rows, cache_keys, cache_values, prefix, slopes):
    queries = merged_rows[:, :, 0]
    new_keys = merged_rows[:, :, 1]
    new_values = merged_rows[:, :, 2]
    group_size = merged_rows.shape[0]
    cache_size = cache_keys.shape[0]
    factor = 1.0 / math.sqrt(merged_rows.shape[-1])
    query_pos = prefix + jnp.arange(group_size, dtype=jnp.int32)
    cache_pos = jnp.arange(cache_size, dtype=jnp.int32)
    cache_dist = (query_pos[:, None] - cache_pos[None, :]).astype(jnp.float32)
    new_dist = (query_pos[:, None] - query_pos[None, :]).astype(jnp.float32)
    cache_scores = (
        jnp.einsum("qhd,khd->hqk", queries, cache_keys, preferred_element_type=jnp.float32) * factor
    )
    cache_scores = cache_scores - slopes[:, None, None] * cache_dist[None]
    cache_scores = jnp.where((cache_pos < prefix)[None, None, :], cache_scores, -jnp.inf)
    new_scores = (
        jnp.einsum("qhd,khd->hqk", queries, new_keys, preferred_element_type=jnp.float32) * factor
    )
    new_scores = new_scores - slopes[:, None, None] * new_dist[None]
    causal = (
        jnp.arange(group_size, dtype=jnp.int32)[None, :]
        <= jnp.arange(group_size, dtype=jnp.int32)[:, None]
    )
    new_scores = jnp.where(causal[None], new_scores, -jnp.inf)
    highest = jnp.maximum(
        jnp.max(cache_scores, axis=-1, keepdims=True), jnp.max(new_scores, axis=-1, keepdims=True)
    )
    cache_exp = jnp.exp(cache_scores - highest)
    new_exp = jnp.exp(new_scores - highest)
    denominator = jnp.sum(cache_exp, axis=-1, keepdims=True) + jnp.sum(
        new_exp, axis=-1, keepdims=True
    )
    cache_probs = (cache_exp / denominator).astype(jnp.bfloat16)
    new_probs = (new_exp / denominator).astype(jnp.bfloat16)
    context = jnp.einsum(
        "hqk,khd->qhd", cache_probs, cache_values, preferred_element_type=jnp.float32
    )
    context = context + jnp.einsum(
        "hqk,khd->qhd", new_probs, new_values, preferred_element_type=jnp.float32
    )
    return context.astype(jnp.bfloat16).reshape(group_size, -1)


def _prefill_kernel(prefix_ref, slopes_ref, q_ref, kn_ref, vn_ref, kc_ref, vc_ref, o_ref, *, tq):
    h = pl.program_id(0)
    i = pl.program_id(1)
    prefix = prefix_ref[0]
    slope = slopes_ref[h]
    factor = 1.0 / math.sqrt(q_ref.shape[-1])
    q = q_ref[...]
    dims = (((1,), (1,)), ((), ()))
    cache_size = kc_ref.shape[0]
    group = kn_ref.shape[0]
    q_tok = i * tq + lax.broadcasted_iota(jnp.int32, (tq, 1), 0)
    q_pos = prefix + q_tok
    c_pos = lax.broadcasted_iota(jnp.int32, (1, cache_size), 1)
    k_tok = lax.broadcasted_iota(jnp.int32, (1, group), 1)
    s_c = lax.dot_general(q, kc_ref[...], dims, preferred_element_type=jnp.float32) * factor
    s_c = s_c - slope * (q_pos - c_pos).astype(jnp.float32)
    s_c = jnp.where(c_pos < prefix, s_c, -jnp.inf)
    s_n = lax.dot_general(q, kn_ref[...], dims, preferred_element_type=jnp.float32) * factor
    s_n = s_n - slope * (q_tok - k_tok).astype(jnp.float32)
    s_n = jnp.where(k_tok <= q_tok, s_n, -jnp.inf)
    m = jnp.maximum(jnp.max(s_c, axis=-1, keepdims=True), jnp.max(s_n, axis=-1, keepdims=True))
    e_c = jnp.exp(s_c - m)
    e_n = jnp.exp(s_n - m)
    l = jnp.sum(e_c, axis=-1, keepdims=True) + jnp.sum(e_n, axis=-1, keepdims=True)
    p_c = (e_c / l).astype(jnp.bfloat16)
    p_n = (e_n / l).astype(jnp.bfloat16)
    ctx = jnp.dot(p_c, vc_ref[...], preferred_element_type=jnp.float32)
    ctx = ctx + jnp.dot(p_n, vn_ref[...], preferred_element_type=jnp.float32)
    o_ref[...] = ctx.astype(o_ref.dtype)

def prefill_attention_kernel(merged, cache_keys, cache_values, prefix, slopes, head_size, tq=256):
    group = merged.shape[0]
    heads = merged.shape[1] // (3 * head_size)
    cache_size = cache_keys.shape[0]
    col = lambda c: (lambda h, i, *_: (0, h * 3 + c))
    return pl.pallas_call(
        functools.partial(_prefill_kernel, tq=tq),
        out_shape=jax.ShapeDtypeStruct((group, heads * head_size), jnp.bfloat16),
        grid_spec=pltpu.PrefetchScalarGridSpec(
            num_scalar_prefetch=2,
            grid=(heads, group // tq),
            in_specs=[
                pl.BlockSpec((tq, head_size), lambda h, i, *_: (i, h * 3)),
                pl.BlockSpec((group, head_size), col(1)),
                pl.BlockSpec((group, head_size), col(2)),
                pl.BlockSpec((cache_size, head_size), lambda h, i, *_: (0, h)),
                pl.BlockSpec((cache_size, head_size), lambda h, i, *_: (0, h)),
            ],
            out_specs=pl.BlockSpec((tq, head_size), lambda h, i, *_: (i, h)),
        ),
        cost_estimate=pl.CostEstimate(
            flops=4 * heads * group * (group + cache_size) * head_size,
            transcendentals=heads * group * (group + cache_size),
            bytes_accessed=2 * (group * heads * 3 * head_size + 2 * cache_size * heads * head_size + group * heads * head_size),
        ),
    )(prefix, slopes, merged, merged, merged, cache_keys, cache_values)


def decode_attention(query_row, new_key, new_value, cache_keys, cache_values, length, slopes):
    heads, head_size = query_row.shape
    factor = 1.0 / math.sqrt(head_size)
    cache_pos = jnp.arange(cache_keys.shape[0], dtype=jnp.int32)
    distance = (length - cache_pos).astype(jnp.float32)
    head_of_col = jnp.arange(heads * head_size, dtype=jnp.int32) // head_size
    own_head = head_of_col[:, None] == jnp.arange(heads, dtype=jnp.int32)[None, :]
    block_query = jnp.where(own_head, query_row.reshape(-1)[:, None], jnp.zeros((), query_row.dtype))
    cache_scores = jnp.dot(cache_keys, block_query, preferred_element_type=jnp.float32).T * factor
    cache_scores = cache_scores - slopes[:, None] * distance[None, :]
    cache_scores = jnp.where((cache_pos < length)[None, :], cache_scores, -jnp.inf)
    own_score = (
        jnp.einsum("hd,hd->h", query_row, new_key, preferred_element_type=jnp.float32)[:, None]
        * factor
    )
    highest = jnp.maximum(jnp.max(cache_scores, axis=-1, keepdims=True), own_score)
    cache_exp = jnp.exp(cache_scores - highest)
    own_exp = jnp.exp(own_score - highest)
    denominator = jnp.sum(cache_exp, axis=-1, keepdims=True) + own_exp
    cache_probs = (cache_exp / denominator).astype(jnp.bfloat16)
    own_prob = (own_exp / denominator).astype(jnp.bfloat16)
    every_head = jnp.dot(cache_probs, cache_values, preferred_element_type=jnp.float32)
    context = jnp.sum(jnp.where(own_head.T, every_head, 0.0), axis=0).reshape(heads, head_size)
    context = context + own_prob.astype(jnp.float32) * new_value.astype(jnp.float32)
    return context.astype(jnp.bfloat16).reshape(-1)


def per_device(
    pre_hidden,
    dec_hidden,
    norm_gain,
    norm_shift,
    qkv_weight,
    qkv_bias,
    out_weight,
    out_bias,
    pre_keys,
    pre_values,
    dec_keys,
    dec_values,
    prefix_lengths,
    cache_lengths,
    slot_of,
):
    head_size = HD
    local_heads = qkv_weight.shape[1] // (3 * head_size)
    slopes = alibi_slopes(lax.axis_index("tensor") * local_heads, local_heads, H)
    bias_sum = out_bias.astype(jnp.float32)
    normed = normalize(pre_hidden, norm_gain, norm_shift)
    normed, dec_hidden = lax.optimization_barrier((normed, dec_hidden))
    slot_count = dec_hidden.shape[0]
    dp_size = lax.axis_size("dp")
    tensor_size = lax.axis_size("tensor")
    group = lax.axis_index("dp")
    member = lax.axis_index("tensor")
    first_slot = group * slot_count
    shifted_rows = dec_hidden
    step = 1
    while step < dp_size:
        shifted_rows = jnp.concatenate(
            [shifted_rows, lax.ppermute(shifted_rows, "dp", [(i, i ^ step) for i in range(dp_size)])], axis=0
        )
        step *= 2
    slot_ids = first_slot + jnp.arange(slot_count, dtype=jnp.int32)
    request_ids = jnp.arange(slot_of.shape[0], dtype=jnp.int32)
    uses_slot = slot_of[None, :] == slot_ids[:, None]
    request_of_slot = jnp.sum(jnp.where(uses_slot, request_ids[None, :], 0), axis=1)
    arrival = ((request_of_slot // slot_count) ^ group) * slot_count + request_of_slot % slot_count
    pick = (arrival[:, None] == jnp.arange(shifted_rows.shape[0], dtype=jnp.int32)[None, :]).astype(
        jnp.bfloat16
    )
    arrived = jnp.dot(pick, shifted_rows, preferred_element_type=jnp.float32).astype(jnp.bfloat16)
    normed_slots = normalize(arrived, norm_gain, norm_shift)
    merged_slots = (
        jnp.dot(normed_slots, qkv_weight, preferred_element_type=jnp.float32)
        + qkv_bias.astype(jnp.float32)
    ).astype(jnp.bfloat16)
    merged_slots = merged_slots.reshape(slot_count, local_heads, 3, head_size)
    dec_cache = dec_keys.shape[1]
    slot_context = jax.vmap(decode_attention, in_axes=(0, 0, 0, 0, 0, 0, None))(
        merged_slots[:, :, 0],
        merged_slots[:, :, 1],
        merged_slots[:, :, 2],
        dec_keys,
        dec_values,
        cache_lengths,
        slopes,
    )
    slot_partial = jnp.dot(slot_context, out_weight, preferred_element_type=jnp.float32)
    partials = slot_partial
    step = 1
    while step < tensor_size:
        partials = jnp.concatenate(
            [partials, lax.ppermute(partials, "tensor", [(i, i ^ step) for i in range(tensor_size)])], axis=0
        )
        step *= 2
    partials = partials.reshape(tensor_size, slot_count, -1)
    slot_summed = partials[member ^ 0]
    for source in range(1, tensor_size):
        slot_summed = slot_summed + partials[member ^ source]
    slot_rows = (slot_summed + bias_sum + arrived.astype(jnp.float32)).astype(jnp.bfloat16)
    tensor_size = lax.axis_size("tensor")
    chips = tensor_size // 2
    member = lax.axis_index("tensor")
    chip = member // 2
    core = member % 2
    block = pre_hidden.shape[0]

    def route(k, flip):
        return [(i, ((i // 2 + k) % chips) * 2 + ((i % 2) ^ flip)) for i in range(tensor_size)]

    across_tokens = [lax.ppermute(normed, "tensor", route(k, 0)) for k in range(1, chips)]
    across_tokens, held_weight = lax.optimization_barrier((across_tokens, out_weight))
    same_core_tokens = [normed] + list(across_tokens)
    sibling_tokens = [lax.ppermute(t, "tensor", route(0, 1)) for t in same_core_tokens]
    sibling_tokens, slot_rows = lax.optimization_barrier((sibling_tokens, slot_rows))
    across_chips = [lax.ppermute(held_weight, "tensor", route(k, 0)) for k in range(1, chips)]
    bias_row = qkv_bias.astype(jnp.float32)
    merged_rows = jnp.zeros((tensor_size * block, qkv_weight.shape[1]), jnp.bfloat16)
    for flip, token_blocks in ((0, same_core_tokens), (1, sibling_tokens)):
        for k, token_block in enumerate(token_blocks):
            source = ((chip - k) % chips) * 2 + (core ^ flip)
            projected = (
                jnp.dot(token_block, qkv_weight, preferred_element_type=jnp.float32) + bias_row
            ).astype(jnp.bfloat16)
            merged_rows = lax.dynamic_update_slice_in_dim(merged_rows, projected, source * block, 0)
    returned = slot_rows
    step = 1
    while step < dp_size:
        returned = jnp.concatenate(
            [returned, lax.ppermute(returned, "dp", [(i, i ^ step) for i in range(dp_size)])], axis=0
        )
        step *= 2
    slot_wanted = lax.dynamic_slice_in_dim(slot_of, first_slot, slot_count)
    back = ((slot_wanted // slot_count) ^ group) * slot_count + slot_wanted % slot_count
    take = (back[:, None] == jnp.arange(returned.shape[0], dtype=jnp.int32)[None, :]).astype(jnp.bfloat16)
    dec_output = jnp.dot(take, returned, preferred_element_type=jnp.float32).astype(jnp.bfloat16)
    merged_rows, dec_output = lax.optimization_barrier((merged_rows, dec_output))
    context = prefill_attention_kernel(
        merged_rows, pre_keys[0], pre_values[0], prefix_lengths, slopes, head_size
    )
    context, across_chips = lax.optimization_barrier((context, across_chips))
    same_core = [out_weight] + list(across_chips)
    weight_blocks = same_core + [lax.ppermute(w, "tensor", route(0, 1)) for w in same_core]
    pieces = []
    for flip in (0, 1):
        for k in range(chips):
            if k == 0 and flip == 0:
                pieces.append(lax.dynamic_slice_in_dim(context, member * block, block))
                continue
            target = ((chip + k) % chips) * 2 + (core ^ flip)
            outgoing = lax.dynamic_slice_in_dim(context, target * block, block)
            pieces.append(lax.ppermute(outgoing, "tensor", route(k, flip)))
    summed = jnp.dot(pieces[0], weight_blocks[0], preferred_element_type=jnp.float32)
    for piece, weight in zip(pieces[1:], weight_blocks[1:]):
        summed = summed + jnp.dot(piece, weight, preferred_element_type=jnp.float32)
    pre_output = (summed + bias_sum + pre_hidden.astype(jnp.float32)).astype(jnp.bfloat16)
    return (pre_output, dec_output)


def solution(mesh):
    placed = (
        P(("dp", "tensor"), None),
        P("dp", None),
        P(),
        P(),
        P(None, "tensor"),
        P("tensor"),
        P("tensor", None),
        P(),
        P("dp", None, "tensor"),
        P("dp", None, "tensor"),
        P("dp", None, "tensor"),
        P("dp", None, "tensor"),
        P("dp"),
        P("dp"),
        P(),
    )
    return jax.shard_map(
        per_device,
        mesh=mesh,
        in_specs=placed,
        out_specs=(P(("dp", "tensor"), None), P("dp", None)),
        check_vma=False,
    )
```

```python
import math

import jax
import jax.numpy as jnp
from jax import lax
from jax.sharding import PartitionSpec as P
from jax.experimental import pallas as pl
from jax.experimental.pallas import tpu as pltpu
import functools

H = 16
HD = 128


EPSILON = 1e-05


def normalize(values, norm_gain, norm_shift):
    values = values.astype(jnp.float32)
    center = values - jnp.mean(values, axis=-1, keepdims=True)
    spread = jnp.mean(center * center, axis=-1, keepdims=True)
    scaled = center * lax.rsqrt(spread + EPSILON)
    return (scaled * norm_gain.astype(jnp.float32) + norm_shift.astype(jnp.float32)).astype(
        jnp.bfloat16
    )


def alibi_slopes(first_head, head_count, total_heads):
    head_ids = (first_head + jnp.arange(head_count, dtype=jnp.int32)).astype(jnp.float32)
    return jnp.exp2(-8.0 * (head_ids + 1.0) / total_heads)


def prefill_attention(merged_rows, cache_keys, cache_values, prefix, slopes):
    queries = merged_rows[:, :, 0]
    new_keys = merged_rows[:, :, 1]
    new_values = merged_rows[:, :, 2]
    group_size = merged_rows.shape[0]
    cache_size = cache_keys.shape[0]
    factor = 1.0 / math.sqrt(merged_rows.shape[-1])
    query_pos = prefix + jnp.arange(group_size, dtype=jnp.int32)
    cache_pos = jnp.arange(cache_size, dtype=jnp.int32)
    cache_dist = (query_pos[:, None] - cache_pos[None, :]).astype(jnp.float32)
    new_dist = (query_pos[:, None] - query_pos[None, :]).astype(jnp.float32)
    cache_scores = (
        jnp.einsum("qhd,khd->hqk", queries, cache_keys, preferred_element_type=jnp.float32) * factor
    )
    cache_scores = cache_scores - slopes[:, None, None] * cache_dist[None]
    cache_scores = jnp.where((cache_pos < prefix)[None, None, :], cache_scores, -jnp.inf)
    new_scores = (
        jnp.einsum("qhd,khd->hqk", queries, new_keys, preferred_element_type=jnp.float32) * factor
    )
    new_scores = new_scores - slopes[:, None, None] * new_dist[None]
    causal = (
        jnp.arange(group_size, dtype=jnp.int32)[None, :]
        <= jnp.arange(group_size, dtype=jnp.int32)[:, None]
    )
    new_scores = jnp.where(causal[None], new_scores, -jnp.inf)
    highest = jnp.maximum(
        jnp.max(cache_scores, axis=-1, keepdims=True), jnp.max(new_scores, axis=-1, keepdims=True)
    )
    cache_exp = jnp.exp(cache_scores - highest)
    new_exp = jnp.exp(new_scores - highest)
    denominator = jnp.sum(cache_exp, axis=-1, keepdims=True) + jnp.sum(
        new_exp, axis=-1, keepdims=True
    )
    cache_probs = (cache_exp / denominator).astype(jnp.bfloat16)
    new_probs = (new_exp / denominator).astype(jnp.bfloat16)
    context = jnp.einsum(
        "hqk,khd->qhd", cache_probs, cache_values, preferred_element_type=jnp.float32
    )
    context = context + jnp.einsum(
        "hqk,khd->qhd", new_probs, new_values, preferred_element_type=jnp.float32
    )
    return context.astype(jnp.bfloat16).reshape(group_size, -1)


def _prefill_kernel(prefix_ref, slopes_ref, tile_ref, q_ref, kn_ref, vn_ref, kc_ref, vc_ref, o_ref, *, tq):
    h = pl.program_id(0)
    i = tile_ref[0]
    prefix = prefix_ref[0]
    slope = slopes_ref[h]
    factor = 1.0 / math.sqrt(q_ref.shape[-1])
    q = q_ref[...]
    dims = (((1,), (1,)), ((), ()))
    cache_size = kc_ref.shape[0]
    group = kn_ref.shape[0]
    q_tok = i * tq + lax.broadcasted_iota(jnp.int32, (tq, 1), 0)
    q_pos = prefix + q_tok
    c_pos = lax.broadcasted_iota(jnp.int32, (1, cache_size), 1)
    k_tok = lax.broadcasted_iota(jnp.int32, (1, group), 1)
    s_c = lax.dot_general(q, kc_ref[...], dims, preferred_element_type=jnp.float32) * factor
    s_c = s_c - slope * (q_pos - c_pos).astype(jnp.float32)
    s_c = jnp.where(c_pos < prefix, s_c, -jnp.inf)
    s_n = lax.dot_general(q, kn_ref[...], dims, preferred_element_type=jnp.float32) * factor
    s_n = s_n - slope * (q_tok - k_tok).astype(jnp.float32)
    s_n = jnp.where(k_tok <= q_tok, s_n, -jnp.inf)
    m = jnp.maximum(jnp.max(s_c, axis=-1, keepdims=True), jnp.max(s_n, axis=-1, keepdims=True))
    e_c = jnp.exp(s_c - m)
    e_n = jnp.exp(s_n - m)
    l = jnp.sum(e_c, axis=-1, keepdims=True) + jnp.sum(e_n, axis=-1, keepdims=True)
    p_c = (e_c / l).astype(jnp.bfloat16)
    p_n = (e_n / l).astype(jnp.bfloat16)
    ctx = jnp.dot(p_c, vc_ref[...], preferred_element_type=jnp.float32)
    ctx = ctx + jnp.dot(p_n, vn_ref[...], preferred_element_type=jnp.float32)
    o_ref[...] = ctx.astype(o_ref.dtype)


def prefill_attention_tile(merged, cache_keys, cache_values, prefix, slopes, tile, head_size, tq):
    group = merged.shape[0]
    heads = merged.shape[1] // (3 * head_size)
    cache_size = cache_keys.shape[0]
    col = lambda c: (lambda h, *_: (0, h * 3 + c))
    return pl.pallas_call(
        functools.partial(_prefill_kernel, tq=tq),
        out_shape=jax.ShapeDtypeStruct((tq, heads * head_size), jnp.bfloat16),
        grid_spec=pltpu.PrefetchScalarGridSpec(
            num_scalar_prefetch=3,
            grid=(heads,),
            in_specs=[
                pl.BlockSpec((tq, head_size), lambda h, p, s, t: (t[0], h * 3)),
                pl.BlockSpec((group, head_size), col(1)),
                pl.BlockSpec((group, head_size), col(2)),
                pl.BlockSpec((cache_size, head_size), lambda h, *_: (0, h)),
                pl.BlockSpec((cache_size, head_size), lambda h, *_: (0, h)),
            ],
            out_specs=pl.BlockSpec((tq, head_size), lambda h, *_: (0, h)),
        ),
        cost_estimate=pl.CostEstimate(
            flops=4 * heads * tq * (group + cache_size) * head_size,
            transcendentals=heads * tq * (group + cache_size),
            bytes_accessed=2 * (4 * group * heads * head_size + 2 * tq * heads * head_size),
        ),
    )(prefix, slopes, tile, merged, merged, merged, cache_keys, cache_values)


def decode_attention(query_row, new_key, new_value, cache_keys, cache_values, length, slopes):
    heads, head_size = query_row.shape
    factor = 1.0 / math.sqrt(head_size)
    cache_pos = jnp.arange(cache_keys.shape[0], dtype=jnp.int32)
    distance = (length - cache_pos).astype(jnp.float32)
    head_of_col = jnp.arange(heads * head_size, dtype=jnp.int32) // head_size
    own_head = head_of_col[:, None] == jnp.arange(heads, dtype=jnp.int32)[None, :]
    block_query = jnp.where(own_head, query_row.reshape(-1)[:, None], jnp.zeros((), query_row.dtype))
    cache_scores = jnp.dot(cache_keys, block_query, preferred_element_type=jnp.float32).T * factor
    cache_scores = cache_scores - slopes[:, None] * distance[None, :]
    cache_scores = jnp.where((cache_pos < length)[None, :], cache_scores, -jnp.inf)
    own_score = (
        jnp.einsum("hd,hd->h", query_row, new_key, preferred_element_type=jnp.float32)[:, None]
        * factor
    )
    highest = jnp.maximum(jnp.max(cache_scores, axis=-1, keepdims=True), own_score)
    cache_exp = jnp.exp(cache_scores - highest)
    own_exp = jnp.exp(own_score - highest)
    denominator = jnp.sum(cache_exp, axis=-1, keepdims=True) + own_exp
    cache_probs = (cache_exp / denominator).astype(jnp.bfloat16)
    own_prob = (own_exp / denominator).astype(jnp.bfloat16)
    every_head = jnp.dot(cache_probs, cache_values, preferred_element_type=jnp.float32)
    context = jnp.sum(jnp.where(own_head.T, every_head, 0.0), axis=0).reshape(heads, head_size)
    context = context + own_prob.astype(jnp.float32) * new_value.astype(jnp.float32)
    return context.astype(jnp.bfloat16).reshape(-1)


def per_device(
    pre_hidden,
    dec_hidden,
    norm_gain,
    norm_shift,
    qkv_weight,
    qkv_bias,
    out_weight,
    out_bias,
    pre_keys,
    pre_values,
    dec_keys,
    dec_values,
    prefix_lengths,
    cache_lengths,
    slot_of,
):
    head_size = HD
    local_heads = qkv_weight.shape[1] // (3 * head_size)
    slopes = alibi_slopes(lax.axis_index("tensor") * local_heads, local_heads, H)
    bias_sum = out_bias.astype(jnp.float32)
    normed = normalize(pre_hidden, norm_gain, norm_shift)
    normed, dec_hidden = lax.optimization_barrier((normed, dec_hidden))
    slot_count = dec_hidden.shape[0]
    dp_size = lax.axis_size("dp")
    tensor_size = lax.axis_size("tensor")
    group = lax.axis_index("dp")
    member = lax.axis_index("tensor")
    first_slot = group * slot_count
    shifted_rows = dec_hidden
    step = 1
    while step < dp_size:
        shifted_rows = jnp.concatenate(
            [shifted_rows, lax.ppermute(shifted_rows, "dp", [(i, i ^ step) for i in range(dp_size)])], axis=0
        )
        step *= 2
    slot_ids = first_slot + jnp.arange(slot_count, dtype=jnp.int32)
    request_ids = jnp.arange(slot_of.shape[0], dtype=jnp.int32)
    uses_slot = slot_of[None, :] == slot_ids[:, None]
    request_of_slot = jnp.sum(jnp.where(uses_slot, request_ids[None, :], 0), axis=1)
    arrival = ((request_of_slot // slot_count) ^ group) * slot_count + request_of_slot % slot_count
    pick = (arrival[:, None] == jnp.arange(shifted_rows.shape[0], dtype=jnp.int32)[None, :]).astype(
        jnp.bfloat16
    )
    arrived = jnp.dot(pick, shifted_rows, preferred_element_type=jnp.float32).astype(jnp.bfloat16)
    normed_slots = normalize(arrived, norm_gain, norm_shift)
    merged_slots = (
        jnp.dot(normed_slots, qkv_weight, preferred_element_type=jnp.float32)
        + qkv_bias.astype(jnp.float32)
    ).astype(jnp.bfloat16)
    merged_slots = merged_slots.reshape(slot_count, local_heads, 3, head_size)
    dec_cache = dec_keys.shape[1]
    slot_context = jax.vmap(decode_attention, in_axes=(0, 0, 0, 0, 0, 0, None))(
        merged_slots[:, :, 0],
        merged_slots[:, :, 1],
        merged_slots[:, :, 2],
        dec_keys,
        dec_values,
        cache_lengths,
        slopes,
    )
    slot_partial = jnp.dot(slot_context, out_weight, preferred_element_type=jnp.float32)
    partials = slot_partial
    step = 1
    while step < tensor_size:
        partials = jnp.concatenate(
            [partials, lax.ppermute(partials, "tensor", [(i, i ^ step) for i in range(tensor_size)])], axis=0
        )
        step *= 2
    partials = partials.reshape(tensor_size, slot_count, -1)
    slot_summed = partials[member ^ 0]
    for source in range(1, tensor_size):
        slot_summed = slot_summed + partials[member ^ source]
    slot_rows = (slot_summed + bias_sum + arrived.astype(jnp.float32)).astype(jnp.bfloat16)
    tensor_size = lax.axis_size("tensor")
    chips = tensor_size // 2
    member = lax.axis_index("tensor")
    chip = member // 2
    core = member % 2
    block = pre_hidden.shape[0]

    def route(k, flip):
        return [(i, ((i // 2 + k) % chips) * 2 + ((i % 2) ^ flip)) for i in range(tensor_size)]

    across_tokens = [lax.ppermute(normed, "tensor", route(k, 0)) for k in range(1, chips)]
    across_tokens, held_weight = lax.optimization_barrier((across_tokens, out_weight))
    same_core_tokens = [normed] + list(across_tokens)
    sibling_tokens = [lax.ppermute(t, "tensor", route(0, 1)) for t in same_core_tokens]
    sibling_tokens, slot_rows = lax.optimization_barrier((sibling_tokens, slot_rows))
    across_chips = [lax.ppermute(held_weight, "tensor", route(k, 0)) for k in range(1, chips)]
    bias_row = qkv_bias.astype(jnp.float32)
    merged_rows = jnp.zeros((tensor_size * block, qkv_weight.shape[1]), jnp.bfloat16)
    for flip, token_blocks in ((0, same_core_tokens), (1, sibling_tokens)):
        for k, token_block in enumerate(token_blocks):
            source = ((chip - k) % chips) * 2 + (core ^ flip)
            projected = (
                jnp.dot(token_block, qkv_weight, preferred_element_type=jnp.float32) + bias_row
            ).astype(jnp.bfloat16)
            merged_rows = lax.dynamic_update_slice_in_dim(merged_rows, projected, source * block, 0)
    returned = slot_rows
    step = 1
    while step < dp_size:
        returned = jnp.concatenate(
            [returned, lax.ppermute(returned, "dp", [(i, i ^ step) for i in range(dp_size)])], axis=0
        )
        step *= 2
    slot_wanted = lax.dynamic_slice_in_dim(slot_of, first_slot, slot_count)
    back = ((slot_wanted // slot_count) ^ group) * slot_count + slot_wanted % slot_count
    take = (back[:, None] == jnp.arange(returned.shape[0], dtype=jnp.int32)[None, :]).astype(jnp.bfloat16)
    dec_output = jnp.dot(take, returned, preferred_element_type=jnp.float32).astype(jnp.bfloat16)
    merged_rows, dec_output = lax.optimization_barrier((merged_rows, dec_output))
    order = [(k, flip) for flip in (0, 1) for k in range(chips)]
    pieces = [None] * len(order)
    for position in sorted(range(len(order)), key=lambda n: (order[n] == (0, 0), -order[n][0], -order[n][1])):
        k, flip = order[position]
        target = ((chip + k) % chips) * 2 + (core ^ flip)
        context = prefill_attention_tile(
            merged_rows, pre_keys[0], pre_values[0], prefix_lengths, slopes,
            target.reshape(1).astype(jnp.int32), head_size, block,
        )
        pieces[position] = context if (k, flip) == (0, 0) else lax.ppermute(context, "tensor", route(k, flip))
    across_chips = list(across_chips)
    pieces[0], across_chips = lax.optimization_barrier((pieces[0], across_chips))
    same_core = [out_weight] + list(across_chips)
    weight_blocks = same_core + [lax.ppermute(w, "tensor", route(0, 1)) for w in same_core]
    summed = jnp.dot(pieces[0], weight_blocks[0], preferred_element_type=jnp.float32)
    for piece, weight in zip(pieces[1:], weight_blocks[1:]):
        summed = summed + jnp.dot(piece, weight, preferred_element_type=jnp.float32)
    pre_output = (summed + bias_sum + pre_hidden.astype(jnp.float32)).astype(jnp.bfloat16)
    return (pre_output, dec_output)


def solution(mesh):
    placed = (
        P(("dp", "tensor"), None),
        P("dp", None),
        P(),
        P(),
        P(None, "tensor"),
        P("tensor"),
        P("tensor", None),
        P(),
        P("dp", None, "tensor"),
        P("dp", None, "tensor"),
        P("dp", None, "tensor"),
        P("dp", None, "tensor"),
        P("dp"),
        P("dp"),
        P(),
    )
    return jax.shard_map(
        per_device,
        mesh=mesh,
        in_specs=placed,
        out_specs=(P(("dp", "tensor"), None), P("dp", None)),
        check_vma=False,
    )
```

```python
import math

import jax
import jax.numpy as jnp
from jax import lax
from jax.sharding import PartitionSpec as P
from jax.experimental import pallas as pl
from jax.experimental.pallas import tpu as pltpu
import functools

H = 16
HD = 128


EPSILON = 1e-05


def normalize(values, norm_gain, norm_shift):
    values = values.astype(jnp.float32)
    center = values - jnp.mean(values, axis=-1, keepdims=True)
    spread = jnp.mean(center * center, axis=-1, keepdims=True)
    scaled = center * lax.rsqrt(spread + EPSILON)
    return (scaled * norm_gain.astype(jnp.float32) + norm_shift.astype(jnp.float32)).astype(
        jnp.bfloat16
    )


def alibi_slopes(first_head, head_count, total_heads):
    head_ids = (first_head + jnp.arange(head_count, dtype=jnp.int32)).astype(jnp.float32)
    return jnp.exp2(-8.0 * (head_ids + 1.0) / total_heads)


def prefill_attention(merged_rows, cache_keys, cache_values, prefix, slopes):
    queries = merged_rows[:, :, 0]
    new_keys = merged_rows[:, :, 1]
    new_values = merged_rows[:, :, 2]
    group_size = merged_rows.shape[0]
    cache_size = cache_keys.shape[0]
    factor = 1.0 / math.sqrt(merged_rows.shape[-1])
    query_pos = prefix + jnp.arange(group_size, dtype=jnp.int32)
    cache_pos = jnp.arange(cache_size, dtype=jnp.int32)
    cache_dist = (query_pos[:, None] - cache_pos[None, :]).astype(jnp.float32)
    new_dist = (query_pos[:, None] - query_pos[None, :]).astype(jnp.float32)
    cache_scores = (
        jnp.einsum("qhd,khd->hqk", queries, cache_keys, preferred_element_type=jnp.float32) * factor
    )
    cache_scores = cache_scores - slopes[:, None, None] * cache_dist[None]
    cache_scores = jnp.where((cache_pos < prefix)[None, None, :], cache_scores, -jnp.inf)
    new_scores = (
        jnp.einsum("qhd,khd->hqk", queries, new_keys, preferred_element_type=jnp.float32) * factor
    )
    new_scores = new_scores - slopes[:, None, None] * new_dist[None]
    causal = (
        jnp.arange(group_size, dtype=jnp.int32)[None, :]
        <= jnp.arange(group_size, dtype=jnp.int32)[:, None]
    )
    new_scores = jnp.where(causal[None], new_scores, -jnp.inf)
    highest = jnp.maximum(
        jnp.max(cache_scores, axis=-1, keepdims=True), jnp.max(new_scores, axis=-1, keepdims=True)
    )
    cache_exp = jnp.exp(cache_scores - highest)
    new_exp = jnp.exp(new_scores - highest)
    denominator = jnp.sum(cache_exp, axis=-1, keepdims=True) + jnp.sum(
        new_exp, axis=-1, keepdims=True
    )
    cache_probs = (cache_exp / denominator).astype(jnp.bfloat16)
    new_probs = (new_exp / denominator).astype(jnp.bfloat16)
    context = jnp.einsum(
        "hqk,khd->qhd", cache_probs, cache_values, preferred_element_type=jnp.float32
    )
    context = context + jnp.einsum(
        "hqk,khd->qhd", new_probs, new_values, preferred_element_type=jnp.float32
    )
    return context.astype(jnp.bfloat16).reshape(group_size, -1)


def _prefill_kernel(prefix_ref, slopes_ref, q_ref, kn_ref, vn_ref, kc_ref, vc_ref, o_ref, *, tq):
    h = pl.program_id(0)
    i = pl.program_id(1)
    prefix = prefix_ref[0]
    slope = slopes_ref[h]
    factor = 1.0 / math.sqrt(q_ref.shape[-1])
    dims = (((1,), (1,)), ((), ()))
    cache_size = kc_ref.shape[0]

    def tile(last, width):
        q = q_ref[...]
        q_tok = last * tq + lax.broadcasted_iota(jnp.int32, (tq, 1), 0)
        q_pos = prefix + q_tok
        c_pos = lax.broadcasted_iota(jnp.int32, (1, cache_size), 1)
        k_tok = lax.broadcasted_iota(jnp.int32, (1, width), 1)
        s_c = lax.dot_general(q, kc_ref[...], dims, preferred_element_type=jnp.float32) * factor
        s_c = s_c - slope * (q_pos - c_pos).astype(jnp.float32)
        s_c = jnp.where(c_pos < prefix, s_c, -jnp.inf)
        s_n = lax.dot_general(q, kn_ref[:width, :], dims, preferred_element_type=jnp.float32) * factor
        s_n = s_n - slope * (q_tok - k_tok).astype(jnp.float32)
        s_n = jnp.where(k_tok <= q_tok, s_n, -jnp.inf)
        m = jnp.maximum(jnp.max(s_c, axis=-1, keepdims=True), jnp.max(s_n, axis=-1, keepdims=True))
        e_c = jnp.exp(s_c - m)
        e_n = jnp.exp(s_n - m)
        l = jnp.sum(e_c, axis=-1, keepdims=True) + jnp.sum(e_n, axis=-1, keepdims=True)
        p_c = (e_c / l).astype(jnp.bfloat16)
        p_n = (e_n / l).astype(jnp.bfloat16)
        ctx = jnp.dot(p_c, vc_ref[...], preferred_element_type=jnp.float32)
        ctx = ctx + jnp.dot(p_n, vn_ref[:width, :], preferred_element_type=jnp.float32)
        o_ref[...] = ctx.astype(o_ref.dtype)

    for last in range(kn_ref.shape[0] // tq):
        pl.when(i == last)(functools.partial(tile, last, (last + 1) * tq))


def prefill_attention_kernel(merged, cache_keys, cache_values, prefix, slopes, head_size, tq=256):
    group = merged.shape[0]
    heads = merged.shape[1] // (3 * head_size)
    cache_size = cache_keys.shape[0]
    col = lambda c: (lambda h, i, *_: (0, h * 3 + c))
    return pl.pallas_call(
        functools.partial(_prefill_kernel, tq=tq),
        out_shape=jax.ShapeDtypeStruct((group, heads * head_size), jnp.bfloat16),
        grid_spec=pltpu.PrefetchScalarGridSpec(
            num_scalar_prefetch=2,
            grid=(heads, group // tq),
            in_specs=[
                pl.BlockSpec((tq, head_size), lambda h, i, *_: (i, h * 3)),
                pl.BlockSpec((group, head_size), col(1)),
                pl.BlockSpec((group, head_size), col(2)),
                pl.BlockSpec((cache_size, head_size), lambda h, i, *_: (0, h)),
                pl.BlockSpec((cache_size, head_size), lambda h, i, *_: (0, h)),
            ],
            out_specs=pl.BlockSpec((tq, head_size), lambda h, i, *_: (i, h)),
        ),
        cost_estimate=pl.CostEstimate(
            flops=4 * heads * group * (group + cache_size) * head_size,
            transcendentals=heads * group * (group + cache_size),
            bytes_accessed=2 * (group * heads * 3 * head_size + 2 * cache_size * heads * head_size + group * heads * head_size),
        ),
    )(prefix, slopes, merged, merged, merged, cache_keys, cache_values)


def decode_attention(query_row, new_key, new_value, cache_keys, cache_values, length, slopes):
    heads, head_size = query_row.shape
    factor = 1.0 / math.sqrt(head_size)
    cache_pos = jnp.arange(cache_keys.shape[0], dtype=jnp.int32)
    distance = (length - cache_pos).astype(jnp.float32)
    head_of_col = jnp.arange(heads * head_size, dtype=jnp.int32) // head_size
    own_head = head_of_col[:, None] == jnp.arange(heads, dtype=jnp.int32)[None, :]
    block_query = jnp.where(own_head, query_row.reshape(-1)[:, None], jnp.zeros((), query_row.dtype))
    cache_scores = jnp.dot(cache_keys, block_query, preferred_element_type=jnp.float32).T * factor
    cache_scores = cache_scores - slopes[:, None] * distance[None, :]
    cache_scores = jnp.where((cache_pos < length)[None, :], cache_scores, -jnp.inf)
    own_score = (
        jnp.einsum("hd,hd->h", query_row, new_key, preferred_element_type=jnp.float32)[:, None]
        * factor
    )
    highest = jnp.maximum(jnp.max(cache_scores, axis=-1, keepdims=True), own_score)
    cache_exp = jnp.exp(cache_scores - highest)
    own_exp = jnp.exp(own_score - highest)
    denominator = jnp.sum(cache_exp, axis=-1, keepdims=True) + own_exp
    cache_probs = (cache_exp / denominator).astype(jnp.bfloat16)
    own_prob = (own_exp / denominator).astype(jnp.bfloat16)
    every_head = jnp.dot(cache_probs, cache_values, preferred_element_type=jnp.float32)
    context = jnp.sum(jnp.where(own_head.T, every_head, 0.0), axis=0).reshape(heads, head_size)
    context = context + own_prob.astype(jnp.float32) * new_value.astype(jnp.float32)
    return context.astype(jnp.bfloat16).reshape(-1)


def per_device(
    pre_hidden,
    dec_hidden,
    norm_gain,
    norm_shift,
    qkv_weight,
    qkv_bias,
    out_weight,
    out_bias,
    pre_keys,
    pre_values,
    dec_keys,
    dec_values,
    prefix_lengths,
    cache_lengths,
    slot_of,
):
    head_size = HD
    local_heads = qkv_weight.shape[1] // (3 * head_size)
    slopes = alibi_slopes(lax.axis_index("tensor") * local_heads, local_heads, H)
    bias_sum = out_bias.astype(jnp.float32)
    normed = normalize(pre_hidden, norm_gain, norm_shift)
    normed, dec_hidden = lax.optimization_barrier((normed, dec_hidden))
    slot_count = dec_hidden.shape[0]
    dp_size = lax.axis_size("dp")
    tensor_size = lax.axis_size("tensor")
    group = lax.axis_index("dp")
    member = lax.axis_index("tensor")
    first_slot = group * slot_count
    shifted_rows = dec_hidden
    step = 1
    while step < dp_size:
        shifted_rows = jnp.concatenate(
            [shifted_rows, lax.ppermute(shifted_rows, "dp", [(i, i ^ step) for i in range(dp_size)])], axis=0
        )
        step *= 2
    slot_ids = first_slot + jnp.arange(slot_count, dtype=jnp.int32)
    request_ids = jnp.arange(slot_of.shape[0], dtype=jnp.int32)
    uses_slot = slot_of[None, :] == slot_ids[:, None]
    request_of_slot = jnp.sum(jnp.where(uses_slot, request_ids[None, :], 0), axis=1)
    arrival = ((request_of_slot // slot_count) ^ group) * slot_count + request_of_slot % slot_count
    pick = (arrival[:, None] == jnp.arange(shifted_rows.shape[0], dtype=jnp.int32)[None, :]).astype(
        jnp.bfloat16
    )
    arrived = jnp.dot(pick, shifted_rows, preferred_element_type=jnp.float32).astype(jnp.bfloat16)
    normed_slots = normalize(arrived, norm_gain, norm_shift)
    merged_slots = (
        jnp.dot(normed_slots, qkv_weight, preferred_element_type=jnp.float32)
        + qkv_bias.astype(jnp.float32)
    ).astype(jnp.bfloat16)
    merged_slots = merged_slots.reshape(slot_count, local_heads, 3, head_size)
    dec_cache = dec_keys.shape[1]
    slot_context = jax.vmap(decode_attention, in_axes=(0, 0, 0, 0, 0, 0, None))(
        merged_slots[:, :, 0],
        merged_slots[:, :, 1],
        merged_slots[:, :, 2],
        dec_keys,
        dec_values,
        cache_lengths,
        slopes,
    )
    slot_partial = jnp.dot(slot_context, out_weight, preferred_element_type=jnp.float32)
    partials = slot_partial
    step = 1
    while step < tensor_size:
        partials = jnp.concatenate(
            [partials, lax.ppermute(partials, "tensor", [(i, i ^ step) for i in range(tensor_size)])], axis=0
        )
        step *= 2
    partials = partials.reshape(tensor_size, slot_count, -1)
    slot_summed = partials[member ^ 0]
    for source in range(1, tensor_size):
        slot_summed = slot_summed + partials[member ^ source]
    slot_rows = (slot_summed + bias_sum + arrived.astype(jnp.float32)).astype(jnp.bfloat16)
    tensor_size = lax.axis_size("tensor")
    chips = tensor_size // 2
    member = lax.axis_index("tensor")
    chip = member // 2
    core = member % 2
    block = pre_hidden.shape[0]

    def route(k, flip):
        return [(i, ((i // 2 + k) % chips) * 2 + ((i % 2) ^ flip)) for i in range(tensor_size)]

    across_tokens = [lax.ppermute(normed, "tensor", route(k, 0)) for k in range(1, chips)]
    across_tokens, held_weight = lax.optimization_barrier((across_tokens, out_weight))
    same_core_tokens = [normed] + list(across_tokens)
    sibling_tokens = [lax.ppermute(t, "tensor", route(0, 1)) for t in same_core_tokens]
    sibling_tokens, slot_rows = lax.optimization_barrier((sibling_tokens, slot_rows))
    across_chips = [lax.ppermute(held_weight, "tensor", route(k, 0)) for k in range(1, chips)]
    tokens = jnp.zeros((tensor_size * block, normed.shape[1]), normed.dtype)
    for flip, token_blocks in ((0, same_core_tokens), (1, sibling_tokens)):
        for k, token_block in enumerate(token_blocks):
            source = ((chip - k) % chips) * 2 + (core ^ flip)
            tokens = lax.dynamic_update_slice_in_dim(tokens, token_block, source * block, 0)
    product = jnp.dot(tokens, qkv_weight, preferred_element_type=jnp.float32)
    merged_rows = (product + qkv_bias.astype(jnp.float32)).astype(jnp.bfloat16)
    returned = slot_rows
    step = 1
    while step < dp_size:
        returned = jnp.concatenate(
            [returned, lax.ppermute(returned, "dp", [(i, i ^ step) for i in range(dp_size)])], axis=0
        )
        step *= 2
    slot_wanted = lax.dynamic_slice_in_dim(slot_of, first_slot, slot_count)
    back = ((slot_wanted // slot_count) ^ group) * slot_count + slot_wanted % slot_count
    take = (back[:, None] == jnp.arange(returned.shape[0], dtype=jnp.int32)[None, :]).astype(jnp.bfloat16)
    dec_output = jnp.dot(take, returned, preferred_element_type=jnp.float32).astype(jnp.bfloat16)
    merged_rows, dec_output = lax.optimization_barrier((merged_rows, dec_output))
    context = prefill_attention_kernel(
        merged_rows, pre_keys[0], pre_values[0], prefix_lengths, slopes, head_size
    )
    context, across_chips = lax.optimization_barrier((context, across_chips))
    same_core = [out_weight] + list(across_chips)
    weight_blocks = same_core + [lax.ppermute(w, "tensor", route(0, 1)) for w in same_core]
    pieces = []
    for flip in (0, 1):
        for k in range(chips):
            if k == 0 and flip == 0:
                pieces.append(lax.dynamic_slice_in_dim(context, member * block, block))
                continue
            target = ((chip + k) % chips) * 2 + (core ^ flip)
            outgoing = lax.dynamic_slice_in_dim(context, target * block, block)
            pieces.append(lax.ppermute(outgoing, "tensor", route(k, flip)))
    summed = jnp.dot(pieces[0], weight_blocks[0], preferred_element_type=jnp.float32)
    for piece, weight in zip(pieces[1:], weight_blocks[1:]):
        summed = summed + jnp.dot(piece, weight, preferred_element_type=jnp.float32)
    pre_output = (summed + bias_sum + pre_hidden.astype(jnp.float32)).astype(jnp.bfloat16)
    return (pre_output, dec_output)


def solution(mesh):
    placed = (
        P(("dp", "tensor"), None),
        P("dp", None),
        P(),
        P(),
        P(None, "tensor"),
        P("tensor"),
        P("tensor", None),
        P(),
        P("dp", None, "tensor"),
        P("dp", None, "tensor"),
        P("dp", None, "tensor"),
        P("dp", None, "tensor"),
        P("dp"),
        P("dp"),
        P(),
    )
    return jax.shard_map(
        per_device,
        mesh=mesh,
        in_specs=placed,
        out_specs=(P(("dp", "tensor"), None), P("dp", None)),
        check_vma=False,
    )
```

```python
import math

import jax
import jax.numpy as jnp
from jax import lax
from jax.sharding import PartitionSpec as P
from jax.experimental import pallas as pl
from jax.experimental.pallas import tpu as pltpu
import functools

H = 16
HD = 128


EPSILON = 1e-05


def normalize(values, norm_gain, norm_shift):
    values = values.astype(jnp.float32)
    center = values - jnp.mean(values, axis=-1, keepdims=True)
    spread = jnp.mean(center * center, axis=-1, keepdims=True)
    scaled = center * lax.rsqrt(spread + EPSILON)
    return (scaled * norm_gain.astype(jnp.float32) + norm_shift.astype(jnp.float32)).astype(
        jnp.bfloat16
    )


def alibi_slopes(first_head, head_count, total_heads):
    head_ids = (first_head + jnp.arange(head_count, dtype=jnp.int32)).astype(jnp.float32)
    return jnp.exp2(-8.0 * (head_ids + 1.0) / total_heads)


def prefill_attention(merged_rows, cache_keys, cache_values, prefix, slopes):
    queries = merged_rows[:, :, 0]
    new_keys = merged_rows[:, :, 1]
    new_values = merged_rows[:, :, 2]
    group_size = merged_rows.shape[0]
    cache_size = cache_keys.shape[0]
    factor = 1.0 / math.sqrt(merged_rows.shape[-1])
    query_pos = prefix + jnp.arange(group_size, dtype=jnp.int32)
    cache_pos = jnp.arange(cache_size, dtype=jnp.int32)
    cache_dist = (query_pos[:, None] - cache_pos[None, :]).astype(jnp.float32)
    new_dist = (query_pos[:, None] - query_pos[None, :]).astype(jnp.float32)
    cache_scores = (
        jnp.einsum("qhd,khd->hqk", queries, cache_keys, preferred_element_type=jnp.float32) * factor
    )
    cache_scores = cache_scores - slopes[:, None, None] * cache_dist[None]
    cache_scores = jnp.where((cache_pos < prefix)[None, None, :], cache_scores, -jnp.inf)
    new_scores = (
        jnp.einsum("qhd,khd->hqk", queries, new_keys, preferred_element_type=jnp.float32) * factor
    )
    new_scores = new_scores - slopes[:, None, None] * new_dist[None]
    causal = (
        jnp.arange(group_size, dtype=jnp.int32)[None, :]
        <= jnp.arange(group_size, dtype=jnp.int32)[:, None]
    )
    new_scores = jnp.where(causal[None], new_scores, -jnp.inf)
    highest = jnp.maximum(
        jnp.max(cache_scores, axis=-1, keepdims=True), jnp.max(new_scores, axis=-1, keepdims=True)
    )
    cache_exp = jnp.exp(cache_scores - highest)
    new_exp = jnp.exp(new_scores - highest)
    denominator = jnp.sum(cache_exp, axis=-1, keepdims=True) + jnp.sum(
        new_exp, axis=-1, keepdims=True
    )
    cache_probs = (cache_exp / denominator).astype(jnp.bfloat16)
    new_probs = (new_exp / denominator).astype(jnp.bfloat16)
    context = jnp.einsum(
        "hqk,khd->qhd", cache_probs, cache_values, preferred_element_type=jnp.float32
    )
    context = context + jnp.einsum(
        "hqk,khd->qhd", new_probs, new_values, preferred_element_type=jnp.float32
    )
    return context.astype(jnp.bfloat16).reshape(group_size, -1)


def _prefill_kernel(prefix_ref, slopes_ref, q_ref, kn_ref, vn_ref, kc_ref, vc_ref, o_ref, *, tq):
    h = pl.program_id(0)
    i = pl.program_id(1)
    prefix = prefix_ref[0]
    slope = slopes_ref[h]
    factor = 1.0 / math.sqrt(q_ref.shape[-1])
    dims = (((1,), (1,)), ((), ()))
    cache_size = kc_ref.shape[0]

    def tile(last, width):
        q = q_ref[...]
        q_tok = last * tq + lax.broadcasted_iota(jnp.int32, (tq, 1), 0)
        q_pos = prefix + q_tok
        c_pos = lax.broadcasted_iota(jnp.int32, (1, cache_size), 1)
        k_tok = lax.broadcasted_iota(jnp.int32, (1, width), 1)
        s_c = lax.dot_general(q, kc_ref[...], dims, preferred_element_type=jnp.float32) * factor
        s_c = s_c - slope * (q_pos - c_pos).astype(jnp.float32)
        s_c = jnp.where(c_pos < prefix, s_c, -jnp.inf)
        s_n = lax.dot_general(q, kn_ref[:width, :], dims, preferred_element_type=jnp.float32) * factor
        s_n = s_n - slope * (q_tok - k_tok).astype(jnp.float32)
        s_n = jnp.where(k_tok <= q_tok, s_n, -jnp.inf)
        m = jnp.maximum(jnp.max(s_c, axis=-1, keepdims=True), jnp.max(s_n, axis=-1, keepdims=True))
        e_c = jnp.exp(s_c - m)
        e_n = jnp.exp(s_n - m)
        l = jnp.sum(e_c, axis=-1, keepdims=True) + jnp.sum(e_n, axis=-1, keepdims=True)
        p_c = (e_c / l).astype(jnp.bfloat16)
        p_n = (e_n / l).astype(jnp.bfloat16)
        ctx = jnp.dot(p_c, vc_ref[...], preferred_element_type=jnp.float32)
        ctx = ctx + jnp.dot(p_n, vn_ref[:width, :], preferred_element_type=jnp.float32)
        o_ref[...] = ctx.astype(o_ref.dtype)

    for last in range(kn_ref.shape[0] // tq):
        pl.when(i == last)(functools.partial(tile, last, (last + 1) * tq))


def prefill_attention_kernel(merged, cache_keys, cache_values, prefix, slopes, head_size, tq=256):
    group = merged.shape[0]
    heads = merged.shape[1] // (3 * head_size)
    cache_size = cache_keys.shape[0]
    col = lambda c: (lambda h, i, *_: (0, h * 3 + c))
    return pl.pallas_call(
        functools.partial(_prefill_kernel, tq=tq),
        out_shape=jax.ShapeDtypeStruct((group, heads * head_size), jnp.bfloat16),
        grid_spec=pltpu.PrefetchScalarGridSpec(
            num_scalar_prefetch=2,
            grid=(heads, group // tq),
            in_specs=[
                pl.BlockSpec((tq, head_size), lambda h, i, *_: (i, h * 3)),
                pl.BlockSpec((group, head_size), col(1)),
                pl.BlockSpec((group, head_size), col(2)),
                pl.BlockSpec((cache_size, head_size), lambda h, i, *_: (0, h)),
                pl.BlockSpec((cache_size, head_size), lambda h, i, *_: (0, h)),
            ],
            out_specs=pl.BlockSpec((tq, head_size), lambda h, i, *_: (i, h)),
        ),
        cost_estimate=pl.CostEstimate(
            flops=4 * heads * group * (group + cache_size) * head_size,
            transcendentals=heads * group * (group + cache_size),
            bytes_accessed=2 * (group * heads * 3 * head_size + 2 * cache_size * heads * head_size + group * heads * head_size),
        ),
    )(prefix, slopes, merged, merged, merged, cache_keys, cache_values)


def decode_attention(query_row, new_key, new_value, cache_keys, cache_values, length, slopes):
    heads, head_size = query_row.shape
    factor = 1.0 / math.sqrt(head_size)
    cache_pos = jnp.arange(cache_keys.shape[0], dtype=jnp.int32)
    distance = (length - cache_pos).astype(jnp.float32)
    head_of_col = jnp.arange(heads * head_size, dtype=jnp.int32) // head_size
    own_head = head_of_col[:, None] == jnp.arange(heads, dtype=jnp.int32)[None, :]
    block_query = jnp.where(own_head, query_row.reshape(-1)[:, None], jnp.zeros((), query_row.dtype))
    cache_scores = jnp.dot(cache_keys, block_query, preferred_element_type=jnp.float32).T * factor
    cache_scores = cache_scores - slopes[:, None] * distance[None, :]
    cache_scores = jnp.where((cache_pos < length)[None, :], cache_scores, -jnp.inf)
    own_score = (
        jnp.einsum("hd,hd->h", query_row, new_key, preferred_element_type=jnp.float32)[:, None]
        * factor
    )
    highest = jnp.maximum(jnp.max(cache_scores, axis=-1, keepdims=True), own_score)
    cache_exp = jnp.exp(cache_scores - highest)
    own_exp = jnp.exp(own_score - highest)
    denominator = jnp.sum(cache_exp, axis=-1, keepdims=True) + own_exp
    cache_probs = (cache_exp / denominator).astype(jnp.bfloat16)
    own_prob = (own_exp / denominator).astype(jnp.bfloat16)
    every_head = jnp.dot(cache_probs, cache_values, preferred_element_type=jnp.float32)
    context = jnp.sum(jnp.where(own_head.T, every_head, 0.0), axis=0).reshape(heads, head_size)
    context = context + own_prob.astype(jnp.float32) * new_value.astype(jnp.float32)
    return context.astype(jnp.bfloat16).reshape(-1)


def per_device(
    pre_hidden,
    dec_hidden,
    norm_gain,
    norm_shift,
    qkv_weight,
    qkv_bias,
    out_weight,
    out_bias,
    pre_keys,
    pre_values,
    dec_keys,
    dec_values,
    prefix_lengths,
    cache_lengths,
    slot_of,
):
    head_size = HD
    local_heads = qkv_weight.shape[1] // (3 * head_size)
    slopes = alibi_slopes(lax.axis_index("tensor") * local_heads, local_heads, H)
    bias_sum = out_bias.astype(jnp.float32)
    normed = normalize(pre_hidden, norm_gain, norm_shift)
    normed, dec_hidden = lax.optimization_barrier((normed, dec_hidden))
    slot_count = dec_hidden.shape[0]
    dp_size = lax.axis_size("dp")
    tensor_size = lax.axis_size("tensor")
    group = lax.axis_index("dp")
    member = lax.axis_index("tensor")
    first_slot = group * slot_count
    shifted_rows = dec_hidden
    step = 1
    while step < dp_size:
        shifted_rows = jnp.concatenate(
            [shifted_rows, lax.ppermute(shifted_rows, "dp", [(i, i ^ step) for i in range(dp_size)])], axis=0
        )
        step *= 2
    slot_ids = first_slot + jnp.arange(slot_count, dtype=jnp.int32)
    request_ids = jnp.arange(slot_of.shape[0], dtype=jnp.int32)
    uses_slot = slot_of[None, :] == slot_ids[:, None]
    request_of_slot = jnp.sum(jnp.where(uses_slot, request_ids[None, :], 0), axis=1)
    arrival = ((request_of_slot // slot_count) ^ group) * slot_count + request_of_slot % slot_count
    pick = (arrival[:, None] == jnp.arange(shifted_rows.shape[0], dtype=jnp.int32)[None, :]).astype(
        jnp.bfloat16
    )
    arrived = jnp.dot(pick, shifted_rows, preferred_element_type=jnp.float32).astype(jnp.bfloat16)
    normed_slots = normalize(arrived, norm_gain, norm_shift)
    merged_slots = (
        jnp.dot(normed_slots, qkv_weight, preferred_element_type=jnp.float32)
        + qkv_bias.astype(jnp.float32)
    ).astype(jnp.bfloat16)
    merged_slots = merged_slots.reshape(slot_count, local_heads, 3, head_size)
    dec_cache = dec_keys.shape[1]
    slot_context = jax.vmap(decode_attention, in_axes=(0, 0, 0, 0, 0, 0, None))(
        merged_slots[:, :, 0],
        merged_slots[:, :, 1],
        merged_slots[:, :, 2],
        dec_keys,
        dec_values,
        cache_lengths,
        slopes,
    )
    slot_partial = jnp.dot(slot_context, out_weight, preferred_element_type=jnp.float32)
    partials = slot_partial
    step = 1
    while step < tensor_size:
        partials = jnp.concatenate(
            [partials, lax.ppermute(partials, "tensor", [(i, i ^ step) for i in range(tensor_size)])], axis=0
        )
        step *= 2
    partials = partials.reshape(tensor_size, slot_count, -1)
    slot_summed = partials[member ^ 0]
    for source in range(1, tensor_size):
        slot_summed = slot_summed + partials[member ^ source]
    slot_rows = (slot_summed + bias_sum + arrived.astype(jnp.float32)).astype(jnp.bfloat16)
    tensor_size = lax.axis_size("tensor")
    chips = tensor_size // 2
    member = lax.axis_index("tensor")
    chip = member // 2
    core = member % 2
    block = pre_hidden.shape[0]

    def route(k, flip):
        return [(i, ((i // 2 + k) % chips) * 2 + ((i % 2) ^ flip)) for i in range(tensor_size)]

    across_tokens = [lax.ppermute(normed, "tensor", route(k, 0)) for k in range(1, chips)]
    across_tokens, held_weight = lax.optimization_barrier((across_tokens, out_weight))
    same_core_tokens = [normed] + list(across_tokens)
    sibling_tokens = [lax.ppermute(t, "tensor", route(0, 1)) for t in same_core_tokens]
    sibling_tokens, slot_rows = lax.optimization_barrier((sibling_tokens, slot_rows))
    across_chips = [lax.ppermute(held_weight, "tensor", route(k, 0)) for k in range(1, chips)]
    members = jnp.arange(tensor_size, dtype=jnp.int32)
    arrival_of = ((members % 2) ^ core) * chips + (chip - members // 2) % chips
    tokens = jnp.take(jnp.stack(list(same_core_tokens) + list(sibling_tokens)), arrival_of, axis=0)
    tokens = tokens.reshape(tensor_size * block, normed.shape[1])
    product = jnp.dot(tokens, qkv_weight, preferred_element_type=jnp.float32)
    merged_rows = (product + qkv_bias.astype(jnp.float32)).astype(jnp.bfloat16)
    returned = slot_rows
    step = 1
    while step < dp_size:
        returned = jnp.concatenate(
            [returned, lax.ppermute(returned, "dp", [(i, i ^ step) for i in range(dp_size)])], axis=0
        )
        step *= 2
    slot_wanted = lax.dynamic_slice_in_dim(slot_of, first_slot, slot_count)
    back = ((slot_wanted // slot_count) ^ group) * slot_count + slot_wanted % slot_count
    take = (back[:, None] == jnp.arange(returned.shape[0], dtype=jnp.int32)[None, :]).astype(jnp.bfloat16)
    dec_output = jnp.dot(take, returned, preferred_element_type=jnp.float32).astype(jnp.bfloat16)
    merged_rows, dec_output = lax.optimization_barrier((merged_rows, dec_output))
    context = prefill_attention_kernel(
        merged_rows, pre_keys[0], pre_values[0], prefix_lengths, slopes, head_size
    )
    context, across_chips = lax.optimization_barrier((context, across_chips))
    same_core = [out_weight] + list(across_chips)
    weight_blocks = same_core + [lax.ppermute(w, "tensor", route(0, 1)) for w in same_core]
    pieces = []
    for flip in (0, 1):
        for k in range(chips):
            if k == 0 and flip == 0:
                pieces.append(lax.dynamic_slice_in_dim(context, member * block, block))
                continue
            target = ((chip + k) % chips) * 2 + (core ^ flip)
            outgoing = lax.dynamic_slice_in_dim(context, target * block, block)
            pieces.append(lax.ppermute(outgoing, "tensor", route(k, flip)))
    summed = jnp.dot(pieces[0], weight_blocks[0], preferred_element_type=jnp.float32)
    for piece, weight in zip(pieces[1:], weight_blocks[1:]):
        summed = summed + jnp.dot(piece, weight, preferred_element_type=jnp.float32)
    pre_output = (summed + bias_sum + pre_hidden.astype(jnp.float32)).astype(jnp.bfloat16)
    return (pre_output, dec_output)


def solution(mesh):
    placed = (
        P(("dp", "tensor"), None),
        P("dp", None),
        P(),
        P(),
        P(None, "tensor"),
        P("tensor"),
        P("tensor", None),
        P(),
        P("dp", None, "tensor"),
        P("dp", None, "tensor"),
        P("dp", None, "tensor"),
        P("dp", None, "tensor"),
        P("dp"),
        P("dp"),
        P(),
    )
    return jax.shard_map(
        per_device,
        mesh=mesh,
        in_specs=placed,
        out_specs=(P(("dp", "tensor"), None), P("dp", None)),
        check_vma=False,
    )
```

```python
import math

import jax
import jax.numpy as jnp
from jax import lax
from jax.sharding import PartitionSpec as P
from jax.experimental import pallas as pl
from jax.experimental.pallas import tpu as pltpu
import functools

H = 16
HD = 128


EPSILON = 1e-05


def normalize(values, norm_gain, norm_shift):
    values = values.astype(jnp.float32)
    center = values - jnp.mean(values, axis=-1, keepdims=True)
    spread = jnp.mean(center * center, axis=-1, keepdims=True)
    scaled = center * lax.rsqrt(spread + EPSILON)
    return (scaled * norm_gain.astype(jnp.float32) + norm_shift.astype(jnp.float32)).astype(
        jnp.bfloat16
    )


def alibi_slopes(first_head, head_count, total_heads):
    head_ids = (first_head + jnp.arange(head_count, dtype=jnp.int32)).astype(jnp.float32)
    return jnp.exp2(-8.0 * (head_ids + 1.0) / total_heads)


def prefill_attention(merged_rows, cache_keys, cache_values, prefix, slopes):
    queries = merged_rows[:, :, 0]
    new_keys = merged_rows[:, :, 1]
    new_values = merged_rows[:, :, 2]
    group_size = merged_rows.shape[0]
    cache_size = cache_keys.shape[0]
    factor = 1.0 / math.sqrt(merged_rows.shape[-1])
    query_pos = prefix + jnp.arange(group_size, dtype=jnp.int32)
    cache_pos = jnp.arange(cache_size, dtype=jnp.int32)
    cache_dist = (query_pos[:, None] - cache_pos[None, :]).astype(jnp.float32)
    new_dist = (query_pos[:, None] - query_pos[None, :]).astype(jnp.float32)
    cache_scores = (
        jnp.einsum("qhd,khd->hqk", queries, cache_keys, preferred_element_type=jnp.float32) * factor
    )
    cache_scores = cache_scores - slopes[:, None, None] * cache_dist[None]
    cache_scores = jnp.where((cache_pos < prefix)[None, None, :], cache_scores, -jnp.inf)
    new_scores = (
        jnp.einsum("qhd,khd->hqk", queries, new_keys, preferred_element_type=jnp.float32) * factor
    )
    new_scores = new_scores - slopes[:, None, None] * new_dist[None]
    causal = (
        jnp.arange(group_size, dtype=jnp.int32)[None, :]
        <= jnp.arange(group_size, dtype=jnp.int32)[:, None]
    )
    new_scores = jnp.where(causal[None], new_scores, -jnp.inf)
    highest = jnp.maximum(
        jnp.max(cache_scores, axis=-1, keepdims=True), jnp.max(new_scores, axis=-1, keepdims=True)
    )
    cache_exp = jnp.exp(cache_scores - highest)
    new_exp = jnp.exp(new_scores - highest)
    denominator = jnp.sum(cache_exp, axis=-1, keepdims=True) + jnp.sum(
        new_exp, axis=-1, keepdims=True
    )
    cache_probs = (cache_exp / denominator).astype(jnp.bfloat16)
    new_probs = (new_exp / denominator).astype(jnp.bfloat16)
    context = jnp.einsum(
        "hqk,khd->qhd", cache_probs, cache_values, preferred_element_type=jnp.float32
    )
    context = context + jnp.einsum(
        "hqk,khd->qhd", new_probs, new_values, preferred_element_type=jnp.float32
    )
    return context.astype(jnp.bfloat16).reshape(group_size, -1)


def _prefill_kernel(prefix_ref, slopes_ref, q_ref, kn_ref, vn_ref, kc_ref, vc_ref, o_ref, *, tq):
    h = pl.program_id(0)
    i = pl.program_id(1)
    prefix = prefix_ref[0]
    slope = slopes_ref[h]
    factor = 1.0 / math.sqrt(q_ref.shape[-1])
    dims = (((1,), (1,)), ((), ()))
    cache_size = kc_ref.shape[0]

    def tile(last, width):
        q = q_ref[...]
        q_tok = last * tq + lax.broadcasted_iota(jnp.int32, (tq, 1), 0)
        q_pos = prefix + q_tok
        c_pos = lax.broadcasted_iota(jnp.int32, (1, cache_size), 1)
        k_tok = lax.broadcasted_iota(jnp.int32, (1, width), 1)
        s_c = lax.dot_general(q, kc_ref[...], dims, preferred_element_type=jnp.float32) * factor
        s_c = s_c - slope * (q_pos - c_pos).astype(jnp.float32)
        s_c = jnp.where(c_pos < prefix, s_c, -jnp.inf)
        s_n = lax.dot_general(q, kn_ref[:width, :], dims, preferred_element_type=jnp.float32) * factor
        s_n = s_n - slope * (q_tok - k_tok).astype(jnp.float32)
        s_n = jnp.where(k_tok <= q_tok, s_n, -jnp.inf)
        m = jnp.maximum(jnp.max(s_c, axis=-1, keepdims=True), jnp.max(s_n, axis=-1, keepdims=True))
        e_c = jnp.exp(s_c - m)
        e_n = jnp.exp(s_n - m)
        l = jnp.sum(e_c, axis=-1, keepdims=True) + jnp.sum(e_n, axis=-1, keepdims=True)
        p_c = (e_c / l).astype(jnp.bfloat16)
        p_n = (e_n / l).astype(jnp.bfloat16)
        ctx = jnp.dot(p_c, vc_ref[...], preferred_element_type=jnp.float32)
        ctx = ctx + jnp.dot(p_n, vn_ref[:width, :], preferred_element_type=jnp.float32)
        o_ref[...] = ctx.astype(o_ref.dtype)

    for last in range(kn_ref.shape[0] // tq):
        pl.when(i == last)(functools.partial(tile, last, (last + 1) * tq))


def prefill_attention_kernel(merged, cache_keys, cache_values, prefix, slopes, head_size, tq=256):
    group = merged.shape[0]
    heads = merged.shape[1] // (3 * head_size)
    cache_size = cache_keys.shape[0]
    col = lambda c: (lambda h, i, *_: (0, h * 3 + c))
    return pl.pallas_call(
        functools.partial(_prefill_kernel, tq=tq),
        out_shape=jax.ShapeDtypeStruct((group, heads * head_size), jnp.bfloat16),
        grid_spec=pltpu.PrefetchScalarGridSpec(
            num_scalar_prefetch=2,
            grid=(heads, group // tq),
            in_specs=[
                pl.BlockSpec((tq, head_size), lambda h, i, *_: (i, h * 3)),
                pl.BlockSpec((group, head_size), col(1)),
                pl.BlockSpec((group, head_size), col(2)),
                pl.BlockSpec((cache_size, head_size), lambda h, i, *_: (0, h)),
                pl.BlockSpec((cache_size, head_size), lambda h, i, *_: (0, h)),
            ],
            out_specs=pl.BlockSpec((tq, head_size), lambda h, i, *_: (i, h)),
        ),
        cost_estimate=pl.CostEstimate(
            flops=4 * heads * group * (group + cache_size) * head_size,
            transcendentals=heads * group * (group + cache_size),
            bytes_accessed=2 * (group * heads * 3 * head_size + 2 * cache_size * heads * head_size + group * heads * head_size),
        ),
    )(prefix, slopes, merged, merged, merged, cache_keys, cache_values)


def decode_attention(query_row, new_key, new_value, cache_keys, cache_values, length, slopes):
    heads, head_size = query_row.shape
    factor = 1.0 / math.sqrt(head_size)
    cache_pos = jnp.arange(cache_keys.shape[0], dtype=jnp.int32)
    distance = (length - cache_pos).astype(jnp.float32)
    head_of_col = jnp.arange(heads * head_size, dtype=jnp.int32) // head_size
    own_head = head_of_col[:, None] == jnp.arange(heads, dtype=jnp.int32)[None, :]
    block_query = jnp.where(own_head, query_row.reshape(-1)[:, None], jnp.zeros((), query_row.dtype))
    cache_scores = jnp.dot(cache_keys, block_query, preferred_element_type=jnp.float32).T * factor
    cache_scores = cache_scores - slopes[:, None] * distance[None, :]
    cache_scores = jnp.where((cache_pos < length)[None, :], cache_scores, -jnp.inf)
    own_score = (
        jnp.einsum("hd,hd->h", query_row, new_key, preferred_element_type=jnp.float32)[:, None]
        * factor
    )
    highest = jnp.maximum(jnp.max(cache_scores, axis=-1, keepdims=True), own_score)
    cache_exp = jnp.exp(cache_scores - highest)
    own_exp = jnp.exp(own_score - highest)
    denominator = jnp.sum(cache_exp, axis=-1, keepdims=True) + own_exp
    cache_probs = (cache_exp / denominator).astype(jnp.bfloat16)
    own_prob = (own_exp / denominator).astype(jnp.bfloat16)
    every_head = jnp.dot(cache_probs, cache_values, preferred_element_type=jnp.float32)
    context = jnp.sum(jnp.where(own_head.T, every_head, 0.0), axis=0).reshape(heads, head_size)
    context = context + own_prob.astype(jnp.float32) * new_value.astype(jnp.float32)
    return context.astype(jnp.bfloat16).reshape(-1)


def per_device(
    pre_hidden,
    dec_hidden,
    norm_gain,
    norm_shift,
    qkv_weight,
    qkv_bias,
    out_weight,
    out_bias,
    pre_keys,
    pre_values,
    dec_keys,
    dec_values,
    prefix_lengths,
    cache_lengths,
    slot_of,
):
    head_size = HD
    local_heads = qkv_weight.shape[1] // (3 * head_size)
    slopes = alibi_slopes(lax.axis_index("tensor") * local_heads, local_heads, H)
    bias_sum = out_bias.astype(jnp.float32)
    normed = normalize(pre_hidden, norm_gain, norm_shift)
    normed, dec_hidden = lax.optimization_barrier((normed, dec_hidden))
    slot_count = dec_hidden.shape[0]
    dp_size = lax.axis_size("dp")
    tensor_size = lax.axis_size("tensor")
    group = lax.axis_index("dp")
    member = lax.axis_index("tensor")
    first_slot = group * slot_count
    shifted_rows = dec_hidden
    step = 1
    while step < dp_size:
        shifted_rows = jnp.concatenate(
            [shifted_rows, lax.ppermute(shifted_rows, "dp", [(i, i ^ step) for i in range(dp_size)])], axis=0
        )
        step *= 2
    slot_ids = first_slot + jnp.arange(slot_count, dtype=jnp.int32)
    request_ids = jnp.arange(slot_of.shape[0], dtype=jnp.int32)
    uses_slot = slot_of[None, :] == slot_ids[:, None]
    request_of_slot = jnp.sum(jnp.where(uses_slot, request_ids[None, :], 0), axis=1)
    arrival = ((request_of_slot // slot_count) ^ group) * slot_count + request_of_slot % slot_count
    pick = (arrival[:, None] == jnp.arange(shifted_rows.shape[0], dtype=jnp.int32)[None, :]).astype(
        jnp.bfloat16
    )
    arrived = jnp.dot(pick, shifted_rows, preferred_element_type=jnp.float32).astype(jnp.bfloat16)
    normed_slots = normalize(arrived, norm_gain, norm_shift)
    merged_slots = (
        jnp.dot(normed_slots, qkv_weight, preferred_element_type=jnp.float32)
        + qkv_bias.astype(jnp.float32)
    ).astype(jnp.bfloat16)
    merged_slots = merged_slots.reshape(slot_count, local_heads, 3, head_size)
    dec_cache = dec_keys.shape[1]
    slot_context = jax.vmap(decode_attention, in_axes=(0, 0, 0, 0, 0, 0, None))(
        merged_slots[:, :, 0],
        merged_slots[:, :, 1],
        merged_slots[:, :, 2],
        dec_keys,
        dec_values,
        cache_lengths,
        slopes,
    )
    slot_partial = jnp.dot(slot_context, out_weight, preferred_element_type=jnp.float32)
    partials = slot_partial
    step = 1
    while step < tensor_size:
        partials = jnp.concatenate(
            [partials, lax.ppermute(partials, "tensor", [(i, i ^ step) for i in range(tensor_size)])], axis=0
        )
        step *= 2
    partials = partials.reshape(tensor_size, slot_count, -1)
    slot_summed = partials[member ^ 0]
    for source in range(1, tensor_size):
        slot_summed = slot_summed + partials[member ^ source]
    slot_rows = (slot_summed + bias_sum + arrived.astype(jnp.float32)).astype(jnp.bfloat16)
    tensor_size = lax.axis_size("tensor")
    chips = tensor_size // 2
    member = lax.axis_index("tensor")
    chip = member // 2
    core = member % 2
    block = pre_hidden.shape[0]

    def route(k, flip):
        return [(i, ((i // 2 + k) % chips) * 2 + ((i % 2) ^ flip)) for i in range(tensor_size)]

    across_tokens = [lax.ppermute(normed, "tensor", route(k, 0)) for k in range(1, chips)]
    across_tokens, held_weight = lax.optimization_barrier((across_tokens, out_weight))
    same_core_tokens = [normed] + list(across_tokens)
    sibling_tokens = [lax.ppermute(t, "tensor", route(0, 1)) for t in same_core_tokens]
    sibling_tokens, slot_rows = lax.optimization_barrier((sibling_tokens, slot_rows))
    across_chips = [lax.ppermute(held_weight, "tensor", route(k, 0)) for k in range(1, chips)]
    bias_row = qkv_bias.astype(jnp.float32)
    merged_rows = jnp.zeros((tensor_size * block, qkv_weight.shape[1]), jnp.bfloat16)
    for flip, token_blocks in ((0, same_core_tokens), (1, sibling_tokens)):
        for k, token_block in enumerate(token_blocks):
            source = ((chip - k) % chips) * 2 + (core ^ flip)
            projected = (
                jnp.dot(token_block, qkv_weight, preferred_element_type=jnp.float32) + bias_row
            ).astype(jnp.bfloat16)
            merged_rows = lax.dynamic_update_slice_in_dim(merged_rows, projected, source * block, 0)
    returned = slot_rows
    step = 1
    while step < dp_size:
        returned = jnp.concatenate(
            [returned, lax.ppermute(returned, "dp", [(i, i ^ step) for i in range(dp_size)])], axis=0
        )
        step *= 2
    slot_wanted = lax.dynamic_slice_in_dim(slot_of, first_slot, slot_count)
    back = ((slot_wanted // slot_count) ^ group) * slot_count + slot_wanted % slot_count
    take = (back[:, None] == jnp.arange(returned.shape[0], dtype=jnp.int32)[None, :]).astype(jnp.bfloat16)
    dec_output = jnp.dot(take, returned, preferred_element_type=jnp.float32).astype(jnp.bfloat16)
    merged_rows, dec_output = lax.optimization_barrier((merged_rows, dec_output))
    context = prefill_attention_kernel(
        merged_rows, pre_keys[0], pre_values[0], prefix_lengths, slopes, head_size
    )
    context, across_chips = lax.optimization_barrier((context, across_chips))
    same_core = [out_weight] + list(across_chips)
    weight_blocks = same_core + [lax.ppermute(w, "tensor", route(0, 1)) for w in same_core]
    pieces = []
    for flip in (0, 1):
        for k in range(chips):
            if k == 0 and flip == 0:
                pieces.append(lax.dynamic_slice_in_dim(context, member * block, block))
                continue
            target = ((chip + k) % chips) * 2 + (core ^ flip)
            outgoing = lax.dynamic_slice_in_dim(context, target * block, block)
            pieces.append(lax.ppermute(outgoing, "tensor", route(k, flip)))
    summed = jnp.dot(pieces[0], weight_blocks[0], preferred_element_type=jnp.float32)
    for piece, weight in zip(pieces[1:], weight_blocks[1:]):
        summed = summed + jnp.dot(piece, weight, preferred_element_type=jnp.float32)
    pre_output = (summed + bias_sum + pre_hidden.astype(jnp.float32)).astype(jnp.bfloat16)
    return (pre_output, dec_output)


def solution(mesh):
    placed = (
        P(("dp", "tensor"), None),
        P("dp", None),
        P(),
        P(),
        P(None, "tensor"),
        P("tensor"),
        P("tensor", None),
        P(),
        P("dp", None, "tensor"),
        P("dp", None, "tensor"),
        P("dp", None, "tensor"),
        P("dp", None, "tensor"),
        P("dp"),
        P("dp"),
        P(),
    )
    return jax.shard_map(
        per_device,
        mesh=mesh,
        in_specs=placed,
        out_specs=(P(("dp", "tensor"), None), P("dp", None)),
        check_vma=False,
    )
```

```python
import math

import jax
import jax.numpy as jnp
from jax import lax
from jax.sharding import PartitionSpec as P
from jax.experimental import pallas as pl
from jax.experimental.pallas import tpu as pltpu
import functools

H = 16
HD = 128


EPSILON = 1e-05


def normalize(values, norm_gain, norm_shift):
    values = values.astype(jnp.float32)
    center = values - jnp.mean(values, axis=-1, keepdims=True)
    spread = jnp.mean(center * center, axis=-1, keepdims=True)
    scaled = center * lax.rsqrt(spread + EPSILON)
    return (scaled * norm_gain.astype(jnp.float32) + norm_shift.astype(jnp.float32)).astype(
        jnp.bfloat16
    )


def alibi_slopes(first_head, head_count, total_heads):
    head_ids = (first_head + jnp.arange(head_count, dtype=jnp.int32)).astype(jnp.float32)
    return jnp.exp2(-8.0 * (head_ids + 1.0) / total_heads)


def prefill_attention(merged_rows, cache_keys, cache_values, prefix, slopes):
    queries = merged_rows[:, :, 0]
    new_keys = merged_rows[:, :, 1]
    new_values = merged_rows[:, :, 2]
    group_size = merged_rows.shape[0]
    cache_size = cache_keys.shape[0]
    factor = 1.0 / math.sqrt(merged_rows.shape[-1])
    query_pos = prefix + jnp.arange(group_size, dtype=jnp.int32)
    cache_pos = jnp.arange(cache_size, dtype=jnp.int32)
    cache_dist = (query_pos[:, None] - cache_pos[None, :]).astype(jnp.float32)
    new_dist = (query_pos[:, None] - query_pos[None, :]).astype(jnp.float32)
    cache_scores = (
        jnp.einsum("qhd,khd->hqk", queries, cache_keys, preferred_element_type=jnp.float32) * factor
    )
    cache_scores = cache_scores - slopes[:, None, None] * cache_dist[None]
    cache_scores = jnp.where((cache_pos < prefix)[None, None, :], cache_scores, -jnp.inf)
    new_scores = (
        jnp.einsum("qhd,khd->hqk", queries, new_keys, preferred_element_type=jnp.float32) * factor
    )
    new_scores = new_scores - slopes[:, None, None] * new_dist[None]
    causal = (
        jnp.arange(group_size, dtype=jnp.int32)[None, :]
        <= jnp.arange(group_size, dtype=jnp.int32)[:, None]
    )
    new_scores = jnp.where(causal[None], new_scores, -jnp.inf)
    highest = jnp.maximum(
        jnp.max(cache_scores, axis=-1, keepdims=True), jnp.max(new_scores, axis=-1, keepdims=True)
    )
    cache_exp = jnp.exp(cache_scores - highest)
    new_exp = jnp.exp(new_scores - highest)
    denominator = jnp.sum(cache_exp, axis=-1, keepdims=True) + jnp.sum(
        new_exp, axis=-1, keepdims=True
    )
    cache_probs = (cache_exp / denominator).astype(jnp.bfloat16)
    new_probs = (new_exp / denominator).astype(jnp.bfloat16)
    context = jnp.einsum(
        "hqk,khd->qhd", cache_probs, cache_values, preferred_element_type=jnp.float32
    )
    context = context + jnp.einsum(
        "hqk,khd->qhd", new_probs, new_values, preferred_element_type=jnp.float32
    )
    return context.astype(jnp.bfloat16).reshape(group_size, -1)


def _prefill_kernel(prefix_ref, slopes_ref, q_ref, kn_ref, vn_ref, kc_ref, vc_ref, o_ref, *, tq):
    h = pl.program_id(0)
    i = pl.program_id(1)
    prefix = prefix_ref[0]
    slope = slopes_ref[h]
    factor = 1.0 / math.sqrt(q_ref.shape[-1])
    dims = (((1,), (1,)), ((), ()))
    cache_size = kc_ref.shape[0]

    def tile(last, width):
        q = q_ref[...]
        q_tok = last * tq + lax.broadcasted_iota(jnp.int32, (tq, 1), 0)
        q_pos = prefix + q_tok
        c_pos = lax.broadcasted_iota(jnp.int32, (1, cache_size), 1)
        k_tok = lax.broadcasted_iota(jnp.int32, (1, width), 1)
        s_c = lax.dot_general(q, kc_ref[...], dims, preferred_element_type=jnp.float32) * factor
        s_c = s_c - slope * (q_pos - c_pos).astype(jnp.float32)
        s_c = jnp.where(c_pos < prefix, s_c, -jnp.inf)
        s_n = lax.dot_general(q, kn_ref[:width, :], dims, preferred_element_type=jnp.float32) * factor
        s_n = s_n - slope * (q_tok - k_tok).astype(jnp.float32)
        s_n = jnp.where(k_tok <= q_tok, s_n, -jnp.inf)
        m = jnp.maximum(jnp.max(s_c, axis=-1, keepdims=True), jnp.max(s_n, axis=-1, keepdims=True))
        e_c = jnp.exp(s_c - m)
        e_n = jnp.exp(s_n - m)
        l = jnp.sum(e_c, axis=-1, keepdims=True) + jnp.sum(e_n, axis=-1, keepdims=True)
        inverse = 1.0 / l
        p_c = (e_c * inverse).astype(jnp.bfloat16)
        p_n = (e_n * inverse).astype(jnp.bfloat16)
        ctx = jnp.dot(p_c, vc_ref[...], preferred_element_type=jnp.float32)
        ctx = ctx + jnp.dot(p_n, vn_ref[:width, :], preferred_element_type=jnp.float32)
        o_ref[...] = ctx.astype(o_ref.dtype)

    for last in range(kn_ref.shape[0] // tq):
        pl.when(i == last)(functools.partial(tile, last, (last + 1) * tq))


def prefill_attention_kernel(merged, cache_keys, cache_values, prefix, slopes, head_size, tq=256):
    group = merged.shape[0]
    heads = merged.shape[1] // (3 * head_size)
    cache_size = cache_keys.shape[0]
    col = lambda c: (lambda h, i, *_: (0, h * 3 + c))
    return pl.pallas_call(
        functools.partial(_prefill_kernel, tq=tq),
        out_shape=jax.ShapeDtypeStruct((group, heads * head_size), jnp.bfloat16),
        grid_spec=pltpu.PrefetchScalarGridSpec(
            num_scalar_prefetch=2,
            grid=(heads, group // tq),
            in_specs=[
                pl.BlockSpec((tq, head_size), lambda h, i, *_: (i, h * 3)),
                pl.BlockSpec((group, head_size), col(1)),
                pl.BlockSpec((group, head_size), col(2)),
                pl.BlockSpec((cache_size, head_size), lambda h, i, *_: (0, h)),
                pl.BlockSpec((cache_size, head_size), lambda h, i, *_: (0, h)),
            ],
            out_specs=pl.BlockSpec((tq, head_size), lambda h, i, *_: (i, h)),
        ),
        cost_estimate=pl.CostEstimate(
            flops=4 * heads * group * (group + cache_size) * head_size,
            transcendentals=heads * group * (group + cache_size),
            bytes_accessed=2 * (group * heads * 3 * head_size + 2 * cache_size * heads * head_size + group * heads * head_size),
        ),
    )(prefix, slopes, merged, merged, merged, cache_keys, cache_values)


def decode_attention(query_row, new_key, new_value, cache_keys, cache_values, length, slopes):
    heads, head_size = query_row.shape
    factor = 1.0 / math.sqrt(head_size)
    cache_pos = jnp.arange(cache_keys.shape[0], dtype=jnp.int32)
    distance = (length - cache_pos).astype(jnp.float32)
    head_of_col = jnp.arange(heads * head_size, dtype=jnp.int32) // head_size
    own_head = head_of_col[:, None] == jnp.arange(heads, dtype=jnp.int32)[None, :]
    block_query = jnp.where(own_head, query_row.reshape(-1)[:, None], jnp.zeros((), query_row.dtype))
    cache_scores = jnp.dot(cache_keys, block_query, preferred_element_type=jnp.float32).T * factor
    cache_scores = cache_scores - slopes[:, None] * distance[None, :]
    cache_scores = jnp.where((cache_pos < length)[None, :], cache_scores, -jnp.inf)
    own_score = (
        jnp.einsum("hd,hd->h", query_row, new_key, preferred_element_type=jnp.float32)[:, None]
        * factor
    )
    highest = jnp.maximum(jnp.max(cache_scores, axis=-1, keepdims=True), own_score)
    cache_exp = jnp.exp(cache_scores - highest)
    own_exp = jnp.exp(own_score - highest)
    denominator = jnp.sum(cache_exp, axis=-1, keepdims=True) + own_exp
    cache_probs = (cache_exp / denominator).astype(jnp.bfloat16)
    own_prob = (own_exp / denominator).astype(jnp.bfloat16)
    every_head = jnp.dot(cache_probs, cache_values, preferred_element_type=jnp.float32)
    context = jnp.sum(jnp.where(own_head.T, every_head, 0.0), axis=0).reshape(heads, head_size)
    context = context + own_prob.astype(jnp.float32) * new_value.astype(jnp.float32)
    return context.astype(jnp.bfloat16).reshape(-1)


def per_device(
    pre_hidden,
    dec_hidden,
    norm_gain,
    norm_shift,
    qkv_weight,
    qkv_bias,
    out_weight,
    out_bias,
    pre_keys,
    pre_values,
    dec_keys,
    dec_values,
    prefix_lengths,
    cache_lengths,
    slot_of,
):
    head_size = HD
    local_heads = qkv_weight.shape[1] // (3 * head_size)
    slopes = alibi_slopes(lax.axis_index("tensor") * local_heads, local_heads, H)
    bias_sum = out_bias.astype(jnp.float32)
    normed = normalize(pre_hidden, norm_gain, norm_shift)
    normed, dec_hidden = lax.optimization_barrier((normed, dec_hidden))
    slot_count = dec_hidden.shape[0]
    dp_size = lax.axis_size("dp")
    tensor_size = lax.axis_size("tensor")
    group = lax.axis_index("dp")
    member = lax.axis_index("tensor")
    first_slot = group * slot_count
    shifted_rows = dec_hidden
    step = 1
    while step < dp_size:
        shifted_rows = jnp.concatenate(
            [shifted_rows, lax.ppermute(shifted_rows, "dp", [(i, i ^ step) for i in range(dp_size)])], axis=0
        )
        step *= 2
    slot_ids = first_slot + jnp.arange(slot_count, dtype=jnp.int32)
    request_ids = jnp.arange(slot_of.shape[0], dtype=jnp.int32)
    uses_slot = slot_of[None, :] == slot_ids[:, None]
    request_of_slot = jnp.sum(jnp.where(uses_slot, request_ids[None, :], 0), axis=1)
    arrival = ((request_of_slot // slot_count) ^ group) * slot_count + request_of_slot % slot_count
    pick = (arrival[:, None] == jnp.arange(shifted_rows.shape[0], dtype=jnp.int32)[None, :]).astype(
        jnp.bfloat16
    )
    arrived = jnp.dot(pick, shifted_rows, preferred_element_type=jnp.float32).astype(jnp.bfloat16)
    normed_slots = normalize(arrived, norm_gain, norm_shift)
    merged_slots = (
        jnp.dot(normed_slots, qkv_weight, preferred_element_type=jnp.float32)
        + qkv_bias.astype(jnp.float32)
    ).astype(jnp.bfloat16)
    merged_slots = merged_slots.reshape(slot_count, local_heads, 3, head_size)
    dec_cache = dec_keys.shape[1]
    slot_context = jax.vmap(decode_attention, in_axes=(0, 0, 0, 0, 0, 0, None))(
        merged_slots[:, :, 0],
        merged_slots[:, :, 1],
        merged_slots[:, :, 2],
        dec_keys,
        dec_values,
        cache_lengths,
        slopes,
    )
    slot_partial = jnp.dot(slot_context, out_weight, preferred_element_type=jnp.float32)
    partials = slot_partial
    step = 1
    while step < tensor_size:
        partials = jnp.concatenate(
            [partials, lax.ppermute(partials, "tensor", [(i, i ^ step) for i in range(tensor_size)])], axis=0
        )
        step *= 2
    partials = partials.reshape(tensor_size, slot_count, -1)
    slot_summed = partials[member ^ 0]
    for source in range(1, tensor_size):
        slot_summed = slot_summed + partials[member ^ source]
    slot_rows = (slot_summed + bias_sum + arrived.astype(jnp.float32)).astype(jnp.bfloat16)
    tensor_size = lax.axis_size("tensor")
    chips = tensor_size // 2
    member = lax.axis_index("tensor")
    chip = member // 2
    core = member % 2
    block = pre_hidden.shape[0]

    def route(k, flip):
        return [(i, ((i // 2 + k) % chips) * 2 + ((i % 2) ^ flip)) for i in range(tensor_size)]

    across_tokens = [lax.ppermute(normed, "tensor", route(k, 0)) for k in range(1, chips)]
    across_tokens, held_weight = lax.optimization_barrier((across_tokens, out_weight))
    same_core_tokens = [normed] + list(across_tokens)
    sibling_tokens = [lax.ppermute(t, "tensor", route(0, 1)) for t in same_core_tokens]
    sibling_tokens, slot_rows = lax.optimization_barrier((sibling_tokens, slot_rows))
    across_chips = [lax.ppermute(held_weight, "tensor", route(k, 0)) for k in range(1, chips)]
    bias_row = qkv_bias.astype(jnp.float32)
    merged_rows = jnp.zeros((tensor_size * block, qkv_weight.shape[1]), jnp.bfloat16)
    for flip, token_blocks in ((0, same_core_tokens), (1, sibling_tokens)):
        for k, token_block in enumerate(token_blocks):
            source = ((chip - k) % chips) * 2 + (core ^ flip)
            projected = (
                jnp.dot(token_block, qkv_weight, preferred_element_type=jnp.float32) + bias_row
            ).astype(jnp.bfloat16)
            merged_rows = lax.dynamic_update_slice_in_dim(merged_rows, projected, source * block, 0)
    returned = slot_rows
    step = 1
    while step < dp_size:
        returned = jnp.concatenate(
            [returned, lax.ppermute(returned, "dp", [(i, i ^ step) for i in range(dp_size)])], axis=0
        )
        step *= 2
    slot_wanted = lax.dynamic_slice_in_dim(slot_of, first_slot, slot_count)
    back = ((slot_wanted // slot_count) ^ group) * slot_count + slot_wanted % slot_count
    take = (back[:, None] == jnp.arange(returned.shape[0], dtype=jnp.int32)[None, :]).astype(jnp.bfloat16)
    dec_output = jnp.dot(take, returned, preferred_element_type=jnp.float32).astype(jnp.bfloat16)
    merged_rows, dec_output = lax.optimization_barrier((merged_rows, dec_output))
    context = prefill_attention_kernel(
        merged_rows, pre_keys[0], pre_values[0], prefix_lengths, slopes, head_size
    )
    context, across_chips = lax.optimization_barrier((context, across_chips))
    same_core = [out_weight] + list(across_chips)
    weight_blocks = same_core + [lax.ppermute(w, "tensor", route(0, 1)) for w in same_core]
    pieces = []
    for flip in (0, 1):
        for k in range(chips):
            if k == 0 and flip == 0:
                pieces.append(lax.dynamic_slice_in_dim(context, member * block, block))
                continue
            target = ((chip + k) % chips) * 2 + (core ^ flip)
            outgoing = lax.dynamic_slice_in_dim(context, target * block, block)
            pieces.append(lax.ppermute(outgoing, "tensor", route(k, flip)))
    summed = jnp.dot(pieces[0], weight_blocks[0], preferred_element_type=jnp.float32)
    for piece, weight in zip(pieces[1:], weight_blocks[1:]):
        summed = summed + jnp.dot(piece, weight, preferred_element_type=jnp.float32)
    pre_output = (summed + bias_sum + pre_hidden.astype(jnp.float32)).astype(jnp.bfloat16)
    return (pre_output, dec_output)


def solution(mesh):
    placed = (
        P(("dp", "tensor"), None),
        P("dp", None),
        P(),
        P(),
        P(None, "tensor"),
        P("tensor"),
        P("tensor", None),
        P(),
        P("dp", None, "tensor"),
        P("dp", None, "tensor"),
        P("dp", None, "tensor"),
        P("dp", None, "tensor"),
        P("dp"),
        P("dp"),
        P(),
    )
    return jax.shard_map(
        per_device,
        mesh=mesh,
        in_specs=placed,
        out_specs=(P(("dp", "tensor"), None), P("dp", None)),
        check_vma=False,
    )
```

```python
import math

import jax
import jax.numpy as jnp
from jax import lax
from jax.sharding import PartitionSpec as P
from jax.experimental import pallas as pl
from jax.experimental.pallas import tpu as pltpu
import functools

H = 16
HD = 128


EPSILON = 1e-05


def normalize(values, norm_gain, norm_shift):
    values = values.astype(jnp.float32)
    center = values - jnp.mean(values, axis=-1, keepdims=True)
    spread = jnp.mean(center * center, axis=-1, keepdims=True)
    scaled = center * lax.rsqrt(spread + EPSILON)
    return (scaled * norm_gain.astype(jnp.float32) + norm_shift.astype(jnp.float32)).astype(
        jnp.bfloat16
    )


def alibi_slopes(first_head, head_count, total_heads):
    head_ids = (first_head + jnp.arange(head_count, dtype=jnp.int32)).astype(jnp.float32)
    return jnp.exp2(-8.0 * (head_ids + 1.0) / total_heads)


def prefill_attention(merged_rows, cache_keys, cache_values, prefix, slopes):
    queries = merged_rows[:, :, 0]
    new_keys = merged_rows[:, :, 1]
    new_values = merged_rows[:, :, 2]
    group_size = merged_rows.shape[0]
    cache_size = cache_keys.shape[0]
    factor = 1.0 / math.sqrt(merged_rows.shape[-1])
    query_pos = prefix + jnp.arange(group_size, dtype=jnp.int32)
    cache_pos = jnp.arange(cache_size, dtype=jnp.int32)
    cache_dist = (query_pos[:, None] - cache_pos[None, :]).astype(jnp.float32)
    new_dist = (query_pos[:, None] - query_pos[None, :]).astype(jnp.float32)
    cache_scores = (
        jnp.einsum("qhd,khd->hqk", queries, cache_keys, preferred_element_type=jnp.float32) * factor
    )
    cache_scores = cache_scores - slopes[:, None, None] * cache_dist[None]
    cache_scores = jnp.where((cache_pos < prefix)[None, None, :], cache_scores, -jnp.inf)
    new_scores = (
        jnp.einsum("qhd,khd->hqk", queries, new_keys, preferred_element_type=jnp.float32) * factor
    )
    new_scores = new_scores - slopes[:, None, None] * new_dist[None]
    causal = (
        jnp.arange(group_size, dtype=jnp.int32)[None, :]
        <= jnp.arange(group_size, dtype=jnp.int32)[:, None]
    )
    new_scores = jnp.where(causal[None], new_scores, -jnp.inf)
    highest = jnp.maximum(
        jnp.max(cache_scores, axis=-1, keepdims=True), jnp.max(new_scores, axis=-1, keepdims=True)
    )
    cache_exp = jnp.exp(cache_scores - highest)
    new_exp = jnp.exp(new_scores - highest)
    denominator = jnp.sum(cache_exp, axis=-1, keepdims=True) + jnp.sum(
        new_exp, axis=-1, keepdims=True
    )
    cache_probs = (cache_exp / denominator).astype(jnp.bfloat16)
    new_probs = (new_exp / denominator).astype(jnp.bfloat16)
    context = jnp.einsum(
        "hqk,khd->qhd", cache_probs, cache_values, preferred_element_type=jnp.float32
    )
    context = context + jnp.einsum(
        "hqk,khd->qhd", new_probs, new_values, preferred_element_type=jnp.float32
    )
    return context.astype(jnp.bfloat16).reshape(group_size, -1)


def _prefill_kernel(prefix_ref, slopes_ref, q_ref, kn_ref, vn_ref, kc_ref, vc_ref, o_ref, *, tq):
    h = pl.program_id(0)
    i = pl.program_id(1)
    prefix = prefix_ref[0]
    slope = slopes_ref[h]
    factor = 1.0 / math.sqrt(q_ref.shape[-1])
    dims = (((1,), (1,)), ((), ()))
    cache_size = kc_ref.shape[0]

    def tile(last, width):
        q = q_ref[...]
        q_tok = last * tq + lax.broadcasted_iota(jnp.int32, (tq, 1), 0)
        q_pos = prefix + q_tok
        c_pos = lax.broadcasted_iota(jnp.int32, (1, cache_size), 1)
        k_tok = lax.broadcasted_iota(jnp.int32, (1, width), 1)
        s_c = lax.dot_general(q, kc_ref[...], dims, preferred_element_type=jnp.float32) * factor
        s_c = s_c - slope * (q_pos - c_pos).astype(jnp.float32)
        s_c = jnp.where(c_pos < prefix, s_c, -jnp.inf)
        s_n = lax.dot_general(q, kn_ref[:width, :], dims, preferred_element_type=jnp.float32) * factor
        s_n = s_n - slope * (q_tok - k_tok).astype(jnp.float32)
        s_n = jnp.where(k_tok <= q_tok, s_n, -jnp.inf)
        m = jnp.maximum(jnp.max(s_c, axis=-1, keepdims=True), jnp.max(s_n, axis=-1, keepdims=True))
        e_c = jnp.exp(s_c - m)
        e_n = jnp.exp(s_n - m)
        l = jnp.sum(e_c, axis=-1, keepdims=True) + jnp.sum(e_n, axis=-1, keepdims=True)
        p_c = (e_c / l).astype(jnp.bfloat16)
        p_n = (e_n / l).astype(jnp.bfloat16)
        ctx = jnp.dot(p_c, vc_ref[...], preferred_element_type=jnp.float32)
        ctx = ctx + jnp.dot(p_n, vn_ref[:width, :], preferred_element_type=jnp.float32)
        o_ref[...] = ctx.astype(o_ref.dtype)

    for last in range(kn_ref.shape[0] // tq):
        pl.when(i == last)(functools.partial(tile, last, (last + 1) * tq))


def prefill_attention_kernel(merged, cache_keys, cache_values, prefix, slopes, head_size, tq=512):
    group = merged.shape[0]
    heads = merged.shape[1] // (3 * head_size)
    cache_size = cache_keys.shape[0]
    col = lambda c: (lambda h, i, *_: (0, h * 3 + c))
    return pl.pallas_call(
        functools.partial(_prefill_kernel, tq=tq),
        out_shape=jax.ShapeDtypeStruct((group, heads * head_size), jnp.bfloat16),
        grid_spec=pltpu.PrefetchScalarGridSpec(
            num_scalar_prefetch=2,
            grid=(heads, group // tq),
            in_specs=[
                pl.BlockSpec((tq, head_size), lambda h, i, *_: (i, h * 3)),
                pl.BlockSpec((group, head_size), col(1)),
                pl.BlockSpec((group, head_size), col(2)),
                pl.BlockSpec((cache_size, head_size), lambda h, i, *_: (0, h)),
                pl.BlockSpec((cache_size, head_size), lambda h, i, *_: (0, h)),
            ],
            out_specs=pl.BlockSpec((tq, head_size), lambda h, i, *_: (i, h)),
        ),
        cost_estimate=pl.CostEstimate(
            flops=4 * heads * group * (group + cache_size) * head_size,
            transcendentals=heads * group * (group + cache_size),
            bytes_accessed=2 * (group * heads * 3 * head_size + 2 * cache_size * heads * head_size + group * heads * head_size),
        ),
    )(prefix, slopes, merged, merged, merged, cache_keys, cache_values)


def decode_attention(query_row, new_key, new_value, cache_keys, cache_values, length, slopes):
    heads, head_size = query_row.shape
    factor = 1.0 / math.sqrt(head_size)
    cache_pos = jnp.arange(cache_keys.shape[0], dtype=jnp.int32)
    distance = (length - cache_pos).astype(jnp.float32)
    head_of_col = jnp.arange(heads * head_size, dtype=jnp.int32) // head_size
    own_head = head_of_col[:, None] == jnp.arange(heads, dtype=jnp.int32)[None, :]
    block_query = jnp.where(own_head, query_row.reshape(-1)[:, None], jnp.zeros((), query_row.dtype))
    cache_scores = jnp.dot(cache_keys, block_query, preferred_element_type=jnp.float32).T * factor
    cache_scores = cache_scores - slopes[:, None] * distance[None, :]
    cache_scores = jnp.where((cache_pos < length)[None, :], cache_scores, -jnp.inf)
    own_score = (
        jnp.einsum("hd,hd->h", query_row, new_key, preferred_element_type=jnp.float32)[:, None]
        * factor
    )
    highest = jnp.maximum(jnp.max(cache_scores, axis=-1, keepdims=True), own_score)
    cache_exp = jnp.exp(cache_scores - highest)
    own_exp = jnp.exp(own_score - highest)
    denominator = jnp.sum(cache_exp, axis=-1, keepdims=True) + own_exp
    cache_probs = (cache_exp / denominator).astype(jnp.bfloat16)
    own_prob = (own_exp / denominator).astype(jnp.bfloat16)
    every_head = jnp.dot(cache_probs, cache_values, preferred_element_type=jnp.float32)
    context = jnp.sum(jnp.where(own_head.T, every_head, 0.0), axis=0).reshape(heads, head_size)
    context = context + own_prob.astype(jnp.float32) * new_value.astype(jnp.float32)
    return context.astype(jnp.bfloat16).reshape(-1)


def per_device(
    pre_hidden,
    dec_hidden,
    norm_gain,
    norm_shift,
    qkv_weight,
    qkv_bias,
    out_weight,
    out_bias,
    pre_keys,
    pre_values,
    dec_keys,
    dec_values,
    prefix_lengths,
    cache_lengths,
    slot_of,
):
    head_size = HD
    local_heads = qkv_weight.shape[1] // (3 * head_size)
    slopes = alibi_slopes(lax.axis_index("tensor") * local_heads, local_heads, H)
    bias_sum = out_bias.astype(jnp.float32)
    normed = normalize(pre_hidden, norm_gain, norm_shift)
    normed, dec_hidden = lax.optimization_barrier((normed, dec_hidden))
    slot_count = dec_hidden.shape[0]
    dp_size = lax.axis_size("dp")
    tensor_size = lax.axis_size("tensor")
    group = lax.axis_index("dp")
    member = lax.axis_index("tensor")
    first_slot = group * slot_count
    shifted_rows = dec_hidden
    step = 1
    while step < dp_size:
        shifted_rows = jnp.concatenate(
            [shifted_rows, lax.ppermute(shifted_rows, "dp", [(i, i ^ step) for i in range(dp_size)])], axis=0
        )
        step *= 2
    slot_ids = first_slot + jnp.arange(slot_count, dtype=jnp.int32)
    request_ids = jnp.arange(slot_of.shape[0], dtype=jnp.int32)
    uses_slot = slot_of[None, :] == slot_ids[:, None]
    request_of_slot = jnp.sum(jnp.where(uses_slot, request_ids[None, :], 0), axis=1)
    arrival = ((request_of_slot // slot_count) ^ group) * slot_count + request_of_slot % slot_count
    pick = (arrival[:, None] == jnp.arange(shifted_rows.shape[0], dtype=jnp.int32)[None, :]).astype(
        jnp.bfloat16
    )
    arrived = jnp.dot(pick, shifted_rows, preferred_element_type=jnp.float32).astype(jnp.bfloat16)
    normed_slots = normalize(arrived, norm_gain, norm_shift)
    merged_slots = (
        jnp.dot(normed_slots, qkv_weight, preferred_element_type=jnp.float32)
        + qkv_bias.astype(jnp.float32)
    ).astype(jnp.bfloat16)
    merged_slots = merged_slots.reshape(slot_count, local_heads, 3, head_size)
    dec_cache = dec_keys.shape[1]
    slot_context = jax.vmap(decode_attention, in_axes=(0, 0, 0, 0, 0, 0, None))(
        merged_slots[:, :, 0],
        merged_slots[:, :, 1],
        merged_slots[:, :, 2],
        dec_keys,
        dec_values,
        cache_lengths,
        slopes,
    )
    slot_partial = jnp.dot(slot_context, out_weight, preferred_element_type=jnp.float32)
    partials = slot_partial
    step = 1
    while step < tensor_size:
        partials = jnp.concatenate(
            [partials, lax.ppermute(partials, "tensor", [(i, i ^ step) for i in range(tensor_size)])], axis=0
        )
        step *= 2
    partials = partials.reshape(tensor_size, slot_count, -1)
    slot_summed = partials[member ^ 0]
    for source in range(1, tensor_size):
        slot_summed = slot_summed + partials[member ^ source]
    slot_rows = (slot_summed + bias_sum + arrived.astype(jnp.float32)).astype(jnp.bfloat16)
    tensor_size = lax.axis_size("tensor")
    chips = tensor_size // 2
    member = lax.axis_index("tensor")
    chip = member // 2
    core = member % 2
    block = pre_hidden.shape[0]

    def route(k, flip):
        return [(i, ((i // 2 + k) % chips) * 2 + ((i % 2) ^ flip)) for i in range(tensor_size)]

    across_tokens = [lax.ppermute(normed, "tensor", route(k, 0)) for k in range(1, chips)]
    across_tokens, held_weight = lax.optimization_barrier((across_tokens, out_weight))
    same_core_tokens = [normed] + list(across_tokens)
    sibling_tokens = [lax.ppermute(t, "tensor", route(0, 1)) for t in same_core_tokens]
    sibling_tokens, slot_rows = lax.optimization_barrier((sibling_tokens, slot_rows))
    across_chips = [lax.ppermute(held_weight, "tensor", route(k, 0)) for k in range(1, chips)]
    bias_row = qkv_bias.astype(jnp.float32)
    merged_rows = jnp.zeros((tensor_size * block, qkv_weight.shape[1]), jnp.bfloat16)
    for flip, token_blocks in ((0, same_core_tokens), (1, sibling_tokens)):
        for k, token_block in enumerate(token_blocks):
            source = ((chip - k) % chips) * 2 + (core ^ flip)
            projected = (
                jnp.dot(token_block, qkv_weight, preferred_element_type=jnp.float32) + bias_row
            ).astype(jnp.bfloat16)
            merged_rows = lax.dynamic_update_slice_in_dim(merged_rows, projected, source * block, 0)
    returned = slot_rows
    step = 1
    while step < dp_size:
        returned = jnp.concatenate(
            [returned, lax.ppermute(returned, "dp", [(i, i ^ step) for i in range(dp_size)])], axis=0
        )
        step *= 2
    slot_wanted = lax.dynamic_slice_in_dim(slot_of, first_slot, slot_count)
    back = ((slot_wanted // slot_count) ^ group) * slot_count + slot_wanted % slot_count
    take = (back[:, None] == jnp.arange(returned.shape[0], dtype=jnp.int32)[None, :]).astype(jnp.bfloat16)
    dec_output = jnp.dot(take, returned, preferred_element_type=jnp.float32).astype(jnp.bfloat16)
    merged_rows, dec_output = lax.optimization_barrier((merged_rows, dec_output))
    context = prefill_attention_kernel(
        merged_rows, pre_keys[0], pre_values[0], prefix_lengths, slopes, head_size
    )
    context, across_chips = lax.optimization_barrier((context, across_chips))
    same_core = [out_weight] + list(across_chips)
    weight_blocks = same_core + [lax.ppermute(w, "tensor", route(0, 1)) for w in same_core]
    pieces = []
    for flip in (0, 1):
        for k in range(chips):
            if k == 0 and flip == 0:
                pieces.append(lax.dynamic_slice_in_dim(context, member * block, block))
                continue
            target = ((chip + k) % chips) * 2 + (core ^ flip)
            outgoing = lax.dynamic_slice_in_dim(context, target * block, block)
            pieces.append(lax.ppermute(outgoing, "tensor", route(k, flip)))
    summed = jnp.dot(pieces[0], weight_blocks[0], preferred_element_type=jnp.float32)
    for piece, weight in zip(pieces[1:], weight_blocks[1:]):
        summed = summed + jnp.dot(piece, weight, preferred_element_type=jnp.float32)
    pre_output = (summed + bias_sum + pre_hidden.astype(jnp.float32)).astype(jnp.bfloat16)
    return (pre_output, dec_output)


def solution(mesh):
    placed = (
        P(("dp", "tensor"), None),
        P("dp", None),
        P(),
        P(),
        P(None, "tensor"),
        P("tensor"),
        P("tensor", None),
        P(),
        P("dp", None, "tensor"),
        P("dp", None, "tensor"),
        P("dp", None, "tensor"),
        P("dp", None, "tensor"),
        P("dp"),
        P("dp"),
        P(),
    )
    return jax.shard_map(
        per_device,
        mesh=mesh,
        in_specs=placed,
        out_specs=(P(("dp", "tensor"), None), P("dp", None)),
        check_vma=False,
    )
```

```python
import math

import jax
import jax.numpy as jnp
from jax import lax
from jax.sharding import PartitionSpec as P
from jax.experimental import pallas as pl
from jax.experimental.pallas import tpu as pltpu
import functools

H = 16
HD = 128


EPSILON = 1e-05


def normalize(values, norm_gain, norm_shift):
    values = values.astype(jnp.float32)
    center = values - jnp.mean(values, axis=-1, keepdims=True)
    spread = jnp.mean(center * center, axis=-1, keepdims=True)
    scaled = center * lax.rsqrt(spread + EPSILON)
    return (scaled * norm_gain.astype(jnp.float32) + norm_shift.astype(jnp.float32)).astype(
        jnp.bfloat16
    )


def alibi_slopes(first_head, head_count, total_heads):
    head_ids = (first_head + jnp.arange(head_count, dtype=jnp.int32)).astype(jnp.float32)
    return jnp.exp2(-8.0 * (head_ids + 1.0) / total_heads)


def prefill_attention(merged_rows, cache_keys, cache_values, prefix, slopes):
    queries = merged_rows[:, :, 0]
    new_keys = merged_rows[:, :, 1]
    new_values = merged_rows[:, :, 2]
    group_size = merged_rows.shape[0]
    cache_size = cache_keys.shape[0]
    factor = 1.0 / math.sqrt(merged_rows.shape[-1])
    query_pos = prefix + jnp.arange(group_size, dtype=jnp.int32)
    cache_pos = jnp.arange(cache_size, dtype=jnp.int32)
    cache_dist = (query_pos[:, None] - cache_pos[None, :]).astype(jnp.float32)
    new_dist = (query_pos[:, None] - query_pos[None, :]).astype(jnp.float32)
    cache_scores = (
        jnp.einsum("qhd,khd->hqk", queries, cache_keys, preferred_element_type=jnp.float32) * factor
    )
    cache_scores = cache_scores - slopes[:, None, None] * cache_dist[None]
    cache_scores = jnp.where((cache_pos < prefix)[None, None, :], cache_scores, -jnp.inf)
    new_scores = (
        jnp.einsum("qhd,khd->hqk", queries, new_keys, preferred_element_type=jnp.float32) * factor
    )
    new_scores = new_scores - slopes[:, None, None] * new_dist[None]
    causal = (
        jnp.arange(group_size, dtype=jnp.int32)[None, :]
        <= jnp.arange(group_size, dtype=jnp.int32)[:, None]
    )
    new_scores = jnp.where(causal[None], new_scores, -jnp.inf)
    highest = jnp.maximum(
        jnp.max(cache_scores, axis=-1, keepdims=True), jnp.max(new_scores, axis=-1, keepdims=True)
    )
    cache_exp = jnp.exp(cache_scores - highest)
    new_exp = jnp.exp(new_scores - highest)
    denominator = jnp.sum(cache_exp, axis=-1, keepdims=True) + jnp.sum(
        new_exp, axis=-1, keepdims=True
    )
    cache_probs = (cache_exp / denominator).astype(jnp.bfloat16)
    new_probs = (new_exp / denominator).astype(jnp.bfloat16)
    context = jnp.einsum(
        "hqk,khd->qhd", cache_probs, cache_values, preferred_element_type=jnp.float32
    )
    context = context + jnp.einsum(
        "hqk,khd->qhd", new_probs, new_values, preferred_element_type=jnp.float32
    )
    return context.astype(jnp.bfloat16).reshape(group_size, -1)


def _prefill_kernel(prefix_ref, slopes_ref, q_ref, kn_ref, vn_ref, kc_ref, vc_ref, o_ref, *, tq):
    h = pl.program_id(0)
    i = pl.program_id(1)
    prefix = prefix_ref[0]
    slope = slopes_ref[h]
    factor = 1.0 / math.sqrt(q_ref.shape[-1])
    dims = (((1,), (1,)), ((), ()))
    cache_size = kc_ref.shape[0]

    def tile(last, width):
        q = q_ref[...]
        q_tok = last * tq + lax.broadcasted_iota(jnp.int32, (tq, 1), 0)
        q_pos = prefix + q_tok
        c_pos = lax.broadcasted_iota(jnp.int32, (1, cache_size), 1)
        k_tok = lax.broadcasted_iota(jnp.int32, (1, width), 1)
        s_c = lax.dot_general(q, kc_ref[...], dims, preferred_element_type=jnp.float32) * factor
        s_c = s_c - slope * (q_pos - c_pos).astype(jnp.float32)
        s_c = jnp.where(c_pos < prefix, s_c, -jnp.inf)
        s_n = lax.dot_general(q, kn_ref[:width, :], dims, preferred_element_type=jnp.float32) * factor
        s_n = s_n - slope * (q_tok - k_tok).astype(jnp.float32)
        s_n = jnp.where(k_tok <= q_tok, s_n, -jnp.inf)
        m = jnp.maximum(jnp.max(s_c, axis=-1, keepdims=True), jnp.max(s_n, axis=-1, keepdims=True))
        e_c = jnp.exp(s_c - m)
        e_n = jnp.exp(s_n - m)
        l = jnp.sum(e_c, axis=-1, keepdims=True) + jnp.sum(e_n, axis=-1, keepdims=True)
        p_c = (e_c / l).astype(jnp.bfloat16)
        p_n = (e_n / l).astype(jnp.bfloat16)
        ctx = jnp.dot(p_c, vc_ref[...], preferred_element_type=jnp.float32)
        ctx = ctx + jnp.dot(p_n, vn_ref[:width, :], preferred_element_type=jnp.float32)
        o_ref[...] = ctx.astype(o_ref.dtype)

    for last in range(kn_ref.shape[0] // tq):
        pl.when(i == last)(functools.partial(tile, last, (last + 1) * tq))


def prefill_attention_kernel(merged, cache_keys, cache_values, prefix, slopes, head_size, tq=256):
    group = merged.shape[0]
    heads = merged.shape[1] // (3 * head_size)
    cache_size = cache_keys.shape[0]
    col = lambda c: (lambda h, i, *_: (0, h * 3 + c))
    return pl.pallas_call(
        functools.partial(_prefill_kernel, tq=tq),
        out_shape=jax.ShapeDtypeStruct((group, heads * head_size), jnp.bfloat16),
        grid_spec=pltpu.PrefetchScalarGridSpec(
            num_scalar_prefetch=2,
            grid=(heads, group // tq),
            in_specs=[
                pl.BlockSpec((tq, head_size), lambda h, i, *_: (i, h * 3)),
                pl.BlockSpec((group, head_size), col(1)),
                pl.BlockSpec((group, head_size), col(2)),
                pl.BlockSpec((cache_size, head_size), lambda h, i, *_: (0, h)),
                pl.BlockSpec((cache_size, head_size), lambda h, i, *_: (0, h)),
            ],
            out_specs=pl.BlockSpec((tq, head_size), lambda h, i, *_: (i, h)),
        ),
        cost_estimate=pl.CostEstimate(
            flops=4 * heads * group * (group + cache_size) * head_size,
            transcendentals=heads * group * (group + cache_size),
            bytes_accessed=2 * (group * heads * 3 * head_size + 2 * cache_size * heads * head_size + group * heads * head_size),
        ),
    )(prefix, slopes, merged, merged, merged, cache_keys, cache_values)


def decode_attention(query_row, new_key, new_value, cache_keys, cache_values, length, slopes):
    heads, head_size = query_row.shape
    factor = 1.0 / math.sqrt(head_size)
    cache_pos = jnp.arange(cache_keys.shape[0], dtype=jnp.int32)
    distance = (length - cache_pos).astype(jnp.float32)
    head_of_col = jnp.arange(heads * head_size, dtype=jnp.int32) // head_size
    own_head = head_of_col[:, None] == jnp.arange(heads, dtype=jnp.int32)[None, :]
    block_query = jnp.where(own_head, query_row.reshape(-1)[:, None], jnp.zeros((), query_row.dtype))
    cache_scores = jnp.dot(cache_keys, block_query, preferred_element_type=jnp.float32).T * factor
    cache_scores = cache_scores - slopes[:, None] * distance[None, :]
    cache_scores = jnp.where((cache_pos < length)[None, :], cache_scores, -jnp.inf)
    own_score = (
        jnp.einsum("hd,hd->h", query_row, new_key, preferred_element_type=jnp.float32)[:, None]
        * factor
    )
    highest = jnp.maximum(jnp.max(cache_scores, axis=-1, keepdims=True), own_score)
    cache_exp = jnp.exp(cache_scores - highest)
    own_exp = jnp.exp(own_score - highest)
    denominator = jnp.sum(cache_exp, axis=-1, keepdims=True) + own_exp
    cache_probs = (cache_exp / denominator).astype(jnp.bfloat16)
    own_prob = (own_exp / denominator).astype(jnp.bfloat16)
    every_head = jnp.dot(cache_probs, cache_values, preferred_element_type=jnp.float32)
    context = jnp.sum(jnp.where(own_head.T, every_head, 0.0), axis=0).reshape(heads, head_size)
    context = context + own_prob.astype(jnp.float32) * new_value.astype(jnp.float32)
    return context.astype(jnp.bfloat16).reshape(-1)


def per_device(
    pre_hidden,
    dec_hidden,
    norm_gain,
    norm_shift,
    qkv_weight,
    qkv_bias,
    out_weight,
    out_bias,
    pre_keys,
    pre_values,
    dec_keys,
    dec_values,
    prefix_lengths,
    cache_lengths,
    slot_of,
):
    head_size = HD
    local_heads = qkv_weight.shape[1] // (3 * head_size)
    slopes = alibi_slopes(lax.axis_index("tensor") * local_heads, local_heads, H)
    bias_sum = out_bias.astype(jnp.float32)
    normed = normalize(pre_hidden, norm_gain, norm_shift)
    normed, dec_hidden = lax.optimization_barrier((normed, dec_hidden))
    slot_count = dec_hidden.shape[0]
    dp_size = lax.axis_size("dp")
    tensor_size = lax.axis_size("tensor")
    group = lax.axis_index("dp")
    member = lax.axis_index("tensor")
    first_slot = group * slot_count
    shifted_rows = dec_hidden
    step = 1
    while step < dp_size:
        shifted_rows = jnp.concatenate(
            [shifted_rows, lax.ppermute(shifted_rows, "dp", [(i, i ^ step) for i in range(dp_size)])], axis=0
        )
        step *= 2
    slot_ids = first_slot + jnp.arange(slot_count, dtype=jnp.int32)
    request_ids = jnp.arange(slot_of.shape[0], dtype=jnp.int32)
    uses_slot = slot_of[None, :] == slot_ids[:, None]
    request_of_slot = jnp.sum(jnp.where(uses_slot, request_ids[None, :], 0), axis=1)
    arrival = ((request_of_slot // slot_count) ^ group) * slot_count + request_of_slot % slot_count
    pick = (arrival[:, None] == jnp.arange(shifted_rows.shape[0], dtype=jnp.int32)[None, :]).astype(
        jnp.bfloat16
    )
    arrived = jnp.dot(pick, shifted_rows, preferred_element_type=jnp.float32).astype(jnp.bfloat16)
    normed_slots = normalize(arrived, norm_gain, norm_shift)
    merged_slots = (
        jnp.dot(normed_slots, qkv_weight, preferred_element_type=jnp.float32)
        + qkv_bias.astype(jnp.float32)
    ).astype(jnp.bfloat16)
    merged_slots = merged_slots.reshape(slot_count, local_heads, 3, head_size)
    dec_cache = dec_keys.shape[1]
    slot_context = jax.vmap(decode_attention, in_axes=(0, 0, 0, 0, 0, 0, None))(
        merged_slots[:, :, 0],
        merged_slots[:, :, 1],
        merged_slots[:, :, 2],
        dec_keys,
        dec_values,
        cache_lengths,
        slopes,
    )
    slot_partial = jnp.dot(slot_context, out_weight, preferred_element_type=jnp.float32)
    partials = slot_partial
    step = 1
    while step < tensor_size:
        partials = jnp.concatenate(
            [partials, lax.ppermute(partials, "tensor", [(i, i ^ step) for i in range(tensor_size)])], axis=0
        )
        step *= 2
    partials = partials.reshape(tensor_size, slot_count, -1)
    slot_summed = partials[member ^ 0]
    for source in range(1, tensor_size):
        slot_summed = slot_summed + partials[member ^ source]
    slot_rows = (slot_summed + bias_sum + arrived.astype(jnp.float32)).astype(jnp.bfloat16)
    tensor_size = lax.axis_size("tensor")
    chips = tensor_size // 2
    member = lax.axis_index("tensor")
    chip = member // 2
    core = member % 2
    block = pre_hidden.shape[0]

    def route(k, flip):
        return [(i, ((i // 2 + k) % chips) * 2 + ((i % 2) ^ flip)) for i in range(tensor_size)]

    across_tokens = [lax.ppermute(normed, "tensor", route(k, 0)) for k in range(1, chips)]
    across_tokens, held_weight = lax.optimization_barrier((across_tokens, out_weight))
    same_core_tokens = [normed] + list(across_tokens)
    sibling_tokens = [lax.ppermute(t, "tensor", route(0, 1)) for t in same_core_tokens]
    sibling_tokens, slot_rows = lax.optimization_barrier((sibling_tokens, slot_rows))
    across_chips = [lax.ppermute(held_weight, "tensor", route(k, 0)) for k in range(1, chips)]
    bias_row = qkv_bias.astype(jnp.float32)
    merged_rows = jnp.zeros((tensor_size * block, qkv_weight.shape[1]), jnp.bfloat16)
    for flip, token_blocks in ((0, same_core_tokens), (1, sibling_tokens)):
        for k, token_block in enumerate(token_blocks):
            source = ((chip - k) % chips) * 2 + (core ^ flip)
            projected = (
                jnp.dot(token_block, qkv_weight, preferred_element_type=jnp.float32) + bias_row
            ).astype(jnp.bfloat16)
            merged_rows = lax.dynamic_update_slice_in_dim(merged_rows, projected, source * block, 0)
    returned = slot_rows
    step = 1
    while step < dp_size:
        returned = jnp.concatenate(
            [returned, lax.ppermute(returned, "dp", [(i, i ^ step) for i in range(dp_size)])], axis=0
        )
        step *= 2
    slot_wanted = lax.dynamic_slice_in_dim(slot_of, first_slot, slot_count)
    back = ((slot_wanted // slot_count) ^ group) * slot_count + slot_wanted % slot_count
    take = (back[:, None] == jnp.arange(returned.shape[0], dtype=jnp.int32)[None, :]).astype(jnp.bfloat16)
    dec_output = jnp.dot(take, returned, preferred_element_type=jnp.float32).astype(jnp.bfloat16)
    merged_rows, dec_output = lax.optimization_barrier((merged_rows, dec_output))
    context = prefill_attention_kernel(
        merged_rows, pre_keys[0], pre_values[0], prefix_lengths, slopes, head_size
    )
    context, across_chips = lax.optimization_barrier((context, across_chips))
    same_core = [out_weight] + list(across_chips)
    weight_blocks = same_core + [lax.ppermute(w, "tensor", route(0, 1)) for w in same_core]
    pieces = []
    for flip in (0, 1):
        for k in range(chips):
            if k == 0 and flip == 0:
                pieces.append(lax.dynamic_slice_in_dim(context, member * block, block))
                continue
            target = ((chip + k) % chips) * 2 + (core ^ flip)
            outgoing = lax.dynamic_slice_in_dim(context, target * block, block)
            pieces.append(lax.ppermute(outgoing, "tensor", route(k, flip)))
    summed = pre_hidden.astype(jnp.float32) + bias_sum
    for piece, weight in zip(pieces, weight_blocks):
        summed = summed + jnp.dot(piece, weight, preferred_element_type=jnp.float32)
    pre_output = summed.astype(jnp.bfloat16)
    return (pre_output, dec_output)


def solution(mesh):
    placed = (
        P(("dp", "tensor"), None),
        P("dp", None),
        P(),
        P(),
        P(None, "tensor"),
        P("tensor"),
        P("tensor", None),
        P(),
        P("dp", None, "tensor"),
        P("dp", None, "tensor"),
        P("dp", None, "tensor"),
        P("dp", None, "tensor"),
        P("dp"),
        P("dp"),
        P(),
    )
    return jax.shard_map(
        per_device,
        mesh=mesh,
        in_specs=placed,
        out_specs=(P(("dp", "tensor"), None), P("dp", None)),
        check_vma=False,
    )
```

```python
import math

import jax
import jax.numpy as jnp
from jax import lax
from jax.sharding import PartitionSpec as P
from jax.experimental import pallas as pl
from jax.experimental.pallas import tpu as pltpu
import functools

H = 16
HD = 128


EPSILON = 1e-05


def normalize(values, norm_gain, norm_shift):
    values = values.astype(jnp.float32)
    center = values - jnp.mean(values, axis=-1, keepdims=True)
    spread = jnp.mean(center * center, axis=-1, keepdims=True)
    scaled = center * lax.rsqrt(spread + EPSILON)
    return (scaled * norm_gain.astype(jnp.float32) + norm_shift.astype(jnp.float32)).astype(
        jnp.bfloat16
    )


def alibi_slopes(first_head, head_count, total_heads):
    head_ids = (first_head + jnp.arange(head_count, dtype=jnp.int32)).astype(jnp.float32)
    return jnp.exp2(-8.0 * (head_ids + 1.0) / total_heads)


def prefill_attention(merged_rows, cache_keys, cache_values, prefix, slopes):
    queries = merged_rows[:, :, 0]
    new_keys = merged_rows[:, :, 1]
    new_values = merged_rows[:, :, 2]
    group_size = merged_rows.shape[0]
    cache_size = cache_keys.shape[0]
    factor = 1.0 / math.sqrt(merged_rows.shape[-1])
    query_pos = prefix + jnp.arange(group_size, dtype=jnp.int32)
    cache_pos = jnp.arange(cache_size, dtype=jnp.int32)
    cache_dist = (query_pos[:, None] - cache_pos[None, :]).astype(jnp.float32)
    new_dist = (query_pos[:, None] - query_pos[None, :]).astype(jnp.float32)
    cache_scores = (
        jnp.einsum("qhd,khd->hqk", queries, cache_keys, preferred_element_type=jnp.float32) * factor
    )
    cache_scores = cache_scores - slopes[:, None, None] * cache_dist[None]
    cache_scores = jnp.where((cache_pos < prefix)[None, None, :], cache_scores, -jnp.inf)
    new_scores = (
        jnp.einsum("qhd,khd->hqk", queries, new_keys, preferred_element_type=jnp.float32) * factor
    )
    new_scores = new_scores - slopes[:, None, None] * new_dist[None]
    causal = (
        jnp.arange(group_size, dtype=jnp.int32)[None, :]
        <= jnp.arange(group_size, dtype=jnp.int32)[:, None]
    )
    new_scores = jnp.where(causal[None], new_scores, -jnp.inf)
    highest = jnp.maximum(
        jnp.max(cache_scores, axis=-1, keepdims=True), jnp.max(new_scores, axis=-1, keepdims=True)
    )
    cache_exp = jnp.exp(cache_scores - highest)
    new_exp = jnp.exp(new_scores - highest)
    denominator = jnp.sum(cache_exp, axis=-1, keepdims=True) + jnp.sum(
        new_exp, axis=-1, keepdims=True
    )
    cache_probs = (cache_exp / denominator).astype(jnp.bfloat16)
    new_probs = (new_exp / denominator).astype(jnp.bfloat16)
    context = jnp.einsum(
        "hqk,khd->qhd", cache_probs, cache_values, preferred_element_type=jnp.float32
    )
    context = context + jnp.einsum(
        "hqk,khd->qhd", new_probs, new_values, preferred_element_type=jnp.float32
    )
    return context.astype(jnp.bfloat16).reshape(group_size, -1)


def _prefill_kernel(prefix_ref, slopes_ref, place_ref, q_ref, kn_ref, vn_ref, kc_ref, vc_ref, o_ref, *, tq):
    h = pl.program_id(0)
    i = pl.program_id(1)
    prefix = prefix_ref[0]
    slope = slopes_ref[h]
    factor = 1.0 / math.sqrt(q_ref.shape[-1])
    dims = (((1,), (1,)), ((), ()))
    cache_size = kc_ref.shape[0]

    def tile(last, width):
        q = q_ref[...]
        q_tok = last * tq + lax.broadcasted_iota(jnp.int32, (tq, 1), 0)
        q_pos = prefix + q_tok
        c_pos = lax.broadcasted_iota(jnp.int32, (1, cache_size), 1)
        k_tok = lax.broadcasted_iota(jnp.int32, (1, width), 1)
        s_c = lax.dot_general(q, kc_ref[...], dims, preferred_element_type=jnp.float32) * factor
        s_c = s_c - slope * (q_pos - c_pos).astype(jnp.float32)
        s_c = jnp.where(c_pos < prefix, s_c, -jnp.inf)
        s_n = lax.dot_general(q, kn_ref[:width, :], dims, preferred_element_type=jnp.float32) * factor
        s_n = s_n - slope * (q_tok - k_tok).astype(jnp.float32)
        s_n = jnp.where(k_tok <= q_tok, s_n, -jnp.inf)
        m = jnp.maximum(jnp.max(s_c, axis=-1, keepdims=True), jnp.max(s_n, axis=-1, keepdims=True))
        e_c = jnp.exp(s_c - m)
        e_n = jnp.exp(s_n - m)
        l = jnp.sum(e_c, axis=-1, keepdims=True) + jnp.sum(e_n, axis=-1, keepdims=True)
        p_c = (e_c / l).astype(jnp.bfloat16)
        p_n = (e_n / l).astype(jnp.bfloat16)
        ctx = jnp.dot(p_c, vc_ref[...], preferred_element_type=jnp.float32)
        ctx = ctx + jnp.dot(p_n, vn_ref[:width, :], preferred_element_type=jnp.float32)
        o_ref[...] = ctx.astype(o_ref.dtype)

    for last in range(kn_ref.shape[0] // tq):
        pl.when(i == last)(functools.partial(tile, last, (last + 1) * tq))


def prefill_attention_kernel(merged, cache_keys, cache_values, prefix, slopes, place, head_size, tq):
    group = merged.shape[0]
    heads = merged.shape[1] // (3 * head_size)
    cache_size = cache_keys.shape[0]
    col = lambda c: (lambda h, i, *_: (0, h * 3 + c))
    return pl.pallas_call(
        functools.partial(_prefill_kernel, tq=tq),
        out_shape=jax.ShapeDtypeStruct((group, heads * head_size), jnp.bfloat16),
        grid_spec=pltpu.PrefetchScalarGridSpec(
            num_scalar_prefetch=3,
            grid=(heads, group // tq),
            in_specs=[
                pl.BlockSpec((tq, head_size), lambda h, i, *_: (i, h * 3)),
                pl.BlockSpec((group, head_size), col(1)),
                pl.BlockSpec((group, head_size), col(2)),
                pl.BlockSpec((cache_size, head_size), lambda h, i, *_: (0, h)),
                pl.BlockSpec((cache_size, head_size), lambda h, i, *_: (0, h)),
            ],
            out_specs=pl.BlockSpec((tq, head_size), lambda h, i, p, s, place: (place[i], h)),
        ),
        cost_estimate=pl.CostEstimate(
            flops=4 * heads * group * (group + cache_size) * head_size,
            transcendentals=heads * group * (group + cache_size),
            bytes_accessed=2 * (group * heads * 3 * head_size + 2 * cache_size * heads * head_size + group * heads * head_size),
        ),
    )(prefix, slopes, place, merged, merged, merged, cache_keys, cache_values)


def decode_attention(query_row, new_key, new_value, cache_keys, cache_values, length, slopes):
    heads, head_size = query_row.shape
    factor = 1.0 / math.sqrt(head_size)
    cache_pos = jnp.arange(cache_keys.shape[0], dtype=jnp.int32)
    distance = (length - cache_pos).astype(jnp.float32)
    head_of_col = jnp.arange(heads * head_size, dtype=jnp.int32) // head_size
    own_head = head_of_col[:, None] == jnp.arange(heads, dtype=jnp.int32)[None, :]
    block_query = jnp.where(own_head, query_row.reshape(-1)[:, None], jnp.zeros((), query_row.dtype))
    cache_scores = jnp.dot(cache_keys, block_query, preferred_element_type=jnp.float32).T * factor
    cache_scores = cache_scores - slopes[:, None] * distance[None, :]
    cache_scores = jnp.where((cache_pos < length)[None, :], cache_scores, -jnp.inf)
    own_score = (
        jnp.einsum("hd,hd->h", query_row, new_key, preferred_element_type=jnp.float32)[:, None]
        * factor
    )
    highest = jnp.maximum(jnp.max(cache_scores, axis=-1, keepdims=True), own_score)
    cache_exp = jnp.exp(cache_scores - highest)
    own_exp = jnp.exp(own_score - highest)
    denominator = jnp.sum(cache_exp, axis=-1, keepdims=True) + own_exp
    cache_probs = (cache_exp / denominator).astype(jnp.bfloat16)
    own_prob = (own_exp / denominator).astype(jnp.bfloat16)
    every_head = jnp.dot(cache_probs, cache_values, preferred_element_type=jnp.float32)
    context = jnp.sum(jnp.where(own_head.T, every_head, 0.0), axis=0).reshape(heads, head_size)
    context = context + own_prob.astype(jnp.float32) * new_value.astype(jnp.float32)
    return context.astype(jnp.bfloat16).reshape(-1)


def per_device(
    pre_hidden,
    dec_hidden,
    norm_gain,
    norm_shift,
    qkv_weight,
    qkv_bias,
    out_weight,
    out_bias,
    pre_keys,
    pre_values,
    dec_keys,
    dec_values,
    prefix_lengths,
    cache_lengths,
    slot_of,
):
    head_size = HD
    local_heads = qkv_weight.shape[1] // (3 * head_size)
    slopes = alibi_slopes(lax.axis_index("tensor") * local_heads, local_heads, H)
    bias_sum = out_bias.astype(jnp.float32)
    normed = normalize(pre_hidden, norm_gain, norm_shift)
    normed, dec_hidden = lax.optimization_barrier((normed, dec_hidden))
    slot_count = dec_hidden.shape[0]
    dp_size = lax.axis_size("dp")
    tensor_size = lax.axis_size("tensor")
    group = lax.axis_index("dp")
    member = lax.axis_index("tensor")
    first_slot = group * slot_count
    shifted_rows = dec_hidden
    step = 1
    while step < dp_size:
        shifted_rows = jnp.concatenate(
            [shifted_rows, lax.ppermute(shifted_rows, "dp", [(i, i ^ step) for i in range(dp_size)])], axis=0
        )
        step *= 2
    slot_ids = first_slot + jnp.arange(slot_count, dtype=jnp.int32)
    request_ids = jnp.arange(slot_of.shape[0], dtype=jnp.int32)
    uses_slot = slot_of[None, :] == slot_ids[:, None]
    request_of_slot = jnp.sum(jnp.where(uses_slot, request_ids[None, :], 0), axis=1)
    arrival = ((request_of_slot // slot_count) ^ group) * slot_count + request_of_slot % slot_count
    pick = (arrival[:, None] == jnp.arange(shifted_rows.shape[0], dtype=jnp.int32)[None, :]).astype(
        jnp.bfloat16
    )
    arrived = jnp.dot(pick, shifted_rows, preferred_element_type=jnp.float32).astype(jnp.bfloat16)
    normed_slots = normalize(arrived, norm_gain, norm_shift)
    merged_slots = (
        jnp.dot(normed_slots, qkv_weight, preferred_element_type=jnp.float32)
        + qkv_bias.astype(jnp.float32)
    ).astype(jnp.bfloat16)
    merged_slots = merged_slots.reshape(slot_count, local_heads, 3, head_size)
    dec_cache = dec_keys.shape[1]
    slot_context = jax.vmap(decode_attention, in_axes=(0, 0, 0, 0, 0, 0, None))(
        merged_slots[:, :, 0],
        merged_slots[:, :, 1],
        merged_slots[:, :, 2],
        dec_keys,
        dec_values,
        cache_lengths,
        slopes,
    )
    slot_partial = jnp.dot(slot_context, out_weight, preferred_element_type=jnp.float32)
    partials = slot_partial
    step = 1
    while step < tensor_size:
        partials = jnp.concatenate(
            [partials, lax.ppermute(partials, "tensor", [(i, i ^ step) for i in range(tensor_size)])], axis=0
        )
        step *= 2
    partials = partials.reshape(tensor_size, slot_count, -1)
    slot_summed = partials[member ^ 0]
    for source in range(1, tensor_size):
        slot_summed = slot_summed + partials[member ^ source]
    slot_rows = (slot_summed + bias_sum + arrived.astype(jnp.float32)).astype(jnp.bfloat16)
    tensor_size = lax.axis_size("tensor")
    chips = tensor_size // 2
    member = lax.axis_index("tensor")
    chip = member // 2
    core = member % 2
    block = pre_hidden.shape[0]

    def route(k, flip):
        return [(i, ((i // 2 + k) % chips) * 2 + ((i % 2) ^ flip)) for i in range(tensor_size)]

    across_tokens = [lax.ppermute(normed, "tensor", route(k, 0)) for k in range(1, chips)]
    across_tokens, held_weight = lax.optimization_barrier((across_tokens, out_weight))
    same_core_tokens = [normed] + list(across_tokens)
    sibling_tokens = [lax.ppermute(t, "tensor", route(0, 1)) for t in same_core_tokens]
    sibling_tokens, slot_rows = lax.optimization_barrier((sibling_tokens, slot_rows))
    across_chips = [lax.ppermute(held_weight, "tensor", route(k, 0)) for k in range(1, chips)]
    bias_row = qkv_bias.astype(jnp.float32)
    merged_rows = jnp.zeros((tensor_size * block, qkv_weight.shape[1]), jnp.bfloat16)
    for flip, token_blocks in ((0, same_core_tokens), (1, sibling_tokens)):
        for k, token_block in enumerate(token_blocks):
            source = ((chip - k) % chips) * 2 + (core ^ flip)
            projected = (
                jnp.dot(token_block, qkv_weight, preferred_element_type=jnp.float32) + bias_row
            ).astype(jnp.bfloat16)
            merged_rows = lax.dynamic_update_slice_in_dim(merged_rows, projected, source * block, 0)
    returned = slot_rows
    step = 1
    while step < dp_size:
        returned = jnp.concatenate(
            [returned, lax.ppermute(returned, "dp", [(i, i ^ step) for i in range(dp_size)])], axis=0
        )
        step *= 2
    slot_wanted = lax.dynamic_slice_in_dim(slot_of, first_slot, slot_count)
    back = ((slot_wanted // slot_count) ^ group) * slot_count + slot_wanted % slot_count
    take = (back[:, None] == jnp.arange(returned.shape[0], dtype=jnp.int32)[None, :]).astype(jnp.bfloat16)
    dec_output = jnp.dot(take, returned, preferred_element_type=jnp.float32).astype(jnp.bfloat16)
    merged_rows, dec_output = lax.optimization_barrier((merged_rows, dec_output))
    members = jnp.arange(tensor_size, dtype=jnp.int32)
    place = ((members % 2) ^ core) * chips + (members // 2 - chip) % chips
    context = prefill_attention_kernel(
        merged_rows, pre_keys[0], pre_values[0], prefix_lengths, slopes, place, head_size, block
    )
    context, across_chips = lax.optimization_barrier((context, across_chips))
    same_core = [out_weight] + list(across_chips)
    weight_blocks = same_core + [lax.ppermute(w, "tensor", route(0, 1)) for w in same_core]
    pieces = []
    for flip in (0, 1):
        for k in range(chips):
            position = flip * chips + k
            outgoing = context[position * block:(position + 1) * block]
            if k == 0 and flip == 0:
                pieces.append(outgoing)
                continue
            pieces.append(lax.ppermute(outgoing, "tensor", route(k, flip)))
    summed = pre_hidden.astype(jnp.float32) + bias_sum
    for piece, weight in zip(pieces, weight_blocks):
        summed = summed + jnp.dot(piece, weight, preferred_element_type=jnp.float32)
    pre_output = summed.astype(jnp.bfloat16)
    return (pre_output, dec_output)


def solution(mesh):
    placed = (
        P(("dp", "tensor"), None),
        P("dp", None),
        P(),
        P(),
        P(None, "tensor"),
        P("tensor"),
        P("tensor", None),
        P(),
        P("dp", None, "tensor"),
        P("dp", None, "tensor"),
        P("dp", None, "tensor"),
        P("dp", None, "tensor"),
        P("dp"),
        P("dp"),
        P(),
    )
    return jax.shard_map(
        per_device,
        mesh=mesh,
        in_specs=placed,
        out_specs=(P(("dp", "tensor"), None), P("dp", None)),
        check_vma=False,
    )
```

```python
import math

import jax
import jax.numpy as jnp
from jax import lax
from jax.sharding import PartitionSpec as P
from jax.experimental import pallas as pl
from jax.experimental.pallas import tpu as pltpu
import functools

H = 16
HD = 128


EPSILON = 1e-05


def normalize(values, norm_gain, norm_shift):
    values = values.astype(jnp.float32)
    center = values - jnp.mean(values, axis=-1, keepdims=True)
    spread = jnp.mean(center * center, axis=-1, keepdims=True)
    scaled = center * lax.rsqrt(spread + EPSILON)
    return (scaled * norm_gain.astype(jnp.float32) + norm_shift.astype(jnp.float32)).astype(
        jnp.bfloat16
    )


def alibi_slopes(first_head, head_count, total_heads):
    head_ids = (first_head + jnp.arange(head_count, dtype=jnp.int32)).astype(jnp.float32)
    return jnp.exp2(-8.0 * (head_ids + 1.0) / total_heads)


def prefill_attention(merged_rows, cache_keys, cache_values, prefix, slopes):
    queries = merged_rows[:, :, 0]
    new_keys = merged_rows[:, :, 1]
    new_values = merged_rows[:, :, 2]
    group_size = merged_rows.shape[0]
    cache_size = cache_keys.shape[0]
    factor = 1.0 / math.sqrt(merged_rows.shape[-1])
    query_pos = prefix + jnp.arange(group_size, dtype=jnp.int32)
    cache_pos = jnp.arange(cache_size, dtype=jnp.int32)
    cache_dist = (query_pos[:, None] - cache_pos[None, :]).astype(jnp.float32)
    new_dist = (query_pos[:, None] - query_pos[None, :]).astype(jnp.float32)
    cache_scores = (
        jnp.einsum("qhd,khd->hqk", queries, cache_keys, preferred_element_type=jnp.float32) * factor
    )
    cache_scores = cache_scores - slopes[:, None, None] * cache_dist[None]
    cache_scores = jnp.where((cache_pos < prefix)[None, None, :], cache_scores, -jnp.inf)
    new_scores = (
        jnp.einsum("qhd,khd->hqk", queries, new_keys, preferred_element_type=jnp.float32) * factor
    )
    new_scores = new_scores - slopes[:, None, None] * new_dist[None]
    causal = (
        jnp.arange(group_size, dtype=jnp.int32)[None, :]
        <= jnp.arange(group_size, dtype=jnp.int32)[:, None]
    )
    new_scores = jnp.where(causal[None], new_scores, -jnp.inf)
    highest = jnp.maximum(
        jnp.max(cache_scores, axis=-1, keepdims=True), jnp.max(new_scores, axis=-1, keepdims=True)
    )
    cache_exp = jnp.exp(cache_scores - highest)
    new_exp = jnp.exp(new_scores - highest)
    denominator = jnp.sum(cache_exp, axis=-1, keepdims=True) + jnp.sum(
        new_exp, axis=-1, keepdims=True
    )
    cache_probs = (cache_exp / denominator).astype(jnp.bfloat16)
    new_probs = (new_exp / denominator).astype(jnp.bfloat16)
    context = jnp.einsum(
        "hqk,khd->qhd", cache_probs, cache_values, preferred_element_type=jnp.float32
    )
    context = context + jnp.einsum(
        "hqk,khd->qhd", new_probs, new_values, preferred_element_type=jnp.float32
    )
    return context.astype(jnp.bfloat16).reshape(group_size, -1)


def _prefill_kernel(prefix_ref, slopes_ref, place_ref, q_ref, kn_ref, vn_ref, kc_ref, vc_ref, o_ref, *, tq):
    h = pl.program_id(0)
    i = pl.program_id(1)
    prefix = prefix_ref[0]
    slope = slopes_ref[h]
    factor = 1.0 / math.sqrt(q_ref.shape[-1])
    dims = (((1,), (1,)), ((), ()))
    cache_size = kc_ref.shape[0]

    def tile(last, width):
        q = q_ref[...]
        q_tok = last * tq + lax.broadcasted_iota(jnp.int32, (tq, 1), 0)
        q_pos = prefix + q_tok
        c_pos = lax.broadcasted_iota(jnp.int32, (1, cache_size), 1)
        k_tok = lax.broadcasted_iota(jnp.int32, (1, width), 1)
        s_c = lax.dot_general(q, kc_ref[...], dims, preferred_element_type=jnp.float32) * factor
        s_c = s_c - slope * (q_pos - c_pos).astype(jnp.float32)
        s_c = jnp.where(c_pos < prefix, s_c, -jnp.inf)
        s_n = lax.dot_general(q, kn_ref[:width, :], dims, preferred_element_type=jnp.float32) * factor
        s_n = s_n - slope * (q_tok - k_tok).astype(jnp.float32)
        s_n = jnp.where(k_tok <= q_tok, s_n, -jnp.inf)
        m = jnp.maximum(jnp.max(s_c, axis=-1, keepdims=True), jnp.max(s_n, axis=-1, keepdims=True))
        e_c = jnp.exp(s_c - m)
        e_n = jnp.exp(s_n - m)
        l = jnp.sum(e_c, axis=-1, keepdims=True) + jnp.sum(e_n, axis=-1, keepdims=True)
        p_c = (e_c / l).astype(jnp.bfloat16)
        p_n = (e_n / l).astype(jnp.bfloat16)
        ctx = jnp.dot(p_c, vc_ref[...], preferred_element_type=jnp.float32)
        ctx = ctx + jnp.dot(p_n, vn_ref[:width, :], preferred_element_type=jnp.float32)
        o_ref[...] = ctx.astype(o_ref.dtype)

    for last in range(kn_ref.shape[0] // tq):
        pl.when(i == last)(functools.partial(tile, last, (last + 1) * tq))


def prefill_attention_kernel(merged, cache_keys, cache_values, prefix, slopes, place, head_size, tq):
    group = merged.shape[0]
    heads = merged.shape[1] // (3 * head_size)
    cache_size = cache_keys.shape[0]
    col = lambda c: (lambda h, i, *_: (0, h * 3 + c))
    return pl.pallas_call(
        functools.partial(_prefill_kernel, tq=tq),
        out_shape=jax.ShapeDtypeStruct((group, heads * head_size), jnp.bfloat16),
        grid_spec=pltpu.PrefetchScalarGridSpec(
            num_scalar_prefetch=3,
            grid=(heads, group // tq),
            in_specs=[
                pl.BlockSpec((tq, head_size), lambda h, i, *_: (i, h * 3)),
                pl.BlockSpec((group, head_size), col(1)),
                pl.BlockSpec((group, head_size), col(2)),
                pl.BlockSpec((cache_size, head_size), lambda h, i, *_: (0, h)),
                pl.BlockSpec((cache_size, head_size), lambda h, i, *_: (0, h)),
            ],
            out_specs=pl.BlockSpec((tq, head_size), lambda h, i, p, s, place: (place[i], h)),
        ),
        cost_estimate=pl.CostEstimate(
            flops=4 * heads * group * (group + cache_size) * head_size,
            transcendentals=heads * group * (group + cache_size),
            bytes_accessed=2 * (group * heads * 3 * head_size + 2 * cache_size * heads * head_size + group * heads * head_size),
        ),
    )(prefix, slopes, place, merged, merged, merged, cache_keys, cache_values)


def decode_attention(query_row, new_key, new_value, cache_keys, cache_values, length, slopes):
    heads, head_size = query_row.shape
    factor = 1.0 / math.sqrt(head_size)
    cache_pos = jnp.arange(cache_keys.shape[0], dtype=jnp.int32)
    distance = (length - cache_pos).astype(jnp.float32)
    head_of_col = jnp.arange(heads * head_size, dtype=jnp.int32) // head_size
    own_head = head_of_col[:, None] == jnp.arange(heads, dtype=jnp.int32)[None, :]
    block_query = jnp.where(own_head, query_row.reshape(-1)[:, None], jnp.zeros((), query_row.dtype))
    cache_scores = jnp.dot(cache_keys, block_query, preferred_element_type=jnp.float32).T * factor
    cache_scores = cache_scores - slopes[:, None] * distance[None, :]
    cache_scores = jnp.where((cache_pos < length)[None, :], cache_scores, -jnp.inf)
    own_score = (
        jnp.einsum("hd,hd->h", query_row, new_key, preferred_element_type=jnp.float32)[:, None]
        * factor
    )
    highest = jnp.maximum(jnp.max(cache_scores, axis=-1, keepdims=True), own_score)
    cache_exp = jnp.exp(cache_scores - highest)
    own_exp = jnp.exp(own_score - highest)
    denominator = jnp.sum(cache_exp, axis=-1, keepdims=True) + own_exp
    cache_probs = (cache_exp / denominator).astype(jnp.bfloat16)
    own_prob = (own_exp / denominator).astype(jnp.bfloat16)
    every_head = jnp.dot(cache_probs, cache_values, preferred_element_type=jnp.float32)
    context = jnp.sum(jnp.where(own_head.T, every_head, 0.0), axis=0).reshape(heads, head_size)
    context = context + own_prob.astype(jnp.float32) * new_value.astype(jnp.float32)
    return context.astype(jnp.bfloat16).reshape(-1)


def per_device(
    pre_hidden,
    dec_hidden,
    norm_gain,
    norm_shift,
    qkv_weight,
    qkv_bias,
    out_weight,
    out_bias,
    pre_keys,
    pre_values,
    dec_keys,
    dec_values,
    prefix_lengths,
    cache_lengths,
    slot_of,
):
    head_size = HD
    local_heads = qkv_weight.shape[1] // (3 * head_size)
    slopes = alibi_slopes(lax.axis_index("tensor") * local_heads, local_heads, H)
    bias_sum = out_bias.astype(jnp.float32)
    normed = normalize(pre_hidden, norm_gain, norm_shift)
    normed, dec_hidden = lax.optimization_barrier((normed, dec_hidden))
    slot_count = dec_hidden.shape[0]
    dp_size = lax.axis_size("dp")
    tensor_size = lax.axis_size("tensor")
    group = lax.axis_index("dp")
    member = lax.axis_index("tensor")
    first_slot = group * slot_count
    shifted_rows = dec_hidden
    step = 1
    while step < dp_size:
        shifted_rows = jnp.concatenate(
            [shifted_rows, lax.ppermute(shifted_rows, "dp", [(i, i ^ step) for i in range(dp_size)])], axis=0
        )
        step *= 2
    slot_ids = first_slot + jnp.arange(slot_count, dtype=jnp.int32)
    request_ids = jnp.arange(slot_of.shape[0], dtype=jnp.int32)
    uses_slot = slot_of[None, :] == slot_ids[:, None]
    request_of_slot = jnp.sum(jnp.where(uses_slot, request_ids[None, :], 0), axis=1)
    arrival = ((request_of_slot // slot_count) ^ group) * slot_count + request_of_slot % slot_count
    pick = (arrival[:, None] == jnp.arange(shifted_rows.shape[0], dtype=jnp.int32)[None, :]).astype(
        jnp.bfloat16
    )
    arrived = jnp.dot(pick, shifted_rows, preferred_element_type=jnp.float32).astype(jnp.bfloat16)
    normed_slots = normalize(arrived, norm_gain, norm_shift)
    merged_slots = (
        jnp.dot(normed_slots, qkv_weight, preferred_element_type=jnp.float32)
        + qkv_bias.astype(jnp.float32)
    ).astype(jnp.bfloat16)
    merged_slots = merged_slots.reshape(slot_count, local_heads, 3, head_size)
    dec_cache = dec_keys.shape[1]
    slot_context = jax.vmap(decode_attention, in_axes=(0, 0, 0, 0, 0, 0, None))(
        merged_slots[:, :, 0],
        merged_slots[:, :, 1],
        merged_slots[:, :, 2],
        dec_keys,
        dec_values,
        cache_lengths,
        slopes,
    )
    slot_partial = jnp.dot(slot_context, out_weight, preferred_element_type=jnp.float32)
    partials = slot_partial
    step = 1
    while step < tensor_size:
        partials = jnp.concatenate(
            [partials, lax.ppermute(partials, "tensor", [(i, i ^ step) for i in range(tensor_size)])], axis=0
        )
        step *= 2
    partials = partials.reshape(tensor_size, slot_count, -1)
    slot_summed = partials[member ^ 0]
    for source in range(1, tensor_size):
        slot_summed = slot_summed + partials[member ^ source]
    slot_rows = (slot_summed + bias_sum + arrived.astype(jnp.float32)).astype(jnp.bfloat16)
    tensor_size = lax.axis_size("tensor")
    chips = tensor_size // 2
    member = lax.axis_index("tensor")
    chip = member // 2
    core = member % 2
    block = pre_hidden.shape[0]

    def route(k, flip):
        return [(i, ((i // 2 + k) % chips) * 2 + ((i % 2) ^ flip)) for i in range(tensor_size)]

    across_tokens = [lax.ppermute(normed, "tensor", route(k, 0)) for k in range(1, chips)]
    across_tokens, held_weight = lax.optimization_barrier((across_tokens, out_weight))
    same_core_tokens = [normed] + list(across_tokens)
    sibling_tokens = [lax.ppermute(t, "tensor", route(0, 1)) for t in same_core_tokens]
    sibling_tokens, slot_rows = lax.optimization_barrier((sibling_tokens, slot_rows))
    across_chips = [lax.ppermute(held_weight, "tensor", route(k, 0)) for k in range(1, chips)]
    bias_row = qkv_bias.astype(jnp.float32)
    merged_rows = jnp.zeros((tensor_size * block, qkv_weight.shape[1]), jnp.bfloat16)
    for flip, token_blocks in ((0, same_core_tokens), (1, sibling_tokens)):
        for k, token_block in enumerate(token_blocks):
            source = ((chip - k) % chips) * 2 + (core ^ flip)
            projected = (
                jnp.dot(token_block, qkv_weight, preferred_element_type=jnp.float32) + bias_row
            ).astype(jnp.bfloat16)
            merged_rows = lax.dynamic_update_slice_in_dim(merged_rows, projected, source * block, 0)
    returned = slot_rows
    step = 1
    while step < dp_size:
        returned = jnp.concatenate(
            [returned, lax.ppermute(returned, "dp", [(i, i ^ step) for i in range(dp_size)])], axis=0
        )
        step *= 2
    slot_wanted = lax.dynamic_slice_in_dim(slot_of, first_slot, slot_count)
    back = ((slot_wanted // slot_count) ^ group) * slot_count + slot_wanted % slot_count
    take = (back[:, None] == jnp.arange(returned.shape[0], dtype=jnp.int32)[None, :]).astype(jnp.bfloat16)
    dec_output = jnp.dot(take, returned, preferred_element_type=jnp.float32).astype(jnp.bfloat16)
    merged_rows, dec_output = lax.optimization_barrier((merged_rows, dec_output))
    members = jnp.arange(tensor_size, dtype=jnp.int32)
    place = ((members % 2) ^ core) * chips + (members // 2 - chip) % chips
    context = prefill_attention_kernel(
        merged_rows, pre_keys[0], pre_values[0], prefix_lengths, slopes, place, head_size, block
    )
    context, across_chips = lax.optimization_barrier((context, across_chips))
    same_core = [out_weight] + list(across_chips)
    weight_blocks = same_core + [lax.ppermute(w, "tensor", route(0, 1)) for w in same_core]
    pieces = []
    for flip in (0, 1):
        for k in range(chips):
            position = flip * chips + k
            outgoing = context[position * block:(position + 1) * block]
            if k == 0 and flip == 0:
                pieces.append(outgoing)
                continue
            pieces.append(lax.ppermute(outgoing, "tensor", route(k, flip)))
    summed = pre_hidden.astype(jnp.float32) + bias_sum
    by_arrival = sorted(range(len(pieces)), key=lambda n: (n % chips != 0, n))
    for n in by_arrival:
        summed = summed + jnp.dot(pieces[n], weight_blocks[n], preferred_element_type=jnp.float32)
    pre_output = summed.astype(jnp.bfloat16)
    return (pre_output, dec_output)


def solution(mesh):
    placed = (
        P(("dp", "tensor"), None),
        P("dp", None),
        P(),
        P(),
        P(None, "tensor"),
        P("tensor"),
        P("tensor", None),
        P(),
        P("dp", None, "tensor"),
        P("dp", None, "tensor"),
        P("dp", None, "tensor"),
        P("dp", None, "tensor"),
        P("dp"),
        P("dp"),
        P(),
    )
    return jax.shard_map(
        per_device,
        mesh=mesh,
        in_specs=placed,
        out_specs=(P(("dp", "tensor"), None), P("dp", None)),
        check_vma=False,
    )
```

```python
import math

import jax
import jax.numpy as jnp
from jax import lax
from jax.sharding import PartitionSpec as P
from jax.experimental import pallas as pl
from jax.experimental.pallas import tpu as pltpu
import functools

H = 16
HD = 128


EPSILON = 1e-05


def normalize(values, norm_gain, norm_shift):
    values = values.astype(jnp.float32)
    center = values - jnp.mean(values, axis=-1, keepdims=True)
    spread = jnp.mean(center * center, axis=-1, keepdims=True)
    scaled = center * lax.rsqrt(spread + EPSILON)
    return (scaled * norm_gain.astype(jnp.float32) + norm_shift.astype(jnp.float32)).astype(
        jnp.bfloat16
    )


def alibi_slopes(first_head, head_count, total_heads):
    head_ids = (first_head + jnp.arange(head_count, dtype=jnp.int32)).astype(jnp.float32)
    return jnp.exp2(-8.0 * (head_ids + 1.0) / total_heads)


def prefill_attention(merged_rows, cache_keys, cache_values, prefix, slopes):
    queries = merged_rows[:, :, 0]
    new_keys = merged_rows[:, :, 1]
    new_values = merged_rows[:, :, 2]
    group_size = merged_rows.shape[0]
    cache_size = cache_keys.shape[0]
    factor = 1.0 / math.sqrt(merged_rows.shape[-1])
    query_pos = prefix + jnp.arange(group_size, dtype=jnp.int32)
    cache_pos = jnp.arange(cache_size, dtype=jnp.int32)
    cache_dist = (query_pos[:, None] - cache_pos[None, :]).astype(jnp.float32)
    new_dist = (query_pos[:, None] - query_pos[None, :]).astype(jnp.float32)
    cache_scores = (
        jnp.einsum("qhd,khd->hqk", queries, cache_keys, preferred_element_type=jnp.float32) * factor
    )
    cache_scores = cache_scores - slopes[:, None, None] * cache_dist[None]
    cache_scores = jnp.where((cache_pos < prefix)[None, None, :], cache_scores, -jnp.inf)
    new_scores = (
        jnp.einsum("qhd,khd->hqk", queries, new_keys, preferred_element_type=jnp.float32) * factor
    )
    new_scores = new_scores - slopes[:, None, None] * new_dist[None]
    causal = (
        jnp.arange(group_size, dtype=jnp.int32)[None, :]
        <= jnp.arange(group_size, dtype=jnp.int32)[:, None]
    )
    new_scores = jnp.where(causal[None], new_scores, -jnp.inf)
    highest = jnp.maximum(
        jnp.max(cache_scores, axis=-1, keepdims=True), jnp.max(new_scores, axis=-1, keepdims=True)
    )
    cache_exp = jnp.exp(cache_scores - highest)
    new_exp = jnp.exp(new_scores - highest)
    denominator = jnp.sum(cache_exp, axis=-1, keepdims=True) + jnp.sum(
        new_exp, axis=-1, keepdims=True
    )
    cache_probs = (cache_exp / denominator).astype(jnp.bfloat16)
    new_probs = (new_exp / denominator).astype(jnp.bfloat16)
    context = jnp.einsum(
        "hqk,khd->qhd", cache_probs, cache_values, preferred_element_type=jnp.float32
    )
    context = context + jnp.einsum(
        "hqk,khd->qhd", new_probs, new_values, preferred_element_type=jnp.float32
    )
    return context.astype(jnp.bfloat16).reshape(group_size, -1)


def _prefill_kernel(prefix_ref, slopes_ref, place_ref, q_ref, kn_ref, vn_ref, kc_ref, vc_ref, o_ref, *, tq):
    h = pl.program_id(0)
    i = pl.program_id(1)
    prefix = prefix_ref[0]
    slope = slopes_ref[h]
    factor = 1.0 / math.sqrt(q_ref.shape[-1])
    dims = (((1,), (1,)), ((), ()))
    cache_size = kc_ref.shape[0]

    def tile(last, width):
        q = q_ref[...]
        q_tok = last * tq + lax.broadcasted_iota(jnp.int32, (tq, 1), 0)
        q_pos = prefix + q_tok
        c_pos = lax.broadcasted_iota(jnp.int32, (1, cache_size), 1)
        k_tok = lax.broadcasted_iota(jnp.int32, (1, width), 1)
        s_c = lax.dot_general(q, kc_ref[...], dims, preferred_element_type=jnp.float32) * factor
        s_c = s_c - slope * (q_pos - c_pos).astype(jnp.float32)
        s_c = jnp.where(c_pos < prefix, s_c, -jnp.inf)
        s_n = lax.dot_general(q, kn_ref[:width, :], dims, preferred_element_type=jnp.float32) * factor
        s_n = s_n - slope * (q_tok - k_tok).astype(jnp.float32)
        s_n = jnp.where(k_tok <= q_tok, s_n, -jnp.inf)
        m = jnp.maximum(jnp.max(s_c, axis=-1, keepdims=True), jnp.max(s_n, axis=-1, keepdims=True))
        e_c = jnp.exp(s_c - m)
        e_n = jnp.exp(s_n - m)
        l = jnp.sum(e_c, axis=-1, keepdims=True) + jnp.sum(e_n, axis=-1, keepdims=True)
        p_c = (e_c / l).astype(jnp.bfloat16)
        p_n = (e_n / l).astype(jnp.bfloat16)
        ctx = jnp.dot(p_c, vc_ref[...], preferred_element_type=jnp.float32)
        ctx = ctx + jnp.dot(p_n, vn_ref[:width, :], preferred_element_type=jnp.float32)
        o_ref[...] = ctx.astype(o_ref.dtype)

    for last in range(kn_ref.shape[0] // tq):
        pl.when(i == last)(functools.partial(tile, last, (last + 1) * tq))


def prefill_attention_kernel(merged, cache_keys, cache_values, prefix, slopes, place, head_size, tq):
    group = merged.shape[0]
    heads = merged.shape[1] // (3 * head_size)
    cache_size = cache_keys.shape[0]
    col = lambda c: (lambda h, i, *_: (0, h * 3 + c))
    return pl.pallas_call(
        functools.partial(_prefill_kernel, tq=tq),
        out_shape=jax.ShapeDtypeStruct((group, heads * head_size), jnp.bfloat16),
        grid_spec=pltpu.PrefetchScalarGridSpec(
            num_scalar_prefetch=3,
            grid=(heads, group // tq),
            in_specs=[
                pl.BlockSpec((tq, head_size), lambda h, i, *_: (i, h * 3)),
                pl.BlockSpec((group, head_size), col(1)),
                pl.BlockSpec((group, head_size), col(2)),
                pl.BlockSpec((cache_size, head_size), lambda h, i, *_: (0, h)),
                pl.BlockSpec((cache_size, head_size), lambda h, i, *_: (0, h)),
            ],
            out_specs=pl.BlockSpec((tq, head_size), lambda h, i, p, s, place: (place[i], h)),
        ),
        cost_estimate=pl.CostEstimate(
            flops=4 * heads * tq * (group // tq * cache_size + tq * (group // tq) * (group // tq + 1) // 2) * head_size,
            transcendentals=heads * tq * (group // tq * cache_size + tq * (group // tq) * (group // tq + 1) // 2),
            bytes_accessed=2 * (group * heads * 3 * head_size + 2 * cache_size * heads * head_size + group * heads * head_size),
        ),
    )(prefix, slopes, place, merged, merged, merged, cache_keys, cache_values)


def decode_attention(query_row, new_key, new_value, cache_keys, cache_values, length, slopes):
    heads, head_size = query_row.shape
    factor = 1.0 / math.sqrt(head_size)
    cache_pos = jnp.arange(cache_keys.shape[0], dtype=jnp.int32)
    distance = (length - cache_pos).astype(jnp.float32)
    head_of_col = jnp.arange(heads * head_size, dtype=jnp.int32) // head_size
    own_head = head_of_col[:, None] == jnp.arange(heads, dtype=jnp.int32)[None, :]
    block_query = jnp.where(own_head, query_row.reshape(-1)[:, None], jnp.zeros((), query_row.dtype))
    cache_scores = jnp.dot(cache_keys, block_query, preferred_element_type=jnp.float32).T * factor
    cache_scores = cache_scores - slopes[:, None] * distance[None, :]
    cache_scores = jnp.where((cache_pos < length)[None, :], cache_scores, -jnp.inf)
    own_score = (
        jnp.einsum("hd,hd->h", query_row, new_key, preferred_element_type=jnp.float32)[:, None]
        * factor
    )
    highest = jnp.maximum(jnp.max(cache_scores, axis=-1, keepdims=True), own_score)
    cache_exp = jnp.exp(cache_scores - highest)
    own_exp = jnp.exp(own_score - highest)
    denominator = jnp.sum(cache_exp, axis=-1, keepdims=True) + own_exp
    cache_probs = (cache_exp / denominator).astype(jnp.bfloat16)
    own_prob = (own_exp / denominator).astype(jnp.bfloat16)
    every_head = jnp.dot(cache_probs, cache_values, preferred_element_type=jnp.float32)
    context = jnp.sum(jnp.where(own_head.T, every_head, 0.0), axis=0).reshape(heads, head_size)
    context = context + own_prob.astype(jnp.float32) * new_value.astype(jnp.float32)
    return context.astype(jnp.bfloat16).reshape(-1)


def per_device(
    pre_hidden,
    dec_hidden,
    norm_gain,
    norm_shift,
    qkv_weight,
    qkv_bias,
    out_weight,
    out_bias,
    pre_keys,
    pre_values,
    dec_keys,
    dec_values,
    prefix_lengths,
    cache_lengths,
    slot_of,
):
    head_size = HD
    local_heads = qkv_weight.shape[1] // (3 * head_size)
    slopes = alibi_slopes(lax.axis_index("tensor") * local_heads, local_heads, H)
    bias_sum = out_bias.astype(jnp.float32)
    normed = normalize(pre_hidden, norm_gain, norm_shift)
    normed, dec_hidden = lax.optimization_barrier((normed, dec_hidden))
    slot_count = dec_hidden.shape[0]
    dp_size = lax.axis_size("dp")
    tensor_size = lax.axis_size("tensor")
    group = lax.axis_index("dp")
    member = lax.axis_index("tensor")
    first_slot = group * slot_count
    shifted_rows = dec_hidden
    step = 1
    while step < dp_size:
        shifted_rows = jnp.concatenate(
            [shifted_rows, lax.ppermute(shifted_rows, "dp", [(i, i ^ step) for i in range(dp_size)])], axis=0
        )
        step *= 2
    slot_ids = first_slot + jnp.arange(slot_count, dtype=jnp.int32)
    request_ids = jnp.arange(slot_of.shape[0], dtype=jnp.int32)
    uses_slot = slot_of[None, :] == slot_ids[:, None]
    request_of_slot = jnp.sum(jnp.where(uses_slot, request_ids[None, :], 0), axis=1)
    arrival = ((request_of_slot // slot_count) ^ group) * slot_count + request_of_slot % slot_count
    pick = (arrival[:, None] == jnp.arange(shifted_rows.shape[0], dtype=jnp.int32)[None, :]).astype(
        jnp.bfloat16
    )
    arrived = jnp.dot(pick, shifted_rows, preferred_element_type=jnp.float32).astype(jnp.bfloat16)
    normed_slots = normalize(arrived, norm_gain, norm_shift)
    merged_slots = (
        jnp.dot(normed_slots, qkv_weight, preferred_element_type=jnp.float32)
        + qkv_bias.astype(jnp.float32)
    ).astype(jnp.bfloat16)
    merged_slots = merged_slots.reshape(slot_count, local_heads, 3, head_size)
    dec_cache = dec_keys.shape[1]
    slot_context = jax.vmap(decode_attention, in_axes=(0, 0, 0, 0, 0, 0, None))(
        merged_slots[:, :, 0],
        merged_slots[:, :, 1],
        merged_slots[:, :, 2],
        dec_keys,
        dec_values,
        cache_lengths,
        slopes,
    )
    slot_partial = jnp.dot(slot_context, out_weight, preferred_element_type=jnp.float32)
    partials = slot_partial
    step = 1
    while step < tensor_size:
        partials = jnp.concatenate(
            [partials, lax.ppermute(partials, "tensor", [(i, i ^ step) for i in range(tensor_size)])], axis=0
        )
        step *= 2
    partials = partials.reshape(tensor_size, slot_count, -1)
    slot_summed = partials[member ^ 0]
    for source in range(1, tensor_size):
        slot_summed = slot_summed + partials[member ^ source]
    slot_rows = (slot_summed + bias_sum + arrived.astype(jnp.float32)).astype(jnp.bfloat16)
    tensor_size = lax.axis_size("tensor")
    chips = tensor_size // 2
    member = lax.axis_index("tensor")
    chip = member // 2
    core = member % 2
    block = pre_hidden.shape[0]

    def route(k, flip):
        return [(i, ((i // 2 + k) % chips) * 2 + ((i % 2) ^ flip)) for i in range(tensor_size)]

    across_tokens = [lax.ppermute(normed, "tensor", route(k, 0)) for k in range(1, chips)]
    across_tokens, held_weight = lax.optimization_barrier((across_tokens, out_weight))
    same_core_tokens = [normed] + list(across_tokens)
    sibling_tokens = [lax.ppermute(t, "tensor", route(0, 1)) for t in same_core_tokens]
    sibling_tokens, slot_rows = lax.optimization_barrier((sibling_tokens, slot_rows))
    across_chips = [lax.ppermute(held_weight, "tensor", route(k, 0)) for k in range(1, chips)]
    bias_row = qkv_bias.astype(jnp.float32)
    merged_rows = jnp.zeros((tensor_size * block, qkv_weight.shape[1]), jnp.bfloat16)
    for flip, token_blocks in ((0, same_core_tokens), (1, sibling_tokens)):
        for k, token_block in enumerate(token_blocks):
            source = ((chip - k) % chips) * 2 + (core ^ flip)
            projected = (
                jnp.dot(token_block, qkv_weight, preferred_element_type=jnp.float32) + bias_row
            ).astype(jnp.bfloat16)
            merged_rows = lax.dynamic_update_slice_in_dim(merged_rows, projected, source * block, 0)
    returned = slot_rows
    step = 1
    while step < dp_size:
        returned = jnp.concatenate(
            [returned, lax.ppermute(returned, "dp", [(i, i ^ step) for i in range(dp_size)])], axis=0
        )
        step *= 2
    slot_wanted = lax.dynamic_slice_in_dim(slot_of, first_slot, slot_count)
    back = ((slot_wanted // slot_count) ^ group) * slot_count + slot_wanted % slot_count
    take = (back[:, None] == jnp.arange(returned.shape[0], dtype=jnp.int32)[None, :]).astype(jnp.bfloat16)
    dec_output = jnp.dot(take, returned, preferred_element_type=jnp.float32).astype(jnp.bfloat16)
    merged_rows, dec_output = lax.optimization_barrier((merged_rows, dec_output))
    members = jnp.arange(tensor_size, dtype=jnp.int32)
    place = ((members % 2) ^ core) * chips + (members // 2 - chip) % chips
    context = prefill_attention_kernel(
        merged_rows, pre_keys[0], pre_values[0], prefix_lengths, slopes, place, head_size, block
    )
    context, across_chips = lax.optimization_barrier((context, across_chips))
    same_core = [out_weight] + list(across_chips)
    weight_blocks = same_core + [lax.ppermute(w, "tensor", route(0, 1)) for w in same_core]
    pieces = []
    for flip in (0, 1):
        for k in range(chips):
            position = flip * chips + k
            outgoing = context[position * block:(position + 1) * block]
            if k == 0 and flip == 0:
                pieces.append(outgoing)
                continue
            pieces.append(lax.ppermute(outgoing, "tensor", route(k, flip)))
    summed = pre_hidden.astype(jnp.float32) + bias_sum
    for piece, weight in zip(pieces, weight_blocks):
        summed = summed + jnp.dot(piece, weight, preferred_element_type=jnp.float32)
    pre_output = summed.astype(jnp.bfloat16)
    return (pre_output, dec_output)


def solution(mesh):
    placed = (
        P(("dp", "tensor"), None),
        P("dp", None),
        P(),
        P(),
        P(None, "tensor"),
        P("tensor"),
        P("tensor", None),
        P(),
        P("dp", None, "tensor"),
        P("dp", None, "tensor"),
        P("dp", None, "tensor"),
        P("dp", None, "tensor"),
        P("dp"),
        P("dp"),
        P(),
    )
    return jax.shard_map(
        per_device,
        mesh=mesh,
        in_specs=placed,
        out_specs=(P(("dp", "tensor"), None), P("dp", None)),
        check_vma=False,
    )
```
